32 devices in a mesh: ens: 2 (over y), step: 8 (over z, x), rows: 2 (over core).
Axes of the slice: x: 2, y: 2, z: 4, core: 2. Of those that a mesh axis runs over, the one named last changes fastest.
Arguments:
- iterates: float32 [8, 8, 32, 512], P('step', 'ens', 'rows'), parts along dimension 1, may hold values from -6 to 6
- window_start: float32 [8, 32, 512], P('ens', 'rows'), parts along dimension 0, may hold values from -6 to 6
- coarse: bfloat16 [24, 32, 512], P('ens', 'rows'), parts along dimension 0, may hold values from -6 to 6
- step_levels: int32 [8, 2], P('step'), may hold values from 0 to 16, as said below
- level_embed: bfloat16 [17, 128], replicated, may hold values from -3 to 3
- lift_weight: bfloat16 [16, 128], replicated, may hold values from -1.5 to 1.5
- conv_first: bfloat16 [3, 3, 128, 128], replicated, may hold values from -0.1875 to 0.1875
- conv_second: bfloat16 [3, 3, 128, 128], replicated, may hold values from -0.1875 to 0.1875
- project_weight: bfloat16 [128, 384], replicated, may hold values from -0.5 to 0.5
- mix_weight: bfloat16 [128, 128], replicated, may hold values from -6 to 6
- output_weight: bfloat16 [128, 4], replicated, may hold values from -0.5 to 0.5
Outputs:
- trajectory: float32 [8, 8, 32, 512], P('step', 'ens', 'rows'), parts along dimension 1
- denoised: float32 [8, 8, 32, 512], P('step', 'ens', 'rows'), parts along dimension 1
The draws below stay inside these ranges and needn't reach their ends.
There are 2 independent parts, one for each index of `ens`. The reference program is written for one: setup_inputs(seed, part) draws one part's arguments, and reference() takes and returns one part's arrays. A program takes and returns all parts, laid end to end along the dimension named above; an argument that names none is the same for every part. Nothing has to cross between parts.
Inputs may be any that keep to these rules, and one draw needn't show every extreme that they name: `step_levels`: row k gives the plan levels at which step k starts and ends: each step ends 1 or 3 levels after it starts (half of the steps each), each step starts where the one before it ends, the first starts at level 0 and the last ends at level 16.
All inputs are finite; a program needn't handle non-finite values.
Results may differ from the reference program's by a relative error of at most 0.0028.
Values may be sent and summed in bfloat16 or wider, within the bound.
No kernel may reach another device: no remote copies, remote signals or barrier semaphores. Data moves between devices by JAX's collectives and lax.ppermute only.
A program may use at most 64 MiB of HBM per device.

```python
import jax
import jax.numpy as jnp
from jax import lax

FEAT = 128
CHANNELS = 4
COND = 12
HEAD_DIM = 64
COLS = 512
STEPS = 8
NLEVELS = 17
ROWS = 32


def draw_step_levels(key, part):
    shuffled = jax.random.permutation(key, STEPS)
    strides = jnp.where(shuffled < STEPS // 2, 1, 3).astype(jnp.int32)
    targets = jnp.cumsum(strides).astype(jnp.int32)
    starts = targets - strides
    return jnp.stack([starts, targets], axis=1).astype(jnp.int32)


def draw_coarse(key, part):
    noise_key = jax.random.fold_in(key, 11)
    amp_key = jax.random.fold_in(key, 12)
    sign_key = jax.random.fold_in(key, 13)
    noise = jax.random.normal(noise_key, (COND, ROWS, COLS), jnp.float32)
    amplitude = jax.random.uniform(amp_key, (COND, 1, 1), jnp.float32, 1.0, 2.0)
    signs = jnp.where(jax.random.bernoulli(sign_key, 0.5, (COND, 1, 1)), 1.0, -1.0).astype(jnp.float32)
    position = (jnp.arange(ROWS, dtype=jnp.float32) + 0.5) / ROWS
    ramp = (2.0 * position - 1.0)[None, :, None] * 1.5
    values = noise + signs * amplitude * ramp
    return jnp.clip(values, -6.0, 6.0).astype(jnp.bfloat16)


def block_scale(stream_key, shape, pieces, smallest, top_value):
    factor_of, own = 1.0, jax.random.fold_in(stream_key, 6)
    for dim, blocks in pieces:
        heights = jnp.exp(jax.random.uniform(jax.random.fold_in(own, dim), (blocks,), jnp.float32, smallest / len(pieces), top_value / len(pieces)))
        factor_of = factor_of * jnp.repeat(heights, shape[dim] // blocks).reshape([-1 if axis == dim else 1 for axis in range(len(shape))])
    return factor_of


def centred(rng, shape, deviation, reach, pieces=(), held_as=jnp.bfloat16):
    entries = deviation * jax.random.normal(rng, shape, jnp.float32)
    if pieces:
        entries = entries * block_scale(rng, shape, pieces, -0.22, 0.18)
    return jnp.clip(entries, -reach, reach).astype(held_as)


def setup_inputs(seed: int = 0, part: int = 0) -> dict:
    key_of = jax.random.split(jax.random.key(seed), 12)
    part_keys = jax.random.split(jax.random.fold_in(key_of[11], part), 12)
    iterates = centred(part_keys[0], (STEPS, CHANNELS, ROWS, COLS), 1.0, 6.0, ((0, 8), (2, 2)), jnp.float32)
    window_start = centred(part_keys[1], (CHANNELS, ROWS, COLS), 1.0, 6.0, ((1, 2),), jnp.float32)
    coarse = draw_coarse(jax.random.fold_in(jax.random.fold_in(key_of[11], part), 71), part)
    step_levels = draw_step_levels(jax.random.fold_in(key_of[11], 71), part)
    level_embed = centred(key_of[4], (NLEVELS, FEAT), 0.5, 3.0)
    lift_weight = centred(key_of[5], (CHANNELS + COND, FEAT), (CHANNELS + COND) ** -0.5, 1.5)
    conv_first = centred(key_of[6], (3, 3, FEAT, FEAT), (9 * FEAT) ** -0.5, 0.1875)
    conv_second = centred(key_of[7], (3, 3, FEAT, FEAT), (9 * FEAT) ** -0.5, 0.1875)
    project_weight = centred(key_of[8], (FEAT, 3 * FEAT), FEAT ** -0.5, 0.5)
    mix_weight = centred(key_of[9], (FEAT, FEAT), (max(1, FEAT // 128)) ** -0.5, 6.0)
    output_weight = centred(key_of[10], (FEAT, CHANNELS), FEAT ** -0.5, 0.5)
    return dict(iterates=iterates, window_start=window_start, coarse=coarse, step_levels=step_levels, level_embed=level_embed, lift_weight=lift_weight, conv_first=conv_first, conv_second=conv_second, project_weight=project_weight, mix_weight=mix_weight, output_weight=output_weight)


SIGMA_TOP = 8.0
SIGMA_END = 0.002

def noise_level(levels, level_count):
    fraction = levels.astype(jnp.float32) / jnp.float32(level_count - 1)
    return SIGMA_TOP * jnp.exp(fraction * jnp.log(jnp.float32(SIGMA_END / SIGMA_TOP)))

def normalize(values):
    return values * lax.rsqrt(lax.optimization_barrier(jnp.mean(values * values, axis=-1, keepdims=True)) + 1e-06)

def silu_norm(values):
    return jax.nn.silu(normalize(values)).astype(jnp.bfloat16)

def feature_map(values):
    return jnp.where(values > 0, values + 1.0, jnp.exp(jnp.minimum(values, 0.0)))

def conv_image(padded, weight):
    image_rows = padded.shape[0] - 2
    image_width = padded.shape[1]
    col_padded = jnp.pad(padded, ((0, 0), (1, 1), (0, 0))).astype(jnp.float32)
    stacked = jnp.concatenate([col_padded[:, 0:image_width], col_padded[:, 1:image_width + 1], col_padded[:, 2:image_width + 2]], axis=-1)
    folded = weight.reshape(3, 3 * weight.shape[2], weight.shape[3]).astype(jnp.float32)
    result = jnp.zeros((image_rows, image_width, weight.shape[3]), jnp.float32)
    for row_shift in range(3):
        result = result + jnp.einsum('rwk,kf->rwf', stacked[row_shift:row_shift + image_rows], folded[row_shift], precision=lax.Precision.HIGHEST)
    return result

def denoise(current, sigma_low, level_index, coarse, level_embed, lift_weight, conv_first, conv_second, project_weight, mix_weight, output_weight):
    spread = sigma_low * sigma_low + 0.25
    scale_in = lax.rsqrt(spread)
    scale_skip = 0.25 / spread
    scale_out = 0.5 * sigma_low * lax.rsqrt(spread)
    inputs = jnp.concatenate([(scale_in * current).astype(jnp.bfloat16), coarse], axis=0)
    embed_row = level_embed[level_index].astype(jnp.float32)
    lifted = (jnp.einsum('crw,cf->rwf', inputs.astype(jnp.float32), lift_weight.astype(jnp.float32), precision=lax.Precision.HIGHEST) + embed_row).astype(jnp.bfloat16)
    act_first = silu_norm(lifted.astype(jnp.float32))
    middle = conv_image(jnp.pad(act_first, ((1, 1), (0, 0), (0, 0))), conv_first)
    act_next = silu_norm(middle)
    hidden = lifted.astype(jnp.float32) + conv_image(jnp.pad(act_next, ((1, 1), (0, 0), (0, 0))), conv_second)
    image_rows, image_width, feat_dim = hidden.shape
    head_count = feat_dim // HEAD_DIM
    pooled = hidden.reshape(image_rows // 4, 4, image_width // 4, 4, feat_dim).mean(axis=(1, 3)).reshape(-1, feat_dim)
    tokens = normalize(pooled).astype(jnp.bfloat16)
    projected = jnp.einsum('tf,fg->tg', tokens.astype(jnp.float32), project_weight.astype(jnp.float32), precision=lax.Precision.HIGHEST)
    queries = feature_map(projected[:, :feat_dim]).reshape(-1, head_count, HEAD_DIM)
    key_feats = feature_map(projected[:, feat_dim:2 * feat_dim]).astype(jnp.bfloat16).astype(jnp.float32).reshape(-1, head_count, HEAD_DIM)
    value_rows = projected[:, 2 * feat_dim:].astype(jnp.bfloat16).astype(jnp.float32).reshape(-1, head_count, HEAD_DIM)
    summary = jnp.einsum('thd,the->hde', key_feats, value_rows, precision=lax.Precision.HIGHEST)
    totals = lax.optimization_barrier(jnp.sum(key_feats, axis=0))
    numerator = jnp.einsum('thd,hde->the', queries, summary, precision=lax.Precision.HIGHEST)
    denominator = jnp.einsum('thd,hd->th', queries, totals, precision=lax.Precision.HIGHEST)
    context = (numerator / denominator[:, :, None]).reshape(-1, feat_dim).astype(jnp.bfloat16)
    mixed = jnp.einsum('tf,fg->tg', context.astype(jnp.float32), mix_weight.astype(jnp.float32), precision=lax.Precision.HIGHEST)
    mixed = jnp.broadcast_to(mixed.reshape(image_rows // 4, 1, image_width // 4, 1, feat_dim), (image_rows // 4, 4, image_width // 4, 4, feat_dim)).reshape(image_rows, image_width, feat_dim)
    act_out = silu_norm(hidden + mixed)
    out_field = jnp.einsum('rwf,fc->crw', act_out.astype(jnp.float32), output_weight.astype(jnp.float32), precision=lax.Precision.HIGHEST)
    return scale_skip * current + scale_out * out_field

def reference(iterates, window_start, coarse, step_levels, level_embed, lift_weight, conv_first, conv_second, project_weight, mix_weight, output_weight):
    sigma_from = noise_level(step_levels[:, 0], NLEVELS)
    sigma_to = noise_level(step_levels[:, 1], NLEVELS)
    states = jnp.concatenate([window_start[None], iterates[:-1]], axis=0)

    def per_step(step_items):
        current, sigma_low, sigma_high, level_index = step_items
        result = denoise(current, sigma_low, level_index, coarse, level_embed, lift_weight, conv_first, conv_second, project_weight, mix_weight, output_weight)
        drift_step = (sigma_high - sigma_low) * (current - result) / sigma_low
        return (result, drift_step)
    denoised, drifts = lax.map(per_step, (states, sigma_from, sigma_to, step_levels[:, 0].astype(jnp.int32)))
    trajectory = window_start[None] + jnp.cumsum(drifts, axis=0)
    return (trajectory, denoised)
```

```python
import jax
import jax.numpy as jnp
from jax import lax
from jax.sharding import PartitionSpec as P

HEAD_DIM = 64


SIGMA_TOP = 8.0
SIGMA_END = 0.002


def from_behind(x, axis, by):
    devices = lax.axis_size(axis)
    pairs = [(i, i + by) for i in range(devices) if 0 <= i + by < devices]
    return lax.ppermute(x, axis, pairs)


def with_halo(x, sides, width):
    for axis, dim in sides:
        devices, length = (lax.axis_size(axis), x.shape[dim])
        last = lax.slice_in_dim(x, length - width, length, axis=dim)
        leading = lax.slice_in_dim(x, 0, width, axis=dim)
        if devices == 2:
            me = lax.axis_index(axis)
            outgoing = jnp.where(me == 0, last, leading)
            incoming = lax.ppermute(outgoing, axis, [(0, 1), (1, 0)])
            zero = jnp.zeros_like(incoming)
            before = jnp.where(me == 0, zero, incoming)
            after = jnp.where(me == 0, incoming, zero)
        else:
            up = [(i, i + 1) for i in range(devices - 1)]
            down = [(j, i) for i, j in up]
            before = lax.ppermute(last, axis, up)
            after = lax.ppermute(leading, axis, down)
        x = jnp.concatenate([before, x, after], axis=dim)
    return x


def band_sum(x, axis):
    devices = lax.axis_size(axis)
    if devices == 2:
        return x + lax.ppermute(x, axis, [(0, 1), (1, 0)])
    return lax.psum(x, axis)


def prefix_sum(x, axis):
    devices = lax.axis_size(axis)
    shift = 1
    while shift < devices:
        pairs = [(i, i + shift) for i in range(devices - shift)]
        x = x + lax.ppermute(x, axis, pairs)
        shift *= 2
    return x


def noise_level(levels, level_count):
    fraction = levels.astype(jnp.float32) / jnp.float32(level_count - 1)
    return SIGMA_TOP * jnp.exp(fraction * jnp.log(jnp.float32(SIGMA_END / SIGMA_TOP)))


def normalize(values):
    return values * lax.rsqrt(jnp.mean(values * values, axis=-1, keepdims=True) + 1e-06)


def silu_norm(values):
    return jax.nn.silu(normalize(values)).astype(jnp.bfloat16)


def feature_map(values):
    return jnp.where(values > 0, values + 1.0, jnp.exp(jnp.minimum(values, 0.0)))


def conv_band(padded, weight):
    band_rows = padded.shape[0] - 2
    band_width = padded.shape[1]
    col_padded = jnp.pad(padded, ((0, 0), (1, 1), (0, 0)))
    stacked = jnp.concatenate(
        [
            col_padded[:, 0:band_width],
            col_padded[:, 1 : band_width + 1],
            col_padded[:, 2 : band_width + 2],
        ],
        axis=-1,
    )
    folded = weight.reshape(3, 3 * weight.shape[2], weight.shape[3])
    result = jnp.zeros((band_rows, band_width, weight.shape[3]), jnp.float32)
    for row_shift in range(3):
        result = result + jnp.einsum(
            "rwk,kf->rwf",
            stacked[row_shift : row_shift + band_rows],
            folded[row_shift],
            preferred_element_type=jnp.float32,
        )
    return result


def local(
    iterates,
    window_start,
    coarse,
    step_levels,
    level_embed,
    lift_weight,
    conv_first,
    conv_second,
    project_weight,
    mix_weight,
    output_weight,
):
    level_count = 2 * lax.axis_size("step") + 1
    previous = from_behind(iterates, "step", 1)
    current = jnp.where(lax.axis_index("step") == 0, window_start, previous[0])
    levels = step_levels[0]
    sigmas = noise_level(levels, level_count)
    sigma_low = sigmas[0]
    sigma_high = sigmas[1]
    spread = sigma_low * sigma_low + 0.25
    scale_in = lax.rsqrt(spread)
    scale_skip = 0.25 / spread
    scale_out = 0.5 * sigma_low * lax.rsqrt(spread)
    inputs = jnp.concatenate([(scale_in * current).astype(jnp.bfloat16), coarse], axis=0)
    picker = (jnp.arange(level_count) == levels[0]).astype(jnp.bfloat16)[None]
    embed_row = jnp.dot(picker, level_embed, preferred_element_type=jnp.float32)[0]
    lifted = (
        jnp.einsum("crw,cf->rwf", inputs, lift_weight, preferred_element_type=jnp.float32)
        + embed_row
    ).astype(jnp.bfloat16)
    band_rows = lifted.shape[0]
    band_width = lifted.shape[1]
    feat_dim = lifted.shape[2]
    act_first = silu_norm(lifted.astype(jnp.float32))
    padded = with_halo(act_first, (("rows", 0),), 1)
    middle = conv_band(padded, conv_first)
    act_next = silu_norm(middle)
    padded_next = with_halo(act_next, (("rows", 0),), 1)
    hidden = lifted.astype(jnp.float32) + conv_band(padded_next, conv_second)
    head_count = feat_dim // HEAD_DIM
    pooled = (
        hidden.reshape(band_rows // 4, 4, band_width // 4, 4, feat_dim)
        .mean(axis=(1, 3))
        .reshape(-1, feat_dim)
    )
    tokens = normalize(pooled).astype(jnp.bfloat16)
    projected = jnp.dot(tokens, project_weight, preferred_element_type=jnp.float32)
    queries = feature_map(projected[:, :feat_dim]).reshape(-1, head_count, HEAD_DIM)
    key_feats = feature_map(projected[:, feat_dim : 2 * feat_dim]).astype(jnp.bfloat16)
    value_rows = projected[:, 2 * feat_dim :].astype(jnp.bfloat16)
    key_heads = key_feats.reshape(-1, head_count, HEAD_DIM)
    value_heads = value_rows.reshape(-1, head_count, HEAD_DIM)
    summary_own = jnp.einsum(
        "thd,the->hde", key_heads, value_heads, preferred_element_type=jnp.float32
    )
    totals_own = jnp.sum(key_heads.astype(jnp.float32), axis=0)
    stats = band_sum(jnp.concatenate([summary_own, totals_own[:, None, :]], axis=1), "rows")
    summary_part = stats[:, :HEAD_DIM]
    totals_part = stats[:, HEAD_DIM]
    numerator = jnp.einsum("thd,hde->the", queries, summary_part, precision=lax.Precision.HIGHEST)
    denominator = jnp.einsum("thd,hd->th", queries, totals_part, precision=lax.Precision.HIGHEST)
    context = (numerator / denominator[:, :, None]).reshape(-1, feat_dim).astype(jnp.bfloat16)
    mixed = jnp.dot(context, mix_weight, preferred_element_type=jnp.float32)
    mixed = jnp.broadcast_to(
        mixed.reshape(band_rows // 4, 1, band_width // 4, 1, feat_dim),
        (band_rows // 4, 4, band_width // 4, 4, feat_dim),
    ).reshape(band_rows, band_width, feat_dim)
    act_out = silu_norm(hidden + mixed)
    out_field = jnp.einsum(
        "rwf,fc->crw", act_out, output_weight, preferred_element_type=jnp.float32
    )
    denoised = scale_skip * current + scale_out * out_field
    drift_step = (sigma_high - sigma_low) * (current - denoised) / sigma_low
    summed = prefix_sum(drift_step, "step")
    trajectory = window_start + summed
    return (trajectory[None], denoised[None])


def solution(mesh):
    return jax.shard_map(
        local,
        mesh=mesh,
        in_specs=(
            P("step", "ens", "rows", None),
            P("ens", "rows", None),
            P("ens", "rows", None),
            P("step", None),
            P(),
            P(),
            P(),
            P(),
            P(),
            P(),
            P(),
        ),
        out_specs=(P("step", "ens", "rows", None), P("step", "ens", "rows", None)),
        check_vma=False,
    )
```

```python
import jax
import jax.numpy as jnp
from jax import lax
from jax.sharding import PartitionSpec as P

HEAD_DIM = 64


SIGMA_TOP = 8.0
SIGMA_END = 0.002


def from_behind(x, axis, by):
    devices = lax.axis_size(axis)
    pairs = [(i, i + by) for i in range(devices) if 0 <= i + by < devices]
    return lax.ppermute(x, axis, pairs)


def with_halo(x, sides, width):
    for axis, dim in sides:
        devices, length = (lax.axis_size(axis), x.shape[dim])
        last = lax.slice_in_dim(x, length - width, length, axis=dim)
        leading = lax.slice_in_dim(x, 0, width, axis=dim)
        if devices == 2:
            me = lax.axis_index(axis)
            outgoing = jnp.where(me == 0, last, leading)
            incoming = lax.ppermute(outgoing, axis, [(0, 1), (1, 0)])
            zero = jnp.zeros_like(incoming)
            before = jnp.where(me == 0, zero, incoming)
            after = jnp.where(me == 0, incoming, zero)
        else:
            up = [(i, i + 1) for i in range(devices - 1)]
            down = [(j, i) for i, j in up]
            before = lax.ppermute(last, axis, up)
            after = lax.ppermute(leading, axis, down)
        x = jnp.concatenate([before, x, after], axis=dim)
    return x


def band_sum(x, axis):
    devices = lax.axis_size(axis)
    if devices == 2:
        return x + lax.ppermute(x, axis, [(0, 1), (1, 0)])
    return lax.psum(x, axis)


def prefix_sum(x, axis):
    devices = lax.axis_size(axis)
    shift = 1
    while shift < devices:
        pairs = [(i, i + shift) for i in range(devices - shift)]
        x = x + lax.ppermute(x, axis, pairs)
        shift *= 2
    return x


def gathered_prefix(x, axis):
    every = lax.all_gather(x, axis, axis=0)
    keep = jnp.arange(every.shape[0]) <= lax.axis_index(axis)
    keep = keep.reshape((-1,) + (1,) * x.ndim)
    return jnp.sum(jnp.where(keep, every, 0.0), axis=0)


def noise_level(levels, level_count):
    fraction = levels.astype(jnp.float32) / jnp.float32(level_count - 1)
    return SIGMA_TOP * jnp.exp(fraction * jnp.log(jnp.float32(SIGMA_END / SIGMA_TOP)))


def normalize(values):
    return values * lax.rsqrt(jnp.mean(values * values, axis=-1, keepdims=True) + 1e-06)


def silu_norm(values):
    return jax.nn.silu(normalize(values)).astype(jnp.bfloat16)


def feature_map(values):
    return jnp.where(values > 0, values + 1.0, jnp.exp(jnp.minimum(values, 0.0)))


def conv_band(padded, weight):
    band_rows = padded.shape[0] - 2
    band_width = padded.shape[1]
    col_padded = jnp.pad(padded, ((0, 0), (1, 1), (0, 0)))
    stacked = jnp.concatenate(
        [
            col_padded[:, 0:band_width],
            col_padded[:, 1 : band_width + 1],
            col_padded[:, 2 : band_width + 2],
        ],
        axis=-1,
    )
    folded = weight.reshape(3, 3 * weight.shape[2], weight.shape[3])
    result = jnp.zeros((band_rows, band_width, weight.shape[3]), jnp.float32)
    for row_shift in range(3):
        result = result + jnp.einsum(
            "rwk,kf->rwf",
            stacked[row_shift : row_shift + band_rows],
            folded[row_shift],
            preferred_element_type=jnp.float32,
        )
    return result


def local(
    iterates,
    window_start,
    coarse,
    step_levels,
    level_embed,
    lift_weight,
    conv_first,
    conv_second,
    project_weight,
    mix_weight,
    output_weight,
):
    level_count = 2 * lax.axis_size("step") + 1
    previous = from_behind(iterates, "step", 1)
    current = jnp.where(lax.axis_index("step") == 0, window_start, previous[0])
    levels = step_levels[0]
    sigmas = noise_level(levels, level_count)
    sigma_low = sigmas[0]
    sigma_high = sigmas[1]
    spread = sigma_low * sigma_low + 0.25
    scale_in = lax.rsqrt(spread)
    scale_skip = 0.25 / spread
    scale_out = 0.5 * sigma_low * lax.rsqrt(spread)
    inputs = jnp.concatenate([(scale_in * current).astype(jnp.bfloat16), coarse], axis=0)
    picker = (jnp.arange(level_count) == levels[0]).astype(jnp.bfloat16)[None]
    embed_row = jnp.dot(picker, level_embed, preferred_element_type=jnp.float32)[0]
    lifted = (
        jnp.einsum("crw,cf->rwf", inputs, lift_weight, preferred_element_type=jnp.float32)
        + embed_row
    ).astype(jnp.bfloat16)
    band_rows = lifted.shape[0]
    band_width = lifted.shape[1]
    feat_dim = lifted.shape[2]
    act_first = silu_norm(lifted.astype(jnp.float32))
    padded = with_halo(act_first, (("rows", 0),), 1)
    middle = conv_band(padded, conv_first)
    act_next = silu_norm(middle)
    padded_next = with_halo(act_next, (("rows", 0),), 1)
    hidden = lifted.astype(jnp.float32) + conv_band(padded_next, conv_second)
    head_count = feat_dim // HEAD_DIM
    pooled = (
        hidden.reshape(band_rows // 4, 4, band_width // 4, 4, feat_dim)
        .mean(axis=(1, 3))
        .reshape(-1, feat_dim)
    )
    tokens = normalize(pooled).astype(jnp.bfloat16)
    projected = jnp.dot(tokens, project_weight, preferred_element_type=jnp.float32)
    queries = feature_map(projected[:, :feat_dim]).reshape(-1, head_count, HEAD_DIM)
    key_feats = feature_map(projected[:, feat_dim : 2 * feat_dim]).astype(jnp.bfloat16)
    value_rows = projected[:, 2 * feat_dim :].astype(jnp.bfloat16)
    key_heads = key_feats.reshape(-1, head_count, HEAD_DIM)
    value_heads = value_rows.reshape(-1, head_count, HEAD_DIM)
    summary_own = jnp.einsum(
        "thd,the->hde", key_heads, value_heads, preferred_element_type=jnp.float32
    )
    totals_own = jnp.sum(key_heads.astype(jnp.float32), axis=0)
    stats = band_sum(jnp.concatenate([summary_own, totals_own[:, None, :]], axis=1), "rows")
    summary_part = stats[:, :HEAD_DIM]
    totals_part = stats[:, HEAD_DIM]
    numerator = jnp.einsum("thd,hde->the", queries, summary_part, precision=lax.Precision.HIGHEST)
    denominator = jnp.einsum("thd,hd->th", queries, totals_part, precision=lax.Precision.HIGHEST)
    context = (numerator / denominator[:, :, None]).reshape(-1, feat_dim).astype(jnp.bfloat16)
    mixed = jnp.dot(context, mix_weight, preferred_element_type=jnp.float32)
    mixed = jnp.broadcast_to(
        mixed.reshape(band_rows // 4, 1, band_width // 4, 1, feat_dim),
        (band_rows // 4, 4, band_width // 4, 4, feat_dim),
    ).reshape(band_rows, band_width, feat_dim)
    act_out = silu_norm(hidden + mixed)
    out_field = jnp.einsum(
        "rwf,fc->crw", act_out, output_weight, preferred_element_type=jnp.float32
    )
    denoised = scale_skip * current + scale_out * out_field
    drift_step = (sigma_high - sigma_low) * (current - denoised) / sigma_low
    summed = gathered_prefix(drift_step, "step")
    trajectory = window_start + summed
    return (trajectory[None], denoised[None])


def solution(mesh):
    return jax.shard_map(
        local,
        mesh=mesh,
        in_specs=(
            P("step", "ens", "rows", None),
            P("ens", "rows", None),
            P("ens", "rows", None),
            P("step", None),
            P(),
            P(),
            P(),
            P(),
            P(),
            P(),
            P(),
        ),
        out_specs=(P("step", "ens", "rows", None), P("step", "ens", "rows", None)),
        check_vma=False,
    )
```

```python
import jax
import jax.numpy as jnp
from jax import lax
from jax.experimental import pallas as pl
from jax.experimental.pallas import tpu as pltpu
from jax.sharding import PartitionSpec as P

HEAD_DIM = 64
HALO = 2
CHUNK_ROWS = 2

SIGMA_TOP = 8.0
SIGMA_END = 0.002


def from_behind(x, axis, by):
    devices = lax.axis_size(axis)
    pairs = [(i, i + by) for i in range(devices) if 0 <= i + by < devices]
    return lax.ppermute(x, axis, pairs)


def with_halo(x, axis, dim, width):
    devices, length = (lax.axis_size(axis), x.shape[dim])
    last = lax.slice_in_dim(x, length - width, length, axis=dim)
    leading = lax.slice_in_dim(x, 0, width, axis=dim)
    if devices == 2:
        me = lax.axis_index(axis)
        outgoing = jnp.where(me == 0, last, leading)
        incoming = lax.ppermute(outgoing, axis, [(0, 1), (1, 0)])
        zero = jnp.zeros_like(incoming)
        before = jnp.where(me == 0, zero, incoming)
        after = jnp.where(me == 0, incoming, zero)
    else:
        up = [(i, i + 1) for i in range(devices - 1)]
        down = [(j, i) for i, j in up]
        before = lax.ppermute(last, axis, up)
        after = lax.ppermute(leading, axis, down)
    return jnp.concatenate([before, x, after], axis=dim)


def band_sum(x, axis):
    devices = lax.axis_size(axis)
    if devices == 2:
        return x + lax.ppermute(x, axis, [(0, 1), (1, 0)])
    return lax.psum(x, axis)


def prefix_sum(x, axis):
    devices = lax.axis_size(axis)
    shift = 1
    while shift < devices:
        pairs = [(i, i + shift) for i in range(devices - shift)]
        x = x + lax.ppermute(x, axis, pairs)
        shift *= 2
    return x


def noise_level(levels, level_count):
    fraction = levels.astype(jnp.float32) / jnp.float32(level_count - 1)
    return SIGMA_TOP * jnp.exp(fraction * jnp.log(jnp.float32(SIGMA_END / SIGMA_TOP)))


def normalize_features(values):
    mean_square = jnp.sum(values * values, axis=0, keepdims=True) * (1.0 / values.shape[0])
    return values * lax.rsqrt(mean_square + 1e-06)


def silu(values):
    return values / (1.0 + jnp.exp(-values))


def feature_map(values):
    return jnp.where(values > 0, values + 1.0, jnp.exp(jnp.minimum(values, 0.0)))


def conv_chunk(source, weight, first_row, rows, width, column):
    span = rows * width
    stacked = jnp.concatenate(
        [source[:, (first_row + i) * width : (first_row + i) * width + span] for i in range(3)],
        axis=0,
    )
    taps = jnp.dot(weight, stacked, preferred_element_type=jnp.float32)
    feat = taps.shape[0] // 3
    left = pltpu.roll(taps[0:feat], 1, 1)
    right = pltpu.roll(taps[2 * feat : 3 * feat], span - 1, 1)
    result = taps[feat : 2 * feat]
    result = result + jnp.where(column != 0, left, 0.0)
    result = result + jnp.where(column != width - 1, right, 0.0)
    return result


def trunk_kernel(
    band_ref, inputs_ref, lift_ref, embed_ref, first_ref, second_ref, pool_ref,
    hidden_ref, pooled_ref, act_first, lifted_keep, act_next, *, width, band_rows, bands,
):
    band = band_ref[0]
    top_outside = band == 0
    bottom_outside = band == bands - 1
    span = CHUNK_ROWS * width
    column = lax.broadcasted_iota(jnp.int32, (1, span), 1) % width
    upper_row = lax.broadcasted_iota(jnp.int32, (1, span), 1) < width
    lift_w = lift_ref[...]
    embed = embed_ref[...]
    in_rows = band_rows + 2 * HALO
    for q in range(in_rows // CHUNK_ROWS):
        start = q * span
        lifted = jnp.dot(lift_w, inputs_ref[:, start : start + span], preferred_element_type=jnp.float32)
        lifted = (lifted + embed).astype(jnp.bfloat16)
        row0 = q * CHUNK_ROWS
        if HALO <= row0 < HALO + band_rows:
            keep = (row0 - HALO) * width
            lifted_keep[:, keep : keep + span] = lifted
        act = silu(normalize_features(lifted.astype(jnp.float32)))
        if row0 < HALO:
            act = jnp.where(top_outside, 0.0, act)
        if row0 >= HALO + band_rows:
            act = jnp.where(bottom_outside, 0.0, act)
        act_first[:, start : start + span] = act.astype(jnp.bfloat16)
    first_w = first_ref[...]
    mid_rows = band_rows + 2
    for q in range(mid_rows // CHUNK_ROWS):
        start = q * span
        middle = conv_chunk(act_first, first_w, q * CHUNK_ROWS, CHUNK_ROWS, width, column)
        act = silu(normalize_features(middle))
        if q == 0:
            act = jnp.where(jnp.logical_and(top_outside, upper_row), 0.0, act)
        if q == mid_rows // CHUNK_ROWS - 1:
            act = jnp.where(jnp.logical_and(bottom_outside, jnp.logical_not(upper_row)), 0.0, act)
        act_next[:, start : start + span] = act.astype(jnp.bfloat16)
    second_w = second_ref[...]
    for q in range(band_rows // CHUNK_ROWS):
        start = q * span
        conv = conv_chunk(act_next, second_w, q * CHUNK_ROWS, CHUNK_ROWS, width, column)
        hidden_ref[:, start : start + span] = lifted_keep[:, start : start + span].astype(jnp.float32) + conv
    pool_w = pool_ref[...]
    tokens_per_row = width // 4
    for a in range(band_rows // 4):
        row_sum = hidden_ref[:, (4 * a) * width : (4 * a + 1) * width]
        for u in range(1, 4):
            row_sum = row_sum + hidden_ref[:, (4 * a + u) * width : (4 * a + u + 1) * width]
        pooled_ref[:, a * tokens_per_row : (a + 1) * tokens_per_row] = jnp.dot(
            row_sum, pool_w, precision=lax.Precision.HIGHEST, preferred_element_type=jnp.float32
        )


def head_kernel(hidden_ref, mixed_ref, expand_ref, out_w_ref, field_ref, *, width, band_rows):
    expand = expand_ref[...]
    out_w = out_w_ref[...]
    tokens_per_row = width // 4
    for a in range(band_rows // 4):
        spread = jnp.dot(
            mixed_ref[:, a * tokens_per_row : (a + 1) * tokens_per_row],
            expand,
            precision=lax.Precision.HIGHEST,
            preferred_element_type=jnp.float32,
        )
        for u in range(4):
            start = (4 * a + u) * width
            combined = hidden_ref[:, start : start + width] + spread
            act = silu(normalize_features(combined)).astype(jnp.bfloat16)
            field = jnp.dot(out_w, act, preferred_element_type=jnp.float32)
            field_ref[:, start : start + width] = field[0:8]


def vmem():
    return pl.BlockSpec(memory_space=pltpu.VMEM)


def local(
    iterates,
    window_start,
    coarse,
    step_levels,
    level_embed,
    lift_weight,
    conv_first,
    conv_second,
    project_weight,
    mix_weight,
    output_weight,
):
    level_count = 2 * lax.axis_size("step") + 1
    bands = lax.axis_size("rows")
    previous = from_behind(iterates, "step", 1)
    current = jnp.where(lax.axis_index("step") == 0, window_start, previous[0])
    levels = step_levels[0]
    sigmas = noise_level(levels, level_count)
    sigma_low = sigmas[0]
    sigma_high = sigmas[1]
    spread = sigma_low * sigma_low + 0.25
    scale_in = lax.rsqrt(spread)
    scale_skip = 0.25 / spread
    scale_out = 0.5 * sigma_low * lax.rsqrt(spread)

    channels, band_rows, width = current.shape
    feat = lift_weight.shape[1]
    coarse_halo = with_halo(coarse, "rows", 1, HALO)
    current_halo = with_halo(current, "rows", 1, HALO)
    inputs = jnp.concatenate([(scale_in * current_halo).astype(jnp.bfloat16), coarse_halo], axis=0)
    inputs = inputs.reshape(inputs.shape[0], -1)
    picker = (jnp.arange(level_count) == levels[0]).astype(jnp.bfloat16)[None]
    embed_row = jnp.dot(picker, level_embed, preferred_element_type=jnp.float32)[0]

    def stack_taps(weight):
        return weight.transpose(1, 3, 0, 2).reshape(3 * feat, 3 * feat)

    tokens_per_row = width // 4
    pool_matrix = jnp.where(
        jnp.arange(width)[:, None] // 4 == jnp.arange(tokens_per_row)[None, :], 1.0 / 16.0, 0.0
    ).astype(jnp.float32)
    expand_matrix = jnp.where(
        jnp.arange(tokens_per_row)[:, None] == jnp.arange(width)[None, :] // 4, 1.0, 0.0
    ).astype(jnp.float32)
    band_index = lax.axis_index("rows").astype(jnp.int32).reshape(1)

    pixels = band_rows * width
    tokens = (band_rows // 4) * tokens_per_row
    trunk = pl.pallas_call(
        lambda *refs: trunk_kernel(*refs, width=width, band_rows=band_rows, bands=bands),
        out_shape=(
            jax.ShapeDtypeStruct((feat, pixels), jnp.float32),
            jax.ShapeDtypeStruct((feat, tokens), jnp.float32),
        ),
        in_specs=[pl.BlockSpec(memory_space=pltpu.SMEM)] + [vmem()] * 6,
        out_specs=(vmem(), vmem()),
        scratch_shapes=[
            pltpu.VMEM((feat, (band_rows + 2 * HALO) * width), jnp.bfloat16),
            pltpu.VMEM((feat, pixels), jnp.bfloat16),
            pltpu.VMEM((feat, (band_rows + 2) * width), jnp.bfloat16),
        ],
    )
    hidden, pooled = trunk(
        band_index,
        inputs,
        lift_weight.T,
        embed_row.reshape(feat, 1),
        stack_taps(conv_first),
        stack_taps(conv_second),
        pool_matrix,
    )

    head_count = feat // HEAD_DIM
    token_feats = normalize_features(pooled).astype(jnp.bfloat16)
    projected = jnp.dot(project_weight.T, token_feats, preferred_element_type=jnp.float32)
    queries = feature_map(projected[:feat]).reshape(head_count, HEAD_DIM, tokens)
    key_feats = feature_map(projected[feat : 2 * feat]).astype(jnp.bfloat16).reshape(head_count, HEAD_DIM, tokens)
    value_rows = projected[2 * feat :].astype(jnp.bfloat16).reshape(head_count, HEAD_DIM, tokens)
    summary_own = jnp.einsum("hdt,het->hde", key_feats, value_rows, preferred_element_type=jnp.float32)
    totals_own = jnp.sum(key_feats.astype(jnp.float32), axis=2)
    stats = band_sum(jnp.concatenate([summary_own, totals_own[:, None, :]], axis=1), "rows")
    summary = stats[:, :HEAD_DIM]
    totals = stats[:, HEAD_DIM]
    numerator = jnp.einsum("hdt,hde->het", queries, summary, precision=lax.Precision.HIGHEST)
    denominator = jnp.einsum("hdt,hd->ht", queries, totals, precision=lax.Precision.HIGHEST)
    context = (numerator / denominator[:, None, :]).reshape(feat, tokens).astype(jnp.bfloat16)
    mixed = jnp.dot(mix_weight.T, context, preferred_element_type=jnp.float32)

    out_w = jnp.zeros((16, feat), jnp.bfloat16).at[:channels].set(output_weight.T)
    head = pl.pallas_call(
        lambda *refs: head_kernel(*refs, width=width, band_rows=band_rows),
        out_shape=jax.ShapeDtypeStruct((8, pixels), jnp.float32),
        in_specs=[vmem()] * 4,
        out_specs=vmem(),
    )
    field = head(hidden, mixed, expand_matrix, out_w)
    out_field = field[:channels].reshape(channels, band_rows, width)

    denoised = scale_skip * current + scale_out * out_field
    drift_step = (sigma_high - sigma_low) * (current - denoised) / sigma_low
    summed = prefix_sum(drift_step, "step")
    trajectory = window_start + summed
    return (trajectory[None], denoised[None])


def solution(mesh):
    return jax.shard_map(
        local,
        mesh=mesh,
        in_specs=(
            P("step", "ens", "rows", None),
            P("ens", "rows", None),
            P("ens", "rows", None),
            P("step", None),
            P(),
            P(),
            P(),
            P(),
            P(),
            P(),
            P(),
        ),
        out_specs=(P("step", "ens", "rows", None), P("step", "ens", "rows", None)),
        check_vma=False,
    )
```

```python
import jax
import jax.numpy as jnp
from jax import lax
from jax.experimental import pallas as pl
from jax.experimental.pallas import tpu as pltpu
from jax.sharding import PartitionSpec as P

HEAD_DIM = 64
HALO = 2
CHUNK_ROWS = 2

SIGMA_TOP = 8.0
SIGMA_END = 0.002


def from_behind(x, axis, by):
    devices = lax.axis_size(axis)
    pairs = [(i, i + by) for i in range(devices) if 0 <= i + by < devices]
    return lax.ppermute(x, axis, pairs)


def with_halo(x, axis, dim, width):
    devices, length = (lax.axis_size(axis), x.shape[dim])
    last = lax.slice_in_dim(x, length - width, length, axis=dim)
    leading = lax.slice_in_dim(x, 0, width, axis=dim)
    if devices == 2:
        me = lax.axis_index(axis)
        outgoing = jnp.where(me == 0, last, leading)
        incoming = lax.ppermute(outgoing, axis, [(0, 1), (1, 0)])
        zero = jnp.zeros_like(incoming)
        before = jnp.where(me == 0, zero, incoming)
        after = jnp.where(me == 0, incoming, zero)
    else:
        up = [(i, i + 1) for i in range(devices - 1)]
        down = [(j, i) for i, j in up]
        before = lax.ppermute(last, axis, up)
        after = lax.ppermute(leading, axis, down)
    return jnp.concatenate([before, x, after], axis=dim)


def band_sum(x, axis):
    devices = lax.axis_size(axis)
    if devices == 2:
        return x + lax.ppermute(x, axis, [(0, 1), (1, 0)])
    return lax.psum(x, axis)


def prefix_sum(x, axis):
    devices = lax.axis_size(axis)
    shift = 1
    while shift < devices:
        pairs = [(i, i + shift) for i in range(devices - shift)]
        x = x + lax.ppermute(x, axis, pairs)
        shift *= 2
    return x


def noise_level(levels, level_count):
    fraction = levels.astype(jnp.float32) / jnp.float32(level_count - 1)
    return SIGMA_TOP * jnp.exp(fraction * jnp.log(jnp.float32(SIGMA_END / SIGMA_TOP)))


def normalize_features(values):
    mean_square = jnp.sum(values * values, axis=0, keepdims=True) * (1.0 / values.shape[0])
    return values * lax.rsqrt(mean_square + 1e-06)


def silu(values):
    return values / (1.0 + jnp.exp(-values))


def feature_map(values):
    return jnp.where(values > 0, values + 1.0, jnp.exp(jnp.minimum(values, 0.0)))


def conv_chunk(source, weight, first_row, rows, width, column):
    span = rows * width
    stacked = jnp.concatenate(
        [source[:, (first_row + i) * width : (first_row + i) * width + span] for i in range(3)],
        axis=0,
    )
    taps = jnp.dot(weight, stacked, preferred_element_type=jnp.float32)
    feat = taps.shape[0] // 3
    left = pltpu.roll(taps[0:feat], 1, 1)
    right = pltpu.roll(taps[2 * feat : 3 * feat], span - 1, 1)
    result = taps[feat : 2 * feat]
    result = result + jnp.where(column != 0, left, 0.0)
    result = result + jnp.where(column != width - 1, right, 0.0)
    return result


def transposed(block):
    return block.astype(jnp.float32).T


def stack_taps(weight_ref):
    return jnp.concatenate(
        [
            jnp.concatenate([transposed(weight_ref[i, j]) for i in range(3)], axis=1)
            for j in range(3)
        ],
        axis=0,
    ).astype(jnp.bfloat16)


def trunk_kernel(
    band_ref, inputs_ref, lift_ref, embed_ref, first_ref, second_ref, project_ref,
    hidden_ref, query_ref, stats_ref, act_first, lifted_keep, act_next, *, width, band_rows, bands,
):
    band = band_ref[0]
    top_outside = band == 0
    bottom_outside = band == bands - 1
    span = CHUNK_ROWS * width
    column = lax.broadcasted_iota(jnp.int32, (1, span), 1) % width
    upper_row = lax.broadcasted_iota(jnp.int32, (1, span), 1) < width
    lift_w = lift_ref[...]
    embed = embed_ref[...]
    in_rows = band_rows + 2 * HALO
    for q in range(in_rows // CHUNK_ROWS):
        start = q * span
        lifted = jnp.dot(lift_w, inputs_ref[:, start : start + span], preferred_element_type=jnp.float32)
        lifted = (lifted + embed).astype(jnp.bfloat16)
        row0 = q * CHUNK_ROWS
        if HALO <= row0 < HALO + band_rows:
            keep = (row0 - HALO) * width
            lifted_keep[:, keep : keep + span] = lifted
        act = silu(normalize_features(lifted.astype(jnp.float32)))
        if row0 < HALO:
            act = jnp.where(top_outside, 0.0, act)
        if row0 >= HALO + band_rows:
            act = jnp.where(bottom_outside, 0.0, act)
        act_first[:, start : start + span] = act.astype(jnp.bfloat16)
    first_w = stack_taps(first_ref)
    mid_rows = band_rows + 2
    for q in range(mid_rows // CHUNK_ROWS):
        start = q * span
        middle = conv_chunk(act_first, first_w, q * CHUNK_ROWS, CHUNK_ROWS, width, column)
        act = silu(normalize_features(middle))
        if q == 0:
            act = jnp.where(jnp.logical_and(top_outside, upper_row), 0.0, act)
        if q == mid_rows // CHUNK_ROWS - 1:
            act = jnp.where(jnp.logical_and(bottom_outside, jnp.logical_not(upper_row)), 0.0, act)
        act_next[:, start : start + span] = act.astype(jnp.bfloat16)
    second_w = stack_taps(second_ref)
    for q in range(band_rows // CHUNK_ROWS):
        start = q * span
        conv = conv_chunk(act_next, second_w, q * CHUNK_ROWS, CHUNK_ROWS, width, column)
        hidden_ref[:, start : start + span] = lifted_keep[:, start : start + span].astype(jnp.float32) + conv
    tokens_per_row = width // 4
    pool_w = jnp.where(
        lax.broadcasted_iota(jnp.int32, (width, tokens_per_row), 0) // 4
        == lax.broadcasted_iota(jnp.int32, (width, tokens_per_row), 1),
        1.0 / 16.0,
        0.0,
    ).astype(jnp.float32)
    pooled = []
    for a in range(band_rows // 4):
        row_sum = hidden_ref[:, (4 * a) * width : (4 * a + 1) * width]
        for u in range(1, 4):
            row_sum = row_sum + hidden_ref[:, (4 * a + u) * width : (4 * a + u + 1) * width]
        pooled.append(
            jnp.dot(row_sum, pool_w, precision=lax.Precision.HIGHEST, preferred_element_type=jnp.float32)
        )
    pooled = jnp.concatenate(pooled, axis=1)
    feat = pooled.shape[0]
    tokens = normalize_features(pooled).astype(jnp.bfloat16)
    project_t = jnp.concatenate(
        [transposed(project_ref[:, g * feat : (g + 1) * feat]) for g in range(3)], axis=0
    ).astype(jnp.bfloat16)
    projected = jnp.dot(project_t, tokens, preferred_element_type=jnp.float32)
    query_ref[...] = feature_map(projected[:feat])
    key_feats = feature_map(projected[feat : 2 * feat]).astype(jnp.bfloat16)
    value_rows = projected[2 * feat :].astype(jnp.bfloat16)
    ones = jnp.ones((HEAD_DIM, key_feats.shape[1]), jnp.bfloat16)
    contract_tokens = (((1,), (1,)), ((), ()))
    for h in range(feat // HEAD_DIM):
        keys_h = key_feats[h * HEAD_DIM : (h + 1) * HEAD_DIM]
        values_h = value_rows[h * HEAD_DIM : (h + 1) * HEAD_DIM]
        summary_t = lax.dot_general(values_h, keys_h, contract_tokens, preferred_element_type=jnp.float32)
        totals = lax.dot_general(ones, keys_h, contract_tokens, preferred_element_type=jnp.float32)
        stats_ref[h * HEAD_DIM : (h + 1) * HEAD_DIM, :] = jnp.concatenate([summary_t, totals], axis=1)


def head_kernel(
    scalar_ref, hidden_ref, query_ref, stats_ref, mix_ref, out_w_ref, current_ref,
    denoised_ref, drift_ref, *, width, band_rows,
):
    scale_skip = scalar_ref[0]
    scale_out = scalar_ref[1]
    sigma_gap = scalar_ref[2]
    sigma_low = scalar_ref[3]
    feat = query_ref.shape[0]
    contexts = []
    for h in range(feat // HEAD_DIM):
        rows = slice(h * HEAD_DIM, (h + 1) * HEAD_DIM)
        queries_h = query_ref[rows, :]
        numerator = jnp.dot(
            stats_ref[rows, 0:HEAD_DIM], queries_h,
            precision=lax.Precision.HIGHEST, preferred_element_type=jnp.float32,
        )
        denominator = jnp.dot(
            stats_ref[rows, HEAD_DIM : 2 * HEAD_DIM], queries_h,
            precision=lax.Precision.HIGHEST, preferred_element_type=jnp.float32,
        )
        contexts.append(numerator / denominator)
    context = jnp.concatenate(contexts, axis=0).astype(jnp.bfloat16)
    mix_t = transposed(mix_ref[...]).astype(jnp.bfloat16)
    mixed = jnp.dot(mix_t, context, preferred_element_type=jnp.float32)
    tokens_per_row = width // 4
    expand = jnp.where(
        lax.broadcasted_iota(jnp.int32, (tokens_per_row, width), 0)
        == lax.broadcasted_iota(jnp.int32, (tokens_per_row, width), 1) // 4,
        1.0,
        0.0,
    ).astype(jnp.float32)
    out_w = out_w_ref[...]
    channels = current_ref.shape[0]
    for a in range(band_rows // 4):
        spread = jnp.dot(
            mixed[:, a * tokens_per_row : (a + 1) * tokens_per_row],
            expand,
            precision=lax.Precision.HIGHEST,
            preferred_element_type=jnp.float32,
        )
        for u in range(4):
            r = 4 * a + u
            start = r * width
            combined = hidden_ref[:, start : start + width] + spread
            act = silu(normalize_features(combined)).astype(jnp.bfloat16)
            field = jnp.dot(out_w, act, preferred_element_type=jnp.float32)[0:channels]
            state = current_ref[:, r, :]
            denoised = scale_skip * state + scale_out * field
            denoised_ref[:, r, :] = denoised
            drift_ref[:, r, :] = sigma_gap * (state - denoised) / sigma_low


def vmem():
    return pl.BlockSpec(memory_space=pltpu.VMEM)


def smem():
    return pl.BlockSpec(memory_space=pltpu.SMEM)


def edge_rows(x, axis, dim, width):
    length = x.shape[dim]
    last = lax.slice_in_dim(x, length - width, length, axis=dim)
    leading = lax.slice_in_dim(x, 0, width, axis=dim)
    return jnp.where(lax.axis_index(axis) == 0, last, leading)


def place_halo(x, incoming, axis, dim):
    me = lax.axis_index(axis)
    zero = jnp.zeros_like(incoming)
    before = jnp.where(me == 0, zero, incoming)
    after = jnp.where(me == 0, incoming, zero)
    return jnp.concatenate([before, x, after], axis=dim)


def local(
    iterates,
    window_start,
    coarse,
    step_levels,
    level_embed,
    lift_weight,
    conv_first,
    conv_second,
    project_weight,
    mix_weight,
    output_weight,
):
    level_count = 2 * lax.axis_size("step") + 1
    bands = lax.axis_size("rows")
    steps = lax.axis_size("step")
    first_step = lax.axis_index("step") == 0
    previous = from_behind(iterates, "step", 1)
    if bands == 2:
        pairs = [(j * 2 + b, (j + 1) * 2 + (1 - b)) for j in range(steps - 1) for b in range(2)]
        iterate_halo = lax.ppermute(edge_rows(iterates[0], "rows", 1, HALO), ("step", "rows"), pairs)
        start_halo = lax.ppermute(edge_rows(window_start, "rows", 1, HALO), "rows", [(0, 1), (1, 0)])
        coarse_halo = lax.ppermute(edge_rows(coarse, "rows", 1, HALO), "rows", [(0, 1), (1, 0)])
    current = jnp.where(first_step, window_start, previous[0])
    if bands == 2:
        current_halo = place_halo(current, jnp.where(first_step, start_halo, iterate_halo), "rows", 1)
        coarse_halo = place_halo(coarse, coarse_halo, "rows", 1)
    else:
        current_halo = with_halo(current, "rows", 1, HALO)
        coarse_halo = with_halo(coarse, "rows", 1, HALO)
    levels = step_levels[0]
    sigmas = noise_level(levels, level_count)
    sigma_low = sigmas[0]
    sigma_high = sigmas[1]
    spread = sigma_low * sigma_low + 0.25
    scale_in = lax.rsqrt(spread)
    scale_skip = 0.25 / spread
    scale_out = 0.5 * sigma_low * lax.rsqrt(spread)

    channels, band_rows, width = current.shape
    feat = lift_weight.shape[1]
    inputs = jnp.concatenate([(scale_in * current_halo).astype(jnp.bfloat16), coarse_halo], axis=0)
    inputs = inputs.reshape(inputs.shape[0], -1)
    picker = (jnp.arange(level_count) == levels[0]).astype(jnp.bfloat16)[None]
    embed_row = jnp.dot(picker, level_embed, preferred_element_type=jnp.float32)[0]
    band_index = lax.axis_index("rows").astype(jnp.int32).reshape(1)

    pixels = band_rows * width
    tokens = (band_rows // 4) * (width // 4)
    trunk = pl.pallas_call(
        lambda *refs: trunk_kernel(*refs, width=width, band_rows=band_rows, bands=bands),
        out_shape=(
            jax.ShapeDtypeStruct((feat, pixels), jnp.float32),
            jax.ShapeDtypeStruct((feat, tokens), jnp.float32),
            jax.ShapeDtypeStruct((feat, 2 * HEAD_DIM), jnp.float32),
        ),
        in_specs=[smem()] + [vmem()] * 6,
        out_specs=(vmem(), vmem(), vmem()),
        scratch_shapes=[
            pltpu.VMEM((feat, (band_rows + 2 * HALO) * width), jnp.bfloat16),
            pltpu.VMEM((feat, pixels), jnp.bfloat16),
            pltpu.VMEM((feat, (band_rows + 2) * width), jnp.bfloat16),
        ],
    )
    hidden, queries, stats_own = trunk(
        band_index,
        inputs,
        lift_weight.T,
        embed_row.reshape(feat, 1),
        conv_first,
        conv_second,
        project_weight,
    )
    stats = band_sum(stats_own, "rows")

    out_w = jnp.pad(output_weight.T, ((0, 16 - channels), (0, 0)))
    scalars = jnp.stack([scale_skip, scale_out, sigma_high - sigma_low, sigma_low]).astype(jnp.float32)
    head = pl.pallas_call(
        lambda *refs: head_kernel(*refs, width=width, band_rows=band_rows),
        out_shape=(
            jax.ShapeDtypeStruct(current.shape, jnp.float32),
            jax.ShapeDtypeStruct(current.shape, jnp.float32),
        ),
        in_specs=[smem()] + [vmem()] * 6,
        out_specs=(vmem(), vmem()),
    )
    denoised, drift_step = head(scalars, hidden, queries, stats, mix_weight, out_w, current)
    summed = prefix_sum(drift_step, "step")
    trajectory = window_start + summed
    return (trajectory[None], denoised[None])


def solution(mesh):
    return jax.shard_map(
        local,
        mesh=mesh,
        in_specs=(
            P("step", "ens", "rows", None),
            P("ens", "rows", None),
            P("ens", "rows", None),
            P("step", None),
            P(),
            P(),
            P(),
            P(),
            P(),
            P(),
            P(),
        ),
        out_specs=(P("step", "ens", "rows", None), P("step", "ens", "rows", None)),
        check_vma=False,
    )
```

```python
import jax
import numpy as np
import jax.numpy as jnp
from jax import lax
from jax.experimental import pallas as pl
from jax.experimental.pallas import tpu as pltpu
from jax.sharding import PartitionSpec as P

HEAD_DIM = 64
HALO = 2
CHUNK_ROWS = 2

SIGMA_TOP = 8.0
SIGMA_END = 0.002
LOG_RATIO = float(np.log(np.float32(SIGMA_END / SIGMA_TOP)))


def from_behind(x, axis, by):
    devices = lax.axis_size(axis)
    pairs = [(i, i + by) for i in range(devices) if 0 <= i + by < devices]
    return lax.ppermute(x, axis, pairs)


def with_halo(x, axis, dim, width):
    devices, length = (lax.axis_size(axis), x.shape[dim])
    last = lax.slice_in_dim(x, length - width, length, axis=dim)
    leading = lax.slice_in_dim(x, 0, width, axis=dim)
    if devices == 2:
        me = lax.axis_index(axis)
        outgoing = jnp.where(me == 0, last, leading)
        incoming = lax.ppermute(outgoing, axis, [(0, 1), (1, 0)])
        zero = jnp.zeros_like(incoming)
        before = jnp.where(me == 0, zero, incoming)
        after = jnp.where(me == 0, incoming, zero)
    else:
        up = [(i, i + 1) for i in range(devices - 1)]
        down = [(j, i) for i, j in up]
        before = lax.ppermute(last, axis, up)
        after = lax.ppermute(leading, axis, down)
    return jnp.concatenate([before, x, after], axis=dim)


def band_sum(x, axis):
    devices = lax.axis_size(axis)
    if devices == 2:
        return x + lax.ppermute(x, axis, [(0, 1), (1, 0)])
    return lax.psum(x, axis)


def prefix_sum(x, axis):
    devices = lax.axis_size(axis)
    shift = 1
    while shift < devices:
        pairs = [(i, i + shift) for i in range(devices - shift)]
        x = x + lax.ppermute(x, axis, pairs)
        shift *= 2
    return x


def noise_level(levels, level_count):
    fraction = levels.astype(jnp.float32) / jnp.float32(level_count - 1)
    return SIGMA_TOP * jnp.exp(fraction * jnp.log(jnp.float32(SIGMA_END / SIGMA_TOP)))


def normalize_features(values):
    mean_square = jnp.sum(values * values, axis=0, keepdims=True) * (1.0 / values.shape[0])
    return values * lax.rsqrt(mean_square + 1e-06)


def silu(values):
    return values / (1.0 + jnp.exp(-values))


def feature_map(values):
    return jnp.where(values > 0, values + 1.0, jnp.exp(jnp.minimum(values, 0.0)))


def conv_chunk(source, weight, first_row, rows, width, column):
    span = rows * width
    stacked = jnp.concatenate(
        [source[:, (first_row + i) * width : (first_row + i) * width + span] for i in range(3)],
        axis=0,
    )
    taps = jnp.dot(weight, stacked, preferred_element_type=jnp.float32)
    feat = taps.shape[0] // 3
    left = pltpu.roll(taps[0:feat], 1, 1)
    right = pltpu.roll(taps[2 * feat : 3 * feat], span - 1, 1)
    result = taps[feat : 2 * feat]
    result = result + jnp.where(column != 0, left, 0.0)
    result = result + jnp.where(column != width - 1, right, 0.0)
    return result


def transposed(block):
    return block.astype(jnp.float32).T


def stack_taps(weight_ref):
    return jnp.concatenate(
        [
            jnp.concatenate([transposed(weight_ref[i, j]) for i in range(3)], axis=1)
            for j in range(3)
        ],
        axis=0,
    ).astype(jnp.bfloat16)


def step_scalars(levels_ref, level_count, shape):
    def sigma(k):
        level = jnp.full(shape, levels_ref[0, k].astype(jnp.float32))
        fraction = level / jnp.float32(level_count - 1)
        return SIGMA_TOP * jnp.exp(fraction * LOG_RATIO)

    sigma_low = sigma(0)
    sigma_high = sigma(1)
    spread = sigma_low * sigma_low + 0.25
    return sigma_low, sigma_high, spread


def trunk_kernel(
    levels_ref, previous_ref, start_ref, start_other_ref, iterate_halo_ref, coarse_ref,
    coarse_other_ref, lift_ref, embed_ref, first_ref, second_ref, project_ref,
    hidden_ref, query_ref, stats_ref, inputs, act_first, lifted_keep, act_next,
    *, width, band_rows, bands, level_count,
):
    band = lax.axis_index("rows")
    first_step = lax.axis_index("step") == 0
    top_outside = band == 0
    bottom_outside = band == bands - 1
    channels = start_ref.shape[0]
    sigma_low, _, spread = step_scalars(levels_ref, level_count, (1, width))
    scale_in = lax.rsqrt(spread)
    for u in range(band_rows + 2 * HALO):
        v = u - HALO
        if 0 <= v < band_rows:
            state = jnp.where(first_step, start_ref[:, v, :], previous_ref[0, :, v, :])
            cond = coarse_ref[:, v, :]
        elif v < 0:
            state = jnp.where(first_step, start_other_ref[:, band_rows + v, :], iterate_halo_ref[:, v + HALO, :])
            cond = coarse_other_ref[:, band_rows + v, :]
        else:
            state = jnp.where(first_step, start_other_ref[:, v - band_rows, :], iterate_halo_ref[:, v - band_rows, :])
            cond = coarse_other_ref[:, v - band_rows, :]
        scaled = (scale_in * state).astype(jnp.bfloat16).astype(jnp.float32)
        inputs[0:channels, u * width : (u + 1) * width] = scaled
        inputs[channels:, u * width : (u + 1) * width] = cond.astype(jnp.float32)
    level = levels_ref[0, 0]
    table = embed_ref[...].astype(jnp.float32)
    picked = jnp.where(lax.broadcasted_iota(jnp.int32, table.shape, 0) == level, table, 0.0)
    embed_row = jnp.sum(picked, axis=0, keepdims=True)
    feat = table.shape[1]
    embed = jnp.broadcast_to(embed_row, (feat, feat)).T[:, 0:1]
    lift_w = transposed(lift_ref[...]).astype(jnp.bfloat16)

    span = CHUNK_ROWS * width
    column = lax.broadcasted_iota(jnp.int32, (1, span), 1) % width
    upper_row = lax.broadcasted_iota(jnp.int32, (1, span), 1) < width
    in_rows = band_rows + 2 * HALO
    for q in range(in_rows // CHUNK_ROWS):
        start = q * span
        chunk = inputs[:, start : start + span].astype(jnp.bfloat16)
        lifted = jnp.dot(lift_w, chunk, preferred_element_type=jnp.float32)
        lifted = (lifted + embed).astype(jnp.bfloat16)
        row0 = q * CHUNK_ROWS
        if HALO <= row0 < HALO + band_rows:
            keep = (row0 - HALO) * width
            lifted_keep[:, keep : keep + span] = lifted
        act = silu(normalize_features(lifted.astype(jnp.float32)))
        if row0 < HALO:
            act = jnp.where(top_outside, 0.0, act)
        if row0 >= HALO + band_rows:
            act = jnp.where(bottom_outside, 0.0, act)
        act_first[:, start : start + span] = act.astype(jnp.bfloat16)
    first_w = stack_taps(first_ref)
    mid_rows = band_rows + 2
    for q in range(mid_rows // CHUNK_ROWS):
        start = q * span
        middle = conv_chunk(act_first, first_w, q * CHUNK_ROWS, CHUNK_ROWS, width, column)
        act = silu(normalize_features(middle))
        if q == 0:
            act = jnp.where(jnp.logical_and(top_outside, upper_row), 0.0, act)
        if q == mid_rows // CHUNK_ROWS - 1:
            act = jnp.where(jnp.logical_and(bottom_outside, jnp.logical_not(upper_row)), 0.0, act)
        act_next[:, start : start + span] = act.astype(jnp.bfloat16)
    second_w = stack_taps(second_ref)
    for q in range(band_rows // CHUNK_ROWS):
        start = q * span
        conv = conv_chunk(act_next, second_w, q * CHUNK_ROWS, CHUNK_ROWS, width, column)
        hidden_ref[:, start : start + span] = lifted_keep[:, start : start + span].astype(jnp.float32) + conv
    tokens_per_row = width // 4
    pool_w = jnp.where(
        lax.broadcasted_iota(jnp.int32, (width, tokens_per_row), 0) // 4
        == lax.broadcasted_iota(jnp.int32, (width, tokens_per_row), 1),
        1.0 / 16.0,
        0.0,
    ).astype(jnp.float32)
    pooled = []
    for a in range(band_rows // 4):
        row_sum = hidden_ref[:, (4 * a) * width : (4 * a + 1) * width]
        for u in range(1, 4):
            row_sum = row_sum + hidden_ref[:, (4 * a + u) * width : (4 * a + u + 1) * width]
        pooled.append(
            jnp.dot(row_sum, pool_w, precision=lax.Precision.HIGHEST, preferred_element_type=jnp.float32)
        )
    pooled = jnp.concatenate(pooled, axis=1)
    tokens = normalize_features(pooled).astype(jnp.bfloat16)
    project_t = jnp.concatenate(
        [transposed(project_ref[:, g * feat : (g + 1) * feat]) for g in range(3)], axis=0
    ).astype(jnp.bfloat16)
    projected = jnp.dot(project_t, tokens, preferred_element_type=jnp.float32)
    query_ref[...] = feature_map(projected[:feat])
    key_feats = feature_map(projected[feat : 2 * feat]).astype(jnp.bfloat16)
    value_rows = projected[2 * feat :].astype(jnp.bfloat16)
    ones = jnp.ones((HEAD_DIM, key_feats.shape[1]), jnp.bfloat16)
    contract_tokens = (((1,), (1,)), ((), ()))
    for h in range(feat // HEAD_DIM):
        keys_h = key_feats[h * HEAD_DIM : (h + 1) * HEAD_DIM]
        values_h = value_rows[h * HEAD_DIM : (h + 1) * HEAD_DIM]
        summary_t = lax.dot_general(values_h, keys_h, contract_tokens, preferred_element_type=jnp.float32)
        totals = lax.dot_general(ones, keys_h, contract_tokens, preferred_element_type=jnp.float32)
        stats_ref[h * HEAD_DIM : (h + 1) * HEAD_DIM, :] = jnp.concatenate([summary_t, totals], axis=1)


def head_kernel(
    levels_ref, hidden_ref, query_ref, stats_own_ref, stats_other_ref, mix_ref, out_w_ref,
    previous_ref, start_ref, denoised_ref, seed_ref, *, width, band_rows, level_count,
):
    first_step = lax.axis_index("step") == 0
    sigma_low, sigma_high, spread = step_scalars(levels_ref, level_count, (1, width))
    scale_skip = 0.25 / spread
    scale_out = 0.5 * sigma_low * lax.rsqrt(spread)
    sigma_gap = sigma_high - sigma_low
    feat = query_ref.shape[0]
    contexts = []
    for h in range(feat // HEAD_DIM):
        rows = slice(h * HEAD_DIM, (h + 1) * HEAD_DIM)
        queries_h = query_ref[rows, :]
        stats_h = stats_own_ref[rows, :] + stats_other_ref[rows, :]
        numerator = jnp.dot(
            stats_h[:, 0:HEAD_DIM], queries_h,
            precision=lax.Precision.HIGHEST, preferred_element_type=jnp.float32,
        )
        denominator = jnp.dot(
            stats_h[:, HEAD_DIM : 2 * HEAD_DIM], queries_h,
            precision=lax.Precision.HIGHEST, preferred_element_type=jnp.float32,
        )
        contexts.append(numerator / denominator)
    context = jnp.concatenate(contexts, axis=0).astype(jnp.bfloat16)
    mix_t = transposed(mix_ref[...]).astype(jnp.bfloat16)
    mixed = jnp.dot(mix_t, context, preferred_element_type=jnp.float32)
    tokens_per_row = width // 4
    expand = jnp.where(
        lax.broadcasted_iota(jnp.int32, (tokens_per_row, width), 0)
        == lax.broadcasted_iota(jnp.int32, (tokens_per_row, width), 1) // 4,
        1.0,
        0.0,
    ).astype(jnp.float32)
    out_w = transposed(out_w_ref[...]).astype(jnp.bfloat16)
    for a in range(band_rows // 4):
        spread_mixed = jnp.dot(
            mixed[:, a * tokens_per_row : (a + 1) * tokens_per_row],
            expand,
            precision=lax.Precision.HIGHEST,
            preferred_element_type=jnp.float32,
        )
        for u in range(4):
            r = 4 * a + u
            start = r * width
            combined = hidden_ref[:, start : start + width] + spread_mixed
            act = silu(normalize_features(combined)).astype(jnp.bfloat16)
            field = jnp.dot(out_w, act, preferred_element_type=jnp.float32)
            state = jnp.where(first_step, start_ref[:, r, :], previous_ref[0, :, r, :])
            denoised = scale_skip * state + scale_out * field
            denoised_ref[:, r, :] = denoised
            drift = sigma_gap * (state - denoised) / sigma_low
            seed_ref[:, r, :] = drift + jnp.where(first_step, state, 0.0)


def vmem():
    return pl.BlockSpec(memory_space=pltpu.VMEM)


def smem():
    return pl.BlockSpec(memory_space=pltpu.SMEM)


def edge_rows(x, axis, dim, width):
    length = x.shape[dim]
    last = lax.slice_in_dim(x, length - width, length, axis=dim)
    leading = lax.slice_in_dim(x, 0, width, axis=dim)
    return jnp.where(lax.axis_index(axis) == 0, last, leading)


def local(
    iterates,
    window_start,
    coarse,
    step_levels,
    level_embed,
    lift_weight,
    conv_first,
    conv_second,
    project_weight,
    mix_weight,
    output_weight,
):
    level_count = 2 * lax.axis_size("step") + 1
    bands = lax.axis_size("rows")
    steps = lax.axis_size("step")
    assert bands == 2
    swap = [(0, 1), (1, 0)]
    previous = from_behind(iterates, "step", 1)
    pairs = [(j * 2 + b, (j + 1) * 2 + (1 - b)) for j in range(steps - 1) for b in range(2)]
    iterate_halo = lax.ppermute(edge_rows(iterates[0], "rows", 1, HALO), ("step", "rows"), pairs)
    start_other = lax.ppermute(window_start, "rows", swap)
    coarse_other = lax.ppermute(coarse, "rows", swap)

    channels, band_rows, width = window_start.shape
    feat = lift_weight.shape[1]
    pixels = band_rows * width
    tokens = (band_rows // 4) * (width // 4)
    trunk = pl.pallas_call(
        lambda *refs: trunk_kernel(
            *refs, width=width, band_rows=band_rows, bands=bands, level_count=level_count
        ),
        out_shape=(
            jax.ShapeDtypeStruct((feat, pixels), jnp.float32),
            jax.ShapeDtypeStruct((feat, tokens), jnp.float32),
            jax.ShapeDtypeStruct((feat, 2 * HEAD_DIM), jnp.float32),
        ),
        in_specs=[smem()] + [vmem()] * 11,
        out_specs=(vmem(), vmem(), vmem()),
        scratch_shapes=[
            pltpu.VMEM((channels + coarse.shape[0], (band_rows + 2 * HALO) * width), jnp.float32),
            pltpu.VMEM((feat, (band_rows + 2 * HALO) * width), jnp.bfloat16),
            pltpu.VMEM((feat, pixels), jnp.bfloat16),
            pltpu.VMEM((feat, (band_rows + 2) * width), jnp.bfloat16),
        ],
    )
    hidden, queries, stats_own = trunk(
        step_levels,
        previous,
        window_start,
        start_other,
        iterate_halo,
        coarse,
        coarse_other,
        lift_weight,
        level_embed,
        conv_first,
        conv_second,
        project_weight,
    )
    stats_other = lax.ppermute(stats_own, "rows", swap)

    head = pl.pallas_call(
        lambda *refs: head_kernel(*refs, width=width, band_rows=band_rows, level_count=level_count),
        out_shape=(
            jax.ShapeDtypeStruct(window_start.shape, jnp.float32),
            jax.ShapeDtypeStruct(window_start.shape, jnp.float32),
        ),
        in_specs=[smem()] + [vmem()] * 8,
        out_specs=(vmem(), vmem()),
    )
    denoised, seed = head(
        step_levels, hidden, queries, stats_own, stats_other, mix_weight, output_weight,
        previous, window_start,
    )
    trajectory = prefix_sum(seed, "step")
    return (trajectory[None], denoised[None])


def solution(mesh):
    return jax.shard_map(
        local,
        mesh=mesh,
        in_specs=(
            P("step", "ens", "rows", None),
            P("ens", "rows", None),
            P("ens", "rows", None),
            P("step", None),
            P(),
            P(),
            P(),
            P(),
            P(),
            P(),
            P(),
        ),
        out_specs=(P("step", "ens", "rows", None), P("step", "ens", "rows", None)),
        check_vma=False,
    )
```

```python
import jax
import numpy as np
import jax.numpy as jnp
from jax import lax
from jax.experimental import pallas as pl
from jax.experimental.pallas import tpu as pltpu
from jax.sharding import PartitionSpec as P

HEAD_DIM = 64
HALO = 2
CHUNK_ROWS = 2
CONV_ROWS = 4

SIGMA_TOP = 8.0
SIGMA_END = 0.002
LOG_RATIO = float(np.log(np.float32(SIGMA_END / SIGMA_TOP)))


def from_behind(x, axis, by):
    devices = lax.axis_size(axis)
    pairs = [(i, i + by) for i in range(devices) if 0 <= i + by < devices]
    return lax.ppermute(x, axis, pairs)


def with_halo(x, axis, dim, width):
    devices, length = (lax.axis_size(axis), x.shape[dim])
    last = lax.slice_in_dim(x, length - width, length, axis=dim)
    leading = lax.slice_in_dim(x, 0, width, axis=dim)
    if devices == 2:
        me = lax.axis_index(axis)
        outgoing = jnp.where(me == 0, last, leading)
        incoming = lax.ppermute(outgoing, axis, [(0, 1), (1, 0)])
        zero = jnp.zeros_like(incoming)
        before = jnp.where(me == 0, zero, incoming)
        after = jnp.where(me == 0, incoming, zero)
    else:
        up = [(i, i + 1) for i in range(devices - 1)]
        down = [(j, i) for i, j in up]
        before = lax.ppermute(last, axis, up)
        after = lax.ppermute(leading, axis, down)
    return jnp.concatenate([before, x, after], axis=dim)


def band_sum(x, axis):
    devices = lax.axis_size(axis)
    if devices == 2:
        return x + lax.ppermute(x, axis, [(0, 1), (1, 0)])
    return lax.psum(x, axis)


def prefix_sum(x, axis):
    devices = lax.axis_size(axis)
    shift = 1
    while shift < devices:
        pairs = [(i, i + shift) for i in range(devices - shift)]
        x = x + lax.ppermute(x, axis, pairs)
        shift *= 2
    return x


def noise_level(levels, level_count):
    fraction = levels.astype(jnp.float32) / jnp.float32(level_count - 1)
    return SIGMA_TOP * jnp.exp(fraction * jnp.log(jnp.float32(SIGMA_END / SIGMA_TOP)))


def normalize_features(values):
    mean_square = jnp.sum(values * values, axis=0, keepdims=True) * (1.0 / values.shape[0])
    return values * lax.rsqrt(mean_square + 1e-06)


def silu(values):
    return values / (1.0 + jnp.exp(-values))


def feature_map(values):
    return jnp.where(values > 0, values + 1.0, jnp.exp(jnp.minimum(values, 0.0)))


def conv_chunk(source, weight, first_row, rows, width, column):
    span = rows * width
    stacked = jnp.concatenate(
        [source[:, (first_row + i) * width : (first_row + i) * width + span] for i in range(3)],
        axis=0,
    )
    taps = jnp.dot(weight, stacked, preferred_element_type=jnp.float32)
    feat = taps.shape[0] // 3
    left = pltpu.roll(taps[0:feat], 1, 1)
    right = pltpu.roll(taps[2 * feat : 3 * feat], span - 1, 1)
    result = taps[feat : 2 * feat]
    result = result + jnp.where(column != 0, left, 0.0)
    result = result + jnp.where(column != width - 1, right, 0.0)
    return result


def row_chunks(rows):
    chunks, first = [], 0
    while first < rows:
        size = min(CONV_ROWS, rows - first)
        chunks.append((first, size))
        first += size
    return chunks


def transposed(block):
    return block.astype(jnp.float32).T


def stack_taps(weight_ref):
    return jnp.concatenate(
        [
            jnp.concatenate([transposed(weight_ref[i, j]) for i in range(3)], axis=1)
            for j in range(3)
        ],
        axis=0,
    ).astype(jnp.bfloat16)


def step_scalars(levels_ref, level_count, shape):
    def sigma(k):
        level = jnp.full(shape, levels_ref[0, k].astype(jnp.float32))
        fraction = level / jnp.float32(level_count - 1)
        return SIGMA_TOP * jnp.exp(fraction * LOG_RATIO)

    sigma_low = sigma(0)
    sigma_high = sigma(1)
    spread = sigma_low * sigma_low + 0.25
    return sigma_low, sigma_high, spread


def trunk_kernel(
    levels_ref, previous_ref, start_ref, start_other_ref, previous_other_ref, coarse_ref,
    coarse_other_ref, lift_ref, embed_ref, first_ref, second_ref, project_ref,
    hidden_ref, query_ref, stats_ref, inputs, act_first, lifted_keep, act_next,
    *, width, band_rows, bands, level_count,
):
    band = lax.axis_index("rows")
    first_step = lax.axis_index("step") == 0
    top_outside = band == 0
    bottom_outside = band == bands - 1
    channels = start_ref.shape[0]
    sigma_low, _, spread = step_scalars(levels_ref, level_count, (1, width))
    scale_in = lax.rsqrt(spread)
    for u in range(band_rows + 2 * HALO):
        v = u - HALO
        if 0 <= v < band_rows:
            state = jnp.where(first_step, start_ref[:, v, :], previous_ref[0, :, v, :])
            cond = coarse_ref[:, v, :]
        elif v < 0:
            state = jnp.where(first_step, start_other_ref[:, band_rows + v, :], previous_other_ref[0, :, band_rows + v, :])
            cond = coarse_other_ref[:, band_rows + v, :]
        else:
            state = jnp.where(first_step, start_other_ref[:, v - band_rows, :], previous_other_ref[0, :, v - band_rows, :])
            cond = coarse_other_ref[:, v - band_rows, :]
        scaled = (scale_in * state).astype(jnp.bfloat16).astype(jnp.float32)
        inputs[0:channels, u * width : (u + 1) * width] = scaled
        inputs[channels:, u * width : (u + 1) * width] = cond.astype(jnp.float32)
    level = levels_ref[0, 0]
    table = embed_ref[...].astype(jnp.float32)
    picked = jnp.where(lax.broadcasted_iota(jnp.int32, table.shape, 0) == level, table, 0.0)
    embed_row = jnp.sum(picked, axis=0, keepdims=True)
    feat = table.shape[1]
    embed = jnp.broadcast_to(embed_row, (feat, feat)).T[:, 0:1]
    lift_w = transposed(lift_ref[...]).astype(jnp.bfloat16)

    span = CHUNK_ROWS * width
    in_rows = band_rows + 2 * HALO
    for q in range(in_rows // CHUNK_ROWS):
        start = q * span
        chunk = inputs[:, start : start + span].astype(jnp.bfloat16)
        lifted = jnp.dot(lift_w, chunk, preferred_element_type=jnp.float32)
        lifted = (lifted + embed).astype(jnp.bfloat16)
        row0 = q * CHUNK_ROWS
        if HALO <= row0 < HALO + band_rows:
            keep = (row0 - HALO) * width
            lifted_keep[:, keep : keep + span] = lifted
        act = silu(normalize_features(lifted.astype(jnp.float32)))
        if row0 < HALO:
            act = jnp.where(top_outside, 0.0, act)
        if row0 >= HALO + band_rows:
            act = jnp.where(bottom_outside, 0.0, act)
        act_first[:, start : start + span] = act.astype(jnp.bfloat16)
    first_w = stack_taps(first_ref)
    mid_rows = band_rows + 2
    chunks = row_chunks(mid_rows)
    for q, (first, rows) in enumerate(chunks):
        span = rows * width
        lanes = lax.broadcasted_iota(jnp.int32, (1, span), 1)
        middle = conv_chunk(act_first, first_w, first, rows, width, lanes % width)
        act = silu(normalize_features(middle))
        if q == 0:
            act = jnp.where(jnp.logical_and(top_outside, lanes < width), 0.0, act)
        if q == len(chunks) - 1:
            act = jnp.where(jnp.logical_and(bottom_outside, lanes >= span - width), 0.0, act)
        act_next[:, first * width : first * width + span] = act.astype(jnp.bfloat16)
    second_w = stack_taps(second_ref)
    for first, rows in row_chunks(band_rows):
        span = rows * width
        lanes = lax.broadcasted_iota(jnp.int32, (1, span), 1)
        conv = conv_chunk(act_next, second_w, first, rows, width, lanes % width)
        start = first * width
        hidden_ref[:, start : start + span] = lifted_keep[:, start : start + span].astype(jnp.float32) + conv
    tokens_per_row = width // 4
    pool_w = jnp.where(
        lax.broadcasted_iota(jnp.int32, (width, tokens_per_row), 0) // 4
        == lax.broadcasted_iota(jnp.int32, (width, tokens_per_row), 1),
        1.0 / 16.0,
        0.0,
    ).astype(jnp.float32)
    pooled = []
    for a in range(band_rows // 4):
        row_sum = hidden_ref[:, (4 * a) * width : (4 * a + 1) * width]
        for u in range(1, 4):
            row_sum = row_sum + hidden_ref[:, (4 * a + u) * width : (4 * a + u + 1) * width]
        pooled.append(
            jnp.dot(row_sum, pool_w, precision=lax.Precision.HIGHEST, preferred_element_type=jnp.float32)
        )
    pooled = jnp.concatenate(pooled, axis=1)
    tokens = normalize_features(pooled).astype(jnp.bfloat16)
    project_t = jnp.concatenate(
        [transposed(project_ref[:, g * feat : (g + 1) * feat]) for g in range(3)], axis=0
    ).astype(jnp.bfloat16)
    projected = jnp.dot(project_t, tokens, preferred_element_type=jnp.float32)
    query_ref[...] = feature_map(projected[:feat])
    key_feats = feature_map(projected[feat : 2 * feat]).astype(jnp.bfloat16)
    value_rows = projected[2 * feat :].astype(jnp.bfloat16)
    ones = jnp.ones((HEAD_DIM, key_feats.shape[1]), jnp.bfloat16)
    contract_tokens = (((1,), (1,)), ((), ()))
    for h in range(feat // HEAD_DIM):
        keys_h = key_feats[h * HEAD_DIM : (h + 1) * HEAD_DIM]
        values_h = value_rows[h * HEAD_DIM : (h + 1) * HEAD_DIM]
        summary_t = lax.dot_general(values_h, keys_h, contract_tokens, preferred_element_type=jnp.float32)
        totals = lax.dot_general(ones, keys_h, contract_tokens, preferred_element_type=jnp.float32)
        stats_ref[h * HEAD_DIM : (h + 1) * HEAD_DIM, :] = jnp.concatenate([summary_t, totals], axis=1)


def head_kernel(
    levels_ref, hidden_ref, query_ref, stats_own_ref, stats_other_ref, mix_ref, out_w_ref,
    previous_ref, start_ref, denoised_ref, seed_ref, *, width, band_rows, level_count,
):
    first_step = lax.axis_index("step") == 0
    sigma_low, sigma_high, spread = step_scalars(levels_ref, level_count, (1, width))
    scale_skip = 0.25 / spread
    scale_out = 0.5 * sigma_low * lax.rsqrt(spread)
    sigma_gap = sigma_high - sigma_low
    feat = query_ref.shape[0]
    contexts = []
    for h in range(feat // HEAD_DIM):
        rows = slice(h * HEAD_DIM, (h + 1) * HEAD_DIM)
        queries_h = query_ref[rows, :]
        stats_h = stats_own_ref[rows, :] + stats_other_ref[rows, :]
        numerator = jnp.dot(
            stats_h[:, 0:HEAD_DIM], queries_h,
            precision=lax.Precision.HIGHEST, preferred_element_type=jnp.float32,
        )
        denominator = jnp.dot(
            stats_h[:, HEAD_DIM : 2 * HEAD_DIM], queries_h,
            precision=lax.Precision.HIGHEST, preferred_element_type=jnp.float32,
        )
        contexts.append(numerator / denominator)
    context = jnp.concatenate(contexts, axis=0).astype(jnp.bfloat16)
    mix_t = transposed(mix_ref[...]).astype(jnp.bfloat16)
    mixed = jnp.dot(mix_t, context, preferred_element_type=jnp.float32)
    tokens_per_row = width // 4
    expand = jnp.where(
        lax.broadcasted_iota(jnp.int32, (tokens_per_row, width), 0)
        == lax.broadcasted_iota(jnp.int32, (tokens_per_row, width), 1) // 4,
        1.0,
        0.0,
    ).astype(jnp.float32)
    out_w = out_w_ref[...]
    for a in range(band_rows // 4):
        spread_mixed = jnp.dot(
            mixed[:, a * tokens_per_row : (a + 1) * tokens_per_row],
            expand,
            precision=lax.Precision.HIGHEST,
            preferred_element_type=jnp.float32,
        )
        for u in range(4):
            r = 4 * a + u
            start = r * width
            combined = hidden_ref[:, start : start + width] + spread_mixed
            act = silu(normalize_features(combined)).astype(jnp.bfloat16)
            field = jnp.dot(out_w, act, preferred_element_type=jnp.float32)
            state = jnp.where(first_step, start_ref[:, r, :], previous_ref[0, :, r, :])
            denoised = scale_skip * state + scale_out * field
            denoised_ref[:, r, :] = denoised
            drift = sigma_gap * (state - denoised) / sigma_low
            seed_ref[:, r, :] = drift + jnp.where(first_step, state, 0.0)


def vmem():
    return pl.BlockSpec(memory_space=pltpu.VMEM)


def smem():
    return pl.BlockSpec(memory_space=pltpu.SMEM)


def edge_rows(x, axis, dim, width):
    length = x.shape[dim]
    last = lax.slice_in_dim(x, length - width, length, axis=dim)
    leading = lax.slice_in_dim(x, 0, width, axis=dim)
    return jnp.where(lax.axis_index(axis) == 0, last, leading)


def local(
    iterates,
    window_start,
    coarse,
    step_levels,
    level_embed,
    lift_weight,
    conv_first,
    conv_second,
    project_weight,
    mix_weight,
    output_weight,
):
    level_count = 2 * lax.axis_size("step") + 1
    bands = lax.axis_size("rows")
    steps = lax.axis_size("step")
    assert bands == 2
    swap = [(0, 1), (1, 0)]
    previous = from_behind(iterates, "step", 1)
    previous_other = lax.ppermute(previous, "rows", swap)
    start_other = lax.ppermute(window_start, "rows", swap)
    coarse_other = lax.ppermute(coarse, "rows", swap)

    channels, band_rows, width = window_start.shape
    feat = lift_weight.shape[1]
    pixels = band_rows * width
    tokens = (band_rows // 4) * (width // 4)
    trunk = pl.pallas_call(
        lambda *refs: trunk_kernel(
            *refs, width=width, band_rows=band_rows, bands=bands, level_count=level_count
        ),
        out_shape=(
            jax.ShapeDtypeStruct((feat, pixels), jnp.float32),
            jax.ShapeDtypeStruct((feat, tokens), jnp.float32),
            jax.ShapeDtypeStruct((feat, 2 * HEAD_DIM), jnp.float32),
        ),
        in_specs=[smem()] + [vmem()] * 11,
        out_specs=(vmem(), vmem(), vmem()),
        scratch_shapes=[
            pltpu.VMEM((channels + coarse.shape[0], (band_rows + 2 * HALO) * width), jnp.float32),
            pltpu.VMEM((feat, (band_rows + 2 * HALO) * width), jnp.bfloat16),
            pltpu.VMEM((feat, pixels), jnp.bfloat16),
            pltpu.VMEM((feat, (band_rows + 2) * width), jnp.bfloat16),
        ],
    )
    hidden, queries, stats_own = trunk(
        step_levels,
        previous,
        window_start,
        start_other,
        previous_other,
        coarse,
        coarse_other,
        lift_weight,
        level_embed,
        conv_first,
        conv_second,
        project_weight,
    )
    stats_other = lax.ppermute(stats_own, "rows", swap)

    head = pl.pallas_call(
        lambda *refs: head_kernel(*refs, width=width, band_rows=band_rows, level_count=level_count),
        out_shape=(
            jax.ShapeDtypeStruct(window_start.shape, jnp.float32),
            jax.ShapeDtypeStruct(window_start.shape, jnp.float32),
        ),
        in_specs=[smem()] + [vmem()] * 8,
        out_specs=(vmem(), vmem()),
    )
    denoised, seed = head(
        step_levels, hidden, queries, stats_own, stats_other, mix_weight, output_weight.T,
        previous, window_start,
    )
    trajectory = prefix_sum(seed, "step")
    return (trajectory[None], denoised[None])


def solution(mesh):
    return jax.shard_map(
        local,
        mesh=mesh,
        in_specs=(
            P("step", "ens", "rows", None),
            P("ens", "rows", None),
            P("ens", "rows", None),
            P("step", None),
            P(),
            P(),
            P(),
            P(),
            P(),
            P(),
            P(),
        ),
        out_specs=(P("step", "ens", "rows", None), P("step", "ens", "rows", None)),
        check_vma=False,
    )
```

```python
import jax
import numpy as np
import jax.numpy as jnp
from jax import lax
from jax.experimental import pallas as pl
from jax.experimental.pallas import tpu as pltpu
from jax.sharding import PartitionSpec as P

HEAD_DIM = 64
HALO = 2
CHUNK_ROWS = 2
CONV_ROWS = 4

SIGMA_TOP = 8.0
SIGMA_END = 0.002
LOG_RATIO = float(np.log(np.float32(SIGMA_END / SIGMA_TOP)))


def from_behind(x, axis, by):
    devices = lax.axis_size(axis)
    pairs = [(i, i + by) for i in range(devices) if 0 <= i + by < devices]
    return lax.ppermute(x, axis, pairs)


def with_halo(x, axis, dim, width):
    devices, length = (lax.axis_size(axis), x.shape[dim])
    last = lax.slice_in_dim(x, length - width, length, axis=dim)
    leading = lax.slice_in_dim(x, 0, width, axis=dim)
    if devices == 2:
        me = lax.axis_index(axis)
        outgoing = jnp.where(me == 0, last, leading)
        incoming = lax.ppermute(outgoing, axis, [(0, 1), (1, 0)])
        zero = jnp.zeros_like(incoming)
        before = jnp.where(me == 0, zero, incoming)
        after = jnp.where(me == 0, incoming, zero)
    else:
        up = [(i, i + 1) for i in range(devices - 1)]
        down = [(j, i) for i, j in up]
        before = lax.ppermute(last, axis, up)
        after = lax.ppermute(leading, axis, down)
    return jnp.concatenate([before, x, after], axis=dim)


def band_sum(x, axis):
    devices = lax.axis_size(axis)
    if devices == 2:
        return x + lax.ppermute(x, axis, [(0, 1), (1, 0)])
    return lax.psum(x, axis)


def prefix_sum(x, axis):
    devices = lax.axis_size(axis)
    shift = 1
    while shift < devices:
        pairs = [(i, i + shift) for i in range(devices - shift)]
        x = x + lax.ppermute(x, axis, pairs)
        shift *= 2
    return x


def noise_level(levels, level_count):
    fraction = levels.astype(jnp.float32) / jnp.float32(level_count - 1)
    return SIGMA_TOP * jnp.exp(fraction * jnp.log(jnp.float32(SIGMA_END / SIGMA_TOP)))


def normalize_features(values):
    mean_square = jnp.sum(values * values, axis=0, keepdims=True) * (1.0 / values.shape[0])
    return values * lax.rsqrt(mean_square + 1e-06)


def silu(values):
    half = 0.5 * values
    return half + half * jnp.tanh(half)


def feature_map(values):
    return jnp.where(values > 0, values + 1.0, jnp.exp(jnp.minimum(values, 0.0)))


def conv_chunk(source, weight, first_row, rows, width, column):
    span = rows * width
    stacked = jnp.concatenate(
        [source[:, (first_row + i) * width : (first_row + i) * width + span] for i in range(3)],
        axis=0,
    )
    taps = jnp.dot(weight, stacked, preferred_element_type=jnp.float32)
    feat = taps.shape[0] // 3
    left = pltpu.roll(taps[0:feat], 1, 1)
    right = pltpu.roll(taps[2 * feat : 3 * feat], span - 1, 1)
    result = taps[feat : 2 * feat]
    result = result + jnp.where(column != 0, left, 0.0)
    result = result + jnp.where(column != width - 1, right, 0.0)
    return result


def row_chunks(rows):
    chunks, first = [], 0
    while first < rows:
        size = min(CONV_ROWS, rows - first)
        chunks.append((first, size))
        first += size
    return chunks


def transposed(block):
    return block.astype(jnp.float32).T


def stack_taps(weight_ref):
    return jnp.concatenate(
        [
            jnp.concatenate([transposed(weight_ref[i, j]) for i in range(3)], axis=1)
            for j in range(3)
        ],
        axis=0,
    ).astype(jnp.bfloat16)


def step_scalars(levels_ref, level_count, shape):
    def sigma(k):
        level = jnp.full(shape, levels_ref[0, k].astype(jnp.float32))
        fraction = level / jnp.float32(level_count - 1)
        return SIGMA_TOP * jnp.exp(fraction * LOG_RATIO)

    sigma_low = sigma(0)
    sigma_high = sigma(1)
    spread = sigma_low * sigma_low + 0.25
    return sigma_low, sigma_high, spread


def trunk_kernel(
    levels_ref, previous_ref, start_ref, start_other_ref, previous_other_ref, coarse_ref,
    coarse_other_ref, lift_ref, embed_ref, first_ref, second_ref, project_ref,
    hidden_ref, query_ref, stats_ref, inputs, act_first, lifted_keep, act_next,
    *, width, band_rows, bands, level_count,
):
    band = lax.axis_index("rows")
    first_step = lax.axis_index("step") == 0
    top_outside = band == 0
    bottom_outside = band == bands - 1
    channels = start_ref.shape[0]
    sigma_low, _, spread = step_scalars(levels_ref, level_count, (1, width))
    scale_in = lax.rsqrt(spread)
    for u in range(band_rows + 2 * HALO):
        v = u - HALO
        if 0 <= v < band_rows:
            state = jnp.where(first_step, start_ref[:, v, :], previous_ref[0, :, v, :])
            cond = coarse_ref[:, v, :]
        elif v < 0:
            state = jnp.where(first_step, start_other_ref[:, band_rows + v, :], previous_other_ref[0, :, band_rows + v, :])
            cond = coarse_other_ref[:, band_rows + v, :]
        else:
            state = jnp.where(first_step, start_other_ref[:, v - band_rows, :], previous_other_ref[0, :, v - band_rows, :])
            cond = coarse_other_ref[:, v - band_rows, :]
        scaled = (scale_in * state).astype(jnp.bfloat16).astype(jnp.float32)
        inputs[0:channels, u * width : (u + 1) * width] = scaled
        inputs[channels:, u * width : (u + 1) * width] = cond.astype(jnp.float32)
    level = levels_ref[0, 0]
    table = embed_ref[...].astype(jnp.float32)
    picked = jnp.where(lax.broadcasted_iota(jnp.int32, table.shape, 0) == level, table, 0.0)
    embed_row = jnp.sum(picked, axis=0, keepdims=True)
    feat = table.shape[1]
    embed = jnp.broadcast_to(embed_row, (feat, feat)).T[:, 0:1]
    lift_w = transposed(lift_ref[...]).astype(jnp.bfloat16)

    span = CHUNK_ROWS * width
    in_rows = band_rows + 2 * HALO
    for q in range(in_rows // CHUNK_ROWS):
        start = q * span
        chunk = inputs[:, start : start + span].astype(jnp.bfloat16)
        lifted = jnp.dot(lift_w, chunk, preferred_element_type=jnp.float32)
        lifted = (lifted + embed).astype(jnp.bfloat16)
        row0 = q * CHUNK_ROWS
        if HALO <= row0 < HALO + band_rows:
            keep = (row0 - HALO) * width
            lifted_keep[:, keep : keep + span] = lifted
        act = silu(normalize_features(lifted.astype(jnp.float32)))
        if row0 < HALO:
            act = jnp.where(top_outside, 0.0, act)
        if row0 >= HALO + band_rows:
            act = jnp.where(bottom_outside, 0.0, act)
        act_first[:, start : start + span] = act.astype(jnp.bfloat16)
    first_w = stack_taps(first_ref)
    mid_rows = band_rows + 2
    chunks = row_chunks(mid_rows)
    for q, (first, rows) in enumerate(chunks):
        span = rows * width
        lanes = lax.broadcasted_iota(jnp.int32, (1, span), 1)
        middle = conv_chunk(act_first, first_w, first, rows, width, lanes % width)
        act = silu(normalize_features(middle))
        if q == 0:
            act = jnp.where(jnp.logical_and(top_outside, lanes < width), 0.0, act)
        if q == len(chunks) - 1:
            act = jnp.where(jnp.logical_and(bottom_outside, lanes >= span - width), 0.0, act)
        act_next[:, first * width : first * width + span] = act.astype(jnp.bfloat16)
    second_w = stack_taps(second_ref)
    for first, rows in row_chunks(band_rows):
        span = rows * width
        lanes = lax.broadcasted_iota(jnp.int32, (1, span), 1)
        conv = conv_chunk(act_next, second_w, first, rows, width, lanes % width)
        start = first * width
        hidden_ref[:, start : start + span] = lifted_keep[:, start : start + span].astype(jnp.float32) + conv
    tokens_per_row = width // 4
    pool_w = jnp.where(
        lax.broadcasted_iota(jnp.int32, (width, tokens_per_row), 0) // 4
        == lax.broadcasted_iota(jnp.int32, (width, tokens_per_row), 1),
        1.0 / 16.0,
        0.0,
    ).astype(jnp.float32)
    pooled = []
    for a in range(band_rows // 4):
        row_sum = hidden_ref[:, (4 * a) * width : (4 * a + 1) * width]
        for u in range(1, 4):
            row_sum = row_sum + hidden_ref[:, (4 * a + u) * width : (4 * a + u + 1) * width]
        pooled.append(
            jnp.dot(row_sum, pool_w, precision=lax.Precision.HIGHEST, preferred_element_type=jnp.float32)
        )
    pooled = jnp.concatenate(pooled, axis=1)
    tokens = normalize_features(pooled).astype(jnp.bfloat16)
    project_t = jnp.concatenate(
        [transposed(project_ref[:, g * feat : (g + 1) * feat]) for g in range(3)], axis=0
    ).astype(jnp.bfloat16)
    projected = jnp.dot(project_t, tokens, preferred_element_type=jnp.float32)
    query_ref[...] = feature_map(projected[:feat])
    key_feats = feature_map(projected[feat : 2 * feat]).astype(jnp.bfloat16)
    value_rows = projected[2 * feat :].astype(jnp.bfloat16)
    ones = jnp.ones((HEAD_DIM, key_feats.shape[1]), jnp.bfloat16)
    contract_tokens = (((1,), (1,)), ((), ()))
    for h in range(feat // HEAD_DIM):
        keys_h = key_feats[h * HEAD_DIM : (h + 1) * HEAD_DIM]
        values_h = value_rows[h * HEAD_DIM : (h + 1) * HEAD_DIM]
        summary_t = lax.dot_general(values_h, keys_h, contract_tokens, preferred_element_type=jnp.float32)
        totals = lax.dot_general(ones, keys_h, contract_tokens, preferred_element_type=jnp.float32)
        stats_ref[h * HEAD_DIM : (h + 1) * HEAD_DIM, :] = jnp.concatenate([summary_t, totals], axis=1)


def head_kernel(
    levels_ref, hidden_ref, query_ref, stats_own_ref, stats_other_ref, mix_ref, out_w_ref,
    previous_ref, start_ref, denoised_ref, seed_ref, *, width, band_rows, level_count,
):
    first_step = lax.axis_index("step") == 0
    sigma_low, sigma_high, spread = step_scalars(levels_ref, level_count, (1, width))
    scale_skip = 0.25 / spread
    scale_out = 0.5 * sigma_low * lax.rsqrt(spread)
    sigma_gap = sigma_high - sigma_low
    feat = query_ref.shape[0]
    contexts = []
    for h in range(feat // HEAD_DIM):
        rows = slice(h * HEAD_DIM, (h + 1) * HEAD_DIM)
        queries_h = query_ref[rows, :]
        stats_h = stats_own_ref[rows, :] + stats_other_ref[rows, :]
        numerator = jnp.dot(
            stats_h[:, 0:HEAD_DIM], queries_h,
            precision=lax.Precision.HIGHEST, preferred_element_type=jnp.float32,
        )
        denominator = jnp.dot(
            stats_h[:, HEAD_DIM : 2 * HEAD_DIM], queries_h,
            precision=lax.Precision.HIGHEST, preferred_element_type=jnp.float32,
        )
        contexts.append(numerator / denominator)
    context = jnp.concatenate(contexts, axis=0).astype(jnp.bfloat16)
    mix_t = transposed(mix_ref[...]).astype(jnp.bfloat16)
    mixed = jnp.dot(mix_t, context, preferred_element_type=jnp.float32)
    tokens_per_row = width // 4
    expand = jnp.where(
        lax.broadcasted_iota(jnp.int32, (tokens_per_row, width), 0)
        == lax.broadcasted_iota(jnp.int32, (tokens_per_row, width), 1) // 4,
        1.0,
        0.0,
    ).astype(jnp.float32)
    out_w = out_w_ref[...]
    for a in range(band_rows // 4):
        spread_mixed = jnp.dot(
            mixed[:, a * tokens_per_row : (a + 1) * tokens_per_row],
            expand,
            precision=lax.Precision.HIGHEST,
            preferred_element_type=jnp.float32,
        )
        for u in range(4):
            r = 4 * a + u
            start = r * width
            combined = hidden_ref[:, start : start + width] + spread_mixed
            act = silu(normalize_features(combined)).astype(jnp.bfloat16)
            field = jnp.dot(out_w, act, preferred_element_type=jnp.float32)
            state = jnp.where(first_step, start_ref[:, r, :], previous_ref[0, :, r, :])
            denoised = scale_skip * state + scale_out * field
            denoised_ref[:, r, :] = denoised
            drift = sigma_gap * (state - denoised) / sigma_low
            seed_ref[:, r, :] = drift + jnp.where(first_step, state, 0.0)


def vmem():
    return pl.BlockSpec(memory_space=pltpu.VMEM)


def smem():
    return pl.BlockSpec(memory_space=pltpu.SMEM)


def edge_rows(x, axis, dim, width):
    length = x.shape[dim]
    last = lax.slice_in_dim(x, length - width, length, axis=dim)
    leading = lax.slice_in_dim(x, 0, width, axis=dim)
    return jnp.where(lax.axis_index(axis) == 0, last, leading)


def local(
    iterates,
    window_start,
    coarse,
    step_levels,
    level_embed,
    lift_weight,
    conv_first,
    conv_second,
    project_weight,
    mix_weight,
    output_weight,
):
    level_count = 2 * lax.axis_size("step") + 1
    bands = lax.axis_size("rows")
    steps = lax.axis_size("step")
    assert bands == 2
    swap = [(0, 1), (1, 0)]
    previous = from_behind(iterates, "step", 1)
    previous_other = lax.ppermute(previous, "rows", swap)
    start_other = lax.ppermute(window_start, "rows", swap)
    coarse_other = lax.ppermute(coarse, "rows", swap)

    channels, band_rows, width = window_start.shape
    feat = lift_weight.shape[1]
    pixels = band_rows * width
    tokens = (band_rows // 4) * (width // 4)
    trunk = pl.pallas_call(
        lambda *refs: trunk_kernel(
            *refs, width=width, band_rows=band_rows, bands=bands, level_count=level_count
        ),
        out_shape=(
            jax.ShapeDtypeStruct((feat, pixels), jnp.float32),
            jax.ShapeDtypeStruct((feat, tokens), jnp.float32),
            jax.ShapeDtypeStruct((feat, 2 * HEAD_DIM), jnp.float32),
        ),
        in_specs=[smem()] + [vmem()] * 11,
        out_specs=(vmem(), vmem(), vmem()),
        scratch_shapes=[
            pltpu.VMEM((channels + coarse.shape[0], (band_rows + 2 * HALO) * width), jnp.float32),
            pltpu.VMEM((feat, (band_rows + 2 * HALO) * width), jnp.bfloat16),
            pltpu.VMEM((feat, pixels), jnp.bfloat16),
            pltpu.VMEM((feat, (band_rows + 2) * width), jnp.bfloat16),
        ],
    )
    hidden, queries, stats_own = trunk(
        step_levels,
        previous,
        window_start,
        start_other,
        previous_other,
        coarse,
        coarse_other,
        lift_weight,
        level_embed,
        conv_first,
        conv_second,
        project_weight,
    )
    stats_other = lax.ppermute(stats_own, "rows", swap)

    head = pl.pallas_call(
        lambda *refs: head_kernel(*refs, width=width, band_rows=band_rows, level_count=level_count),
        out_shape=(
            jax.ShapeDtypeStruct(window_start.shape, jnp.float32),
            jax.ShapeDtypeStruct(window_start.shape, jnp.float32),
        ),
        in_specs=[smem()] + [vmem()] * 8,
        out_specs=(vmem(), vmem()),
    )
    denoised, seed = head(
        step_levels, hidden, queries, stats_own, stats_other, mix_weight, output_weight.T,
        previous, window_start,
    )
    trajectory = prefix_sum(seed, "step")
    return (trajectory[None], denoised[None])


def solution(mesh):
    return jax.shard_map(
        local,
        mesh=mesh,
        in_specs=(
            P("step", "ens", "rows", None),
            P("ens", "rows", None),
            P("ens", "rows", None),
            P("step", None),
            P(),
            P(),
            P(),
            P(),
            P(),
            P(),
            P(),
        ),
        out_specs=(P("step", "ens", "rows", None), P("step", "ens", "rows", None)),
        check_vma=False,
    )
```

```python
import jax
import numpy as np
import jax.numpy as jnp
from jax import lax
from jax.experimental import pallas as pl
from jax.experimental.pallas import tpu as pltpu
from jax.sharding import PartitionSpec as P

HEAD_DIM = 64
HALO = 2
CHUNK_ROWS = 2
CONV_ROWS = 4

SIGMA_TOP = 8.0
SIGMA_END = 0.002
LOG_RATIO = float(np.log(np.float32(SIGMA_END / SIGMA_TOP)))


def from_behind(x, axis, by):
    devices = lax.axis_size(axis)
    pairs = [(i, i + by) for i in range(devices) if 0 <= i + by < devices]
    return lax.ppermute(x, axis, pairs)


def with_halo(x, axis, dim, width):
    devices, length = (lax.axis_size(axis), x.shape[dim])
    last = lax.slice_in_dim(x, length - width, length, axis=dim)
    leading = lax.slice_in_dim(x, 0, width, axis=dim)
    if devices == 2:
        me = lax.axis_index(axis)
        outgoing = jnp.where(me == 0, last, leading)
        incoming = lax.ppermute(outgoing, axis, [(0, 1), (1, 0)])
        zero = jnp.zeros_like(incoming)
        before = jnp.where(me == 0, zero, incoming)
        after = jnp.where(me == 0, incoming, zero)
    else:
        up = [(i, i + 1) for i in range(devices - 1)]
        down = [(j, i) for i, j in up]
        before = lax.ppermute(last, axis, up)
        after = lax.ppermute(leading, axis, down)
    return jnp.concatenate([before, x, after], axis=dim)


def band_sum(x, axis):
    devices = lax.axis_size(axis)
    if devices == 2:
        return x + lax.ppermute(x, axis, [(0, 1), (1, 0)])
    return lax.psum(x, axis)


def prefix_sum(x, axis):
    devices = lax.axis_size(axis)
    shift = 1
    while shift < devices:
        pairs = [(i, i + shift) for i in range(devices - shift)]
        x = x + lax.ppermute(x, axis, pairs)
        shift *= 2
    return x


def noise_level(levels, level_count):
    fraction = levels.astype(jnp.float32) / jnp.float32(level_count - 1)
    return SIGMA_TOP * jnp.exp(fraction * jnp.log(jnp.float32(SIGMA_END / SIGMA_TOP)))


def normalize_features(values):
    mean_square = jnp.sum(values * values, axis=0, keepdims=True) * (1.0 / values.shape[0])
    return values * lax.rsqrt(mean_square + 1e-06)


def silu(values):
    return values / (1.0 + jnp.exp(-values))


def feature_map(values):
    return jnp.where(values > 0, values + 1.0, jnp.exp(jnp.minimum(values, 0.0)))


def conv_chunk(source, weight, first_row, rows, width, column):
    span = rows * width
    stacked = jnp.concatenate(
        [source[:, (first_row + i) * width : (first_row + i) * width + span] for i in range(3)],
        axis=0,
    )
    taps = jnp.dot(weight, stacked, preferred_element_type=jnp.float32)
    feat = taps.shape[0] // 3
    left = pltpu.roll(taps[0:feat], 1, 1)
    right = pltpu.roll(taps[2 * feat : 3 * feat], span - 1, 1)
    result = taps[feat : 2 * feat]
    result = result + jnp.where(column != 0, left, 0.0)
    result = result + jnp.where(column != width - 1, right, 0.0)
    return result


def row_chunks(rows):
    chunks, first = [], 0
    while first < rows:
        size = min(CONV_ROWS, rows - first)
        chunks.append((first, size))
        first += size
    return chunks


def transposed(block):
    return block.astype(jnp.float32).T


def stack_taps(weight_ref):
    return jnp.concatenate(
        [
            jnp.concatenate([transposed(weight_ref[i, j]) for i in range(3)], axis=1)
            for j in range(3)
        ],
        axis=0,
    ).astype(jnp.bfloat16)


def step_scalars(levels_ref, level_count, shape):
    def sigma(k):
        level = jnp.full(shape, levels_ref[0, k].astype(jnp.float32))
        fraction = level / jnp.float32(level_count - 1)
        return SIGMA_TOP * jnp.exp(fraction * LOG_RATIO)

    sigma_low = sigma(0)
    sigma_high = sigma(1)
    spread = sigma_low * sigma_low + 0.25
    return sigma_low, sigma_high, spread


def trunk_kernel(
    levels_ref, previous_ref, start_ref, start_other_ref, previous_other_ref, coarse_ref,
    coarse_other_ref, lift_ref, embed_ref, first_ref, second_ref, project_ref,
    hidden_ref, query_ref, stats_ref, inputs, act_first, lifted_keep, act_next, hidden_local,
    hidden_sems, *, width, band_rows, bands, level_count,
):
    band = lax.axis_index("rows")
    first_step = lax.axis_index("step") == 0
    top_outside = band == 0
    bottom_outside = band == bands - 1
    channels = start_ref.shape[0]
    sigma_low, _, spread = step_scalars(levels_ref, level_count, (1, width))
    scale_in = lax.rsqrt(spread)
    for u in range(band_rows + 2 * HALO):
        v = u - HALO
        if 0 <= v < band_rows:
            state = jnp.where(first_step, start_ref[:, v, :], previous_ref[0, :, v, :])
            cond = coarse_ref[:, v, :]
        elif v < 0:
            state = jnp.where(first_step, start_other_ref[:, band_rows + v, :], previous_other_ref[0, :, band_rows + v, :])
            cond = coarse_other_ref[:, band_rows + v, :]
        else:
            state = jnp.where(first_step, start_other_ref[:, v - band_rows, :], previous_other_ref[0, :, v - band_rows, :])
            cond = coarse_other_ref[:, v - band_rows, :]
        scaled = (scale_in * state).astype(jnp.bfloat16).astype(jnp.float32)
        inputs[0:channels, u * width : (u + 1) * width] = scaled
        inputs[channels:, u * width : (u + 1) * width] = cond.astype(jnp.float32)
    level = levels_ref[0, 0]
    table = embed_ref[...].astype(jnp.float32)
    picked = jnp.where(lax.broadcasted_iota(jnp.int32, table.shape, 0) == level, table, 0.0)
    embed_row = jnp.sum(picked, axis=0, keepdims=True)
    feat = table.shape[1]
    embed = jnp.broadcast_to(embed_row, (feat, feat)).T[:, 0:1]
    lift_w = transposed(lift_ref[...]).astype(jnp.bfloat16)

    span = CHUNK_ROWS * width
    in_rows = band_rows + 2 * HALO
    for q in range(in_rows // CHUNK_ROWS):
        start = q * span
        chunk = inputs[:, start : start + span].astype(jnp.bfloat16)
        lifted = jnp.dot(lift_w, chunk, preferred_element_type=jnp.float32)
        lifted = (lifted + embed).astype(jnp.bfloat16)
        row0 = q * CHUNK_ROWS
        if HALO <= row0 < HALO + band_rows:
            keep = (row0 - HALO) * width
            lifted_keep[:, keep : keep + span] = lifted
        act = silu(normalize_features(lifted.astype(jnp.float32)))
        if row0 < HALO:
            act = jnp.where(top_outside, 0.0, act)
        if row0 >= HALO + band_rows:
            act = jnp.where(bottom_outside, 0.0, act)
        act_first[:, start : start + span] = act.astype(jnp.bfloat16)
    first_w = stack_taps(first_ref)
    mid_rows = band_rows + 2
    chunks = row_chunks(mid_rows)
    for q, (first, rows) in enumerate(chunks):
        span = rows * width
        lanes = lax.broadcasted_iota(jnp.int32, (1, span), 1)
        middle = conv_chunk(act_first, first_w, first, rows, width, lanes % width)
        act = silu(normalize_features(middle))
        if q == 0:
            act = jnp.where(jnp.logical_and(top_outside, lanes < width), 0.0, act)
        if q == len(chunks) - 1:
            act = jnp.where(jnp.logical_and(bottom_outside, lanes >= span - width), 0.0, act)
        act_next[:, first * width : first * width + span] = act.astype(jnp.bfloat16)
    second_w = stack_taps(second_ref)
    outgoing = []
    for q, (first, rows) in enumerate(row_chunks(band_rows)):
        span = rows * width
        lanes = lax.broadcasted_iota(jnp.int32, (1, span), 1)
        conv = conv_chunk(act_next, second_w, first, rows, width, lanes % width)
        start = first * width
        hidden_local[:, start : start + span] = lifted_keep[:, start : start + span].astype(jnp.float32) + conv
        copy = pltpu.make_async_copy(
            hidden_local.at[:, pl.ds(start, span)], hidden_ref.at[:, pl.ds(start, span)], hidden_sems.at[q]
        )
        copy.start()
        outgoing.append(copy)
    tokens_per_row = width // 4
    pool_w = jnp.where(
        lax.broadcasted_iota(jnp.int32, (width, tokens_per_row), 0) // 4
        == lax.broadcasted_iota(jnp.int32, (width, tokens_per_row), 1),
        1.0 / 16.0,
        0.0,
    ).astype(jnp.float32)
    pooled = []
    for a in range(band_rows // 4):
        row_sum = hidden_local[:, (4 * a) * width : (4 * a + 1) * width]
        for u in range(1, 4):
            row_sum = row_sum + hidden_local[:, (4 * a + u) * width : (4 * a + u + 1) * width]
        pooled.append(
            jnp.dot(row_sum, pool_w, precision=lax.Precision.HIGHEST, preferred_element_type=jnp.float32)
        )
    pooled = jnp.concatenate(pooled, axis=1)
    tokens = normalize_features(pooled).astype(jnp.bfloat16)
    project_t = jnp.concatenate(
        [transposed(project_ref[:, g * feat : (g + 1) * feat]) for g in range(3)], axis=0
    ).astype(jnp.bfloat16)
    projected = jnp.dot(project_t, tokens, preferred_element_type=jnp.float32)
    query_ref[...] = feature_map(projected[:feat])
    key_feats = feature_map(projected[feat : 2 * feat]).astype(jnp.bfloat16)
    value_rows = projected[2 * feat :].astype(jnp.bfloat16)
    ones = jnp.ones((HEAD_DIM, key_feats.shape[1]), jnp.bfloat16)
    contract_tokens = (((1,), (1,)), ((), ()))
    for h in range(feat // HEAD_DIM):
        keys_h = key_feats[h * HEAD_DIM : (h + 1) * HEAD_DIM]
        values_h = value_rows[h * HEAD_DIM : (h + 1) * HEAD_DIM]
        summary_t = lax.dot_general(values_h, keys_h, contract_tokens, preferred_element_type=jnp.float32)
        totals = lax.dot_general(ones, keys_h, contract_tokens, preferred_element_type=jnp.float32)
        stats_ref[h * HEAD_DIM : (h + 1) * HEAD_DIM, :] = jnp.concatenate([summary_t, totals], axis=1)
    for copy in outgoing:
        copy.wait()


def head_kernel(
    levels_ref, hidden_ref, query_ref, stats_own_ref, stats_other_ref, mix_ref, out_w_ref,
    previous_ref, start_ref, denoised_ref, seed_ref, hidden_local, hidden_sems,
    *, width, band_rows, level_count,
):
    group = 4 * width
    incoming = []
    for a in range(band_rows // 4):
        copy = pltpu.make_async_copy(
            hidden_ref.at[:, pl.ds(a * group, group)], hidden_local.at[:, pl.ds(a * group, group)], hidden_sems.at[a]
        )
        copy.start()
        incoming.append(copy)
    first_step = lax.axis_index("step") == 0
    sigma_low, sigma_high, spread = step_scalars(levels_ref, level_count, (1, width))
    scale_skip = 0.25 / spread
    scale_out = 0.5 * sigma_low * lax.rsqrt(spread)
    sigma_gap = sigma_high - sigma_low
    feat = query_ref.shape[0]
    contexts = []
    for h in range(feat // HEAD_DIM):
        rows = slice(h * HEAD_DIM, (h + 1) * HEAD_DIM)
        queries_h = query_ref[rows, :]
        stats_h = stats_own_ref[rows, :] + stats_other_ref[rows, :]
        numerator = jnp.dot(
            stats_h[:, 0:HEAD_DIM], queries_h,
            precision=lax.Precision.HIGHEST, preferred_element_type=jnp.float32,
        )
        denominator = jnp.dot(
            stats_h[:, HEAD_DIM : 2 * HEAD_DIM], queries_h,
            precision=lax.Precision.HIGHEST, preferred_element_type=jnp.float32,
        )
        contexts.append(numerator / denominator)
    context = jnp.concatenate(contexts, axis=0).astype(jnp.bfloat16)
    mix_t = transposed(mix_ref[...]).astype(jnp.bfloat16)
    mixed = jnp.dot(mix_t, context, preferred_element_type=jnp.float32)
    tokens_per_row = width // 4
    expand = jnp.where(
        lax.broadcasted_iota(jnp.int32, (tokens_per_row, width), 0)
        == lax.broadcasted_iota(jnp.int32, (tokens_per_row, width), 1) // 4,
        1.0,
        0.0,
    ).astype(jnp.float32)
    out_w = out_w_ref[...]
    for a in range(band_rows // 4):
        incoming[a].wait()
        spread_mixed = jnp.dot(
            mixed[:, a * tokens_per_row : (a + 1) * tokens_per_row],
            expand,
            precision=lax.Precision.HIGHEST,
            preferred_element_type=jnp.float32,
        )
        for u in range(4):
            r = 4 * a + u
            start = r * width
            combined = hidden_local[:, start : start + width] + spread_mixed
            act = silu(normalize_features(combined)).astype(jnp.bfloat16)
            field = jnp.dot(out_w, act, preferred_element_type=jnp.float32)
            state = jnp.where(first_step, start_ref[:, r, :], previous_ref[0, :, r, :])
            denoised = scale_skip * state + scale_out * field
            denoised_ref[:, r, :] = denoised
            drift = sigma_gap * (state - denoised) / sigma_low
            seed_ref[:, r, :] = drift + jnp.where(first_step, state, 0.0)


def vmem():
    return pl.BlockSpec(memory_space=pltpu.VMEM)


def smem():
    return pl.BlockSpec(memory_space=pltpu.SMEM)


def edge_rows(x, axis, dim, width):
    length = x.shape[dim]
    last = lax.slice_in_dim(x, length - width, length, axis=dim)
    leading = lax.slice_in_dim(x, 0, width, axis=dim)
    return jnp.where(lax.axis_index(axis) == 0, last, leading)


def local(
    iterates,
    window_start,
    coarse,
    step_levels,
    level_embed,
    lift_weight,
    conv_first,
    conv_second,
    project_weight,
    mix_weight,
    output_weight,
):
    level_count = 2 * lax.axis_size("step") + 1
    bands = lax.axis_size("rows")
    steps = lax.axis_size("step")
    assert bands == 2
    swap = [(0, 1), (1, 0)]
    previous = from_behind(iterates, "step", 1)
    previous_other = lax.ppermute(previous, "rows", swap)
    start_other = lax.ppermute(window_start, "rows", swap)
    coarse_other = lax.ppermute(coarse, "rows", swap)

    channels, band_rows, width = window_start.shape
    feat = lift_weight.shape[1]
    pixels = band_rows * width
    tokens = (band_rows // 4) * (width // 4)
    trunk = pl.pallas_call(
        lambda *refs: trunk_kernel(
            *refs, width=width, band_rows=band_rows, bands=bands, level_count=level_count
        ),
        out_shape=(
            jax.ShapeDtypeStruct((feat, pixels), jnp.float32),
            jax.ShapeDtypeStruct((feat, tokens), jnp.float32),
            jax.ShapeDtypeStruct((feat, 2 * HEAD_DIM), jnp.float32),
        ),
        in_specs=[smem()] + [vmem()] * 11,
        out_specs=(pl.BlockSpec(memory_space=pl.ANY), vmem(), vmem()),
        scratch_shapes=[
            pltpu.VMEM((channels + coarse.shape[0], (band_rows + 2 * HALO) * width), jnp.float32),
            pltpu.VMEM((feat, (band_rows + 2 * HALO) * width), jnp.bfloat16),
            pltpu.VMEM((feat, pixels), jnp.bfloat16),
            pltpu.VMEM((feat, (band_rows + 2) * width), jnp.bfloat16),
            pltpu.VMEM((feat, pixels), jnp.float32),
            pltpu.SemaphoreType.DMA((len(row_chunks(band_rows)),)),
        ],
    )
    hidden, queries, stats_own = trunk(
        step_levels,
        previous,
        window_start,
        start_other,
        previous_other,
        coarse,
        coarse_other,
        lift_weight,
        level_embed,
        conv_first,
        conv_second,
        project_weight,
    )
    stats_other = lax.ppermute(stats_own, "rows", swap)

    head = pl.pallas_call(
        lambda *refs: head_kernel(*refs, width=width, band_rows=band_rows, level_count=level_count),
        out_shape=(
            jax.ShapeDtypeStruct(window_start.shape, jnp.float32),
            jax.ShapeDtypeStruct(window_start.shape, jnp.float32),
        ),
        in_specs=[smem(), pl.BlockSpec(memory_space=pl.ANY)] + [vmem()] * 7,
        out_specs=(vmem(), vmem()),
        scratch_shapes=[
            pltpu.VMEM((feat, pixels), jnp.float32),
            pltpu.SemaphoreType.DMA((band_rows // 4,)),
        ],
    )
    denoised, seed = head(
        step_levels, hidden, queries, stats_own, stats_other, mix_weight, output_weight.T,
        previous, window_start,
    )
    trajectory = prefix_sum(seed, "step")
    return (trajectory[None], denoised[None])


def solution(mesh):
    return jax.shard_map(
        local,
        mesh=mesh,
        in_specs=(
            P("step", "ens", "rows", None),
            P("ens", "rows", None),
            P("ens", "rows", None),
            P("step", None),
            P(),
            P(),
            P(),
            P(),
            P(),
            P(),
            P(),
        ),
        out_specs=(P("step", "ens", "rows", None), P("step", "ens", "rows", None)),
        check_vma=False,
    )
```

```python
import jax
import numpy as np
import jax.numpy as jnp
from jax import lax
from jax.experimental import pallas as pl
from jax.experimental.pallas import tpu as pltpu
from jax.sharding import PartitionSpec as P

HEAD_DIM = 64
HALO = 2
CHUNK_ROWS = 2
CONV_ROWS = 4

SIGMA_TOP = 8.0
SIGMA_END = 0.002
LOG_RATIO = float(np.log(np.float32(SIGMA_END / SIGMA_TOP)))


def from_behind(x, axis, by):
    devices = lax.axis_size(axis)
    pairs = [(i, i + by) for i in range(devices) if 0 <= i + by < devices]
    return lax.ppermute(x, axis, pairs)


def with_halo(x, axis, dim, width):
    devices, length = (lax.axis_size(axis), x.shape[dim])
    last = lax.slice_in_dim(x, length - width, length, axis=dim)
    leading = lax.slice_in_dim(x, 0, width, axis=dim)
    if devices == 2:
        me = lax.axis_index(axis)
        outgoing = jnp.where(me == 0, last, leading)
        incoming = lax.ppermute(outgoing, axis, [(0, 1), (1, 0)])
        zero = jnp.zeros_like(incoming)
        before = jnp.where(me == 0, zero, incoming)
        after = jnp.where(me == 0, incoming, zero)
    else:
        up = [(i, i + 1) for i in range(devices - 1)]
        down = [(j, i) for i, j in up]
        before = lax.ppermute(last, axis, up)
        after = lax.ppermute(leading, axis, down)
    return jnp.concatenate([before, x, after], axis=dim)


def band_sum(x, axis):
    devices = lax.axis_size(axis)
    if devices == 2:
        return x + lax.ppermute(x, axis, [(0, 1), (1, 0)])
    return lax.psum(x, axis)


def prefix_sum(x, axis):
    devices = lax.axis_size(axis)
    shift = 1
    while shift < devices:
        pairs = [(i, i + shift) for i in range(devices - shift)]
        x = x + lax.ppermute(x, axis, pairs)
        shift *= 2
    return x


def noise_level(levels, level_count):
    fraction = levels.astype(jnp.float32) / jnp.float32(level_count - 1)
    return SIGMA_TOP * jnp.exp(fraction * jnp.log(jnp.float32(SIGMA_END / SIGMA_TOP)))


def normalize_features(values):
    mean_square = jnp.sum(values * values, axis=0, keepdims=True) * (1.0 / values.shape[0])
    return values * lax.rsqrt(mean_square + 1e-06)


def silu(values):
    return values / (1.0 + jnp.exp(-values))


def feature_map(values):
    return jnp.where(values > 0, values + 1.0, jnp.exp(jnp.minimum(values, 0.0)))


def conv_chunk(source, weight, first_row, rows, width, column):
    span = rows * width
    stacked = jnp.concatenate(
        [source[:, (first_row + i) * width : (first_row + i) * width + span] for i in range(3)],
        axis=0,
    )
    taps = jnp.dot(weight, stacked, preferred_element_type=jnp.float32)
    feat = taps.shape[0] // 3
    left = pltpu.roll(taps[0:feat], 1, 1)
    right = pltpu.roll(taps[2 * feat : 3 * feat], span - 1, 1)
    result = taps[feat : 2 * feat]
    result = result + jnp.where(column != 0, left, 0.0)
    result = result + jnp.where(column != width - 1, right, 0.0)
    return result


def row_chunks(rows):
    chunks, first = [], 0
    while first < rows:
        size = min(CONV_ROWS, rows - first)
        chunks.append((first, size))
        first += size
    return chunks


def exact_weight_dot(values, weight):
    high = values.astype(jnp.bfloat16)
    low = (values - high.astype(jnp.float32)).astype(jnp.bfloat16)
    return jnp.dot(high, weight, preferred_element_type=jnp.float32) + jnp.dot(
        low, weight, preferred_element_type=jnp.float32
    )


def transposed(block):
    return block.astype(jnp.float32).T


def stack_taps(weight_ref):
    return jnp.concatenate(
        [
            jnp.concatenate([transposed(weight_ref[i, j]) for i in range(3)], axis=1)
            for j in range(3)
        ],
        axis=0,
    ).astype(jnp.bfloat16)


def step_scalars(levels_ref, level_count, shape):
    def sigma(k):
        level = jnp.full(shape, levels_ref[0, k].astype(jnp.float32))
        fraction = level / jnp.float32(level_count - 1)
        return SIGMA_TOP * jnp.exp(fraction * LOG_RATIO)

    sigma_low = sigma(0)
    sigma_high = sigma(1)
    spread = sigma_low * sigma_low + 0.25
    return sigma_low, sigma_high, spread


def trunk_kernel(
    levels_ref, previous_ref, start_ref, start_other_ref, previous_other_ref, coarse_ref,
    coarse_other_ref, lift_ref, embed_ref, first_ref, second_ref, project_ref,
    hidden_ref, query_ref, stats_ref, inputs, act_first, lifted_keep, act_next, hidden_local,
    hidden_sems, *, width, band_rows, bands, level_count,
):
    band = lax.axis_index("rows")
    first_step = lax.axis_index("step") == 0
    top_outside = band == 0
    bottom_outside = band == bands - 1
    channels = start_ref.shape[0]
    sigma_low, _, spread = step_scalars(levels_ref, level_count, (1, width))
    scale_in = lax.rsqrt(spread)
    for u in range(band_rows + 2 * HALO):
        v = u - HALO
        if 0 <= v < band_rows:
            state = jnp.where(first_step, start_ref[:, v, :], previous_ref[0, :, v, :])
            cond = coarse_ref[:, v, :]
        elif v < 0:
            state = jnp.where(first_step, start_other_ref[:, band_rows + v, :], previous_other_ref[0, :, band_rows + v, :])
            cond = coarse_other_ref[:, band_rows + v, :]
        else:
            state = jnp.where(first_step, start_other_ref[:, v - band_rows, :], previous_other_ref[0, :, v - band_rows, :])
            cond = coarse_other_ref[:, v - band_rows, :]
        scaled = (scale_in * state).astype(jnp.bfloat16).astype(jnp.float32)
        inputs[0:channels, u * width : (u + 1) * width] = scaled
        inputs[channels:, u * width : (u + 1) * width] = cond.astype(jnp.float32)
    level = levels_ref[0, 0]
    table = embed_ref[...].astype(jnp.float32)
    picked = jnp.where(lax.broadcasted_iota(jnp.int32, table.shape, 0) == level, table, 0.0)
    embed_row = jnp.sum(picked, axis=0, keepdims=True)
    feat = table.shape[1]
    embed = jnp.broadcast_to(embed_row, (feat, feat)).T[:, 0:1]
    lift_w = transposed(lift_ref[...]).astype(jnp.bfloat16)

    span = CHUNK_ROWS * width
    in_rows = band_rows + 2 * HALO
    for q in range(in_rows // CHUNK_ROWS):
        start = q * span
        chunk = inputs[:, start : start + span].astype(jnp.bfloat16)
        lifted = jnp.dot(lift_w, chunk, preferred_element_type=jnp.float32)
        lifted = (lifted + embed).astype(jnp.bfloat16)
        row0 = q * CHUNK_ROWS
        if HALO <= row0 < HALO + band_rows:
            keep = (row0 - HALO) * width
            lifted_keep[:, keep : keep + span] = lifted
        act = silu(normalize_features(lifted.astype(jnp.float32)))
        if row0 < HALO:
            act = jnp.where(top_outside, 0.0, act)
        if row0 >= HALO + band_rows:
            act = jnp.where(bottom_outside, 0.0, act)
        act_first[:, start : start + span] = act.astype(jnp.bfloat16)
    first_w = stack_taps(first_ref)
    mid_rows = band_rows + 2
    chunks = row_chunks(mid_rows)
    for q, (first, rows) in enumerate(chunks):
        span = rows * width
        lanes = lax.broadcasted_iota(jnp.int32, (1, span), 1)
        middle = conv_chunk(act_first, first_w, first, rows, width, lanes % width)
        act = silu(normalize_features(middle))
        if q == 0:
            act = jnp.where(jnp.logical_and(top_outside, lanes < width), 0.0, act)
        if q == len(chunks) - 1:
            act = jnp.where(jnp.logical_and(bottom_outside, lanes >= span - width), 0.0, act)
        act_next[:, first * width : first * width + span] = act.astype(jnp.bfloat16)
    second_w = stack_taps(second_ref)
    outgoing = []
    for q, (first, rows) in enumerate(row_chunks(band_rows)):
        span = rows * width
        lanes = lax.broadcasted_iota(jnp.int32, (1, span), 1)
        conv = conv_chunk(act_next, second_w, first, rows, width, lanes % width)
        start = first * width
        hidden_local[:, start : start + span] = lifted_keep[:, start : start + span].astype(jnp.float32) + conv
        copy = pltpu.make_async_copy(
            hidden_local.at[:, pl.ds(start, span)], hidden_ref.at[:, pl.ds(start, span)], hidden_sems.at[q]
        )
        copy.start()
        outgoing.append(copy)
    tokens_per_row = width // 4
    pool_w = jnp.where(
        lax.broadcasted_iota(jnp.int32, (width, tokens_per_row), 0) // 4
        == lax.broadcasted_iota(jnp.int32, (width, tokens_per_row), 1),
        1.0 / 16.0,
        0.0,
    ).astype(jnp.bfloat16)
    pooled = []
    for a in range(band_rows // 4):
        row_sum = hidden_local[:, (4 * a) * width : (4 * a + 1) * width]
        for u in range(1, 4):
            row_sum = row_sum + hidden_local[:, (4 * a + u) * width : (4 * a + u + 1) * width]
        pooled.append(exact_weight_dot(row_sum, pool_w))
    pooled = jnp.concatenate(pooled, axis=1)
    tokens = normalize_features(pooled).astype(jnp.bfloat16)
    project_t = jnp.concatenate(
        [transposed(project_ref[:, g * feat : (g + 1) * feat]) for g in range(3)], axis=0
    ).astype(jnp.bfloat16)
    projected = jnp.dot(project_t, tokens, preferred_element_type=jnp.float32)
    query_ref[...] = feature_map(projected[:feat])
    key_feats = feature_map(projected[feat : 2 * feat]).astype(jnp.bfloat16)
    value_rows = projected[2 * feat :].astype(jnp.bfloat16)
    ones = jnp.ones((HEAD_DIM, key_feats.shape[1]), jnp.bfloat16)
    contract_tokens = (((1,), (1,)), ((), ()))
    for h in range(feat // HEAD_DIM):
        keys_h = key_feats[h * HEAD_DIM : (h + 1) * HEAD_DIM]
        values_h = value_rows[h * HEAD_DIM : (h + 1) * HEAD_DIM]
        summary_t = lax.dot_general(values_h, keys_h, contract_tokens, preferred_element_type=jnp.float32)
        totals = lax.dot_general(ones, keys_h, contract_tokens, preferred_element_type=jnp.float32)
        stats_ref[h * HEAD_DIM : (h + 1) * HEAD_DIM, :] = jnp.concatenate([summary_t, totals], axis=1)
    for copy in outgoing:
        copy.wait()


def head_kernel(
    levels_ref, hidden_ref, query_ref, stats_own_ref, stats_other_ref, mix_ref, out_w_ref,
    previous_ref, start_ref, denoised_ref, seed_ref, hidden_local, hidden_sems, stats_local,
    stats_sem, *, width, band_rows, level_count,
):
    stats_copy = pltpu.make_async_copy(stats_other_ref, stats_local, stats_sem.at[0])
    stats_copy.start()
    group = 4 * width
    incoming = []
    for a in range(band_rows // 4):
        copy = pltpu.make_async_copy(
            hidden_ref.at[:, pl.ds(a * group, group)], hidden_local.at[:, pl.ds(a * group, group)], hidden_sems.at[a]
        )
        copy.start()
        incoming.append(copy)
    first_step = lax.axis_index("step") == 0
    sigma_low, sigma_high, spread = step_scalars(levels_ref, level_count, (1, width))
    scale_skip = 0.25 / spread
    scale_out = 0.5 * sigma_low * lax.rsqrt(spread)
    sigma_gap = sigma_high - sigma_low
    feat = query_ref.shape[0]
    stats_copy.wait()
    contexts = []
    for h in range(feat // HEAD_DIM):
        rows = slice(h * HEAD_DIM, (h + 1) * HEAD_DIM)
        queries_h = query_ref[rows, :]
        stats_h = stats_own_ref[rows, :] + stats_local[rows, :]
        numerator = jnp.dot(
            stats_h[:, 0:HEAD_DIM], queries_h,
            precision=lax.Precision.HIGHEST, preferred_element_type=jnp.float32,
        )
        denominator = jnp.dot(
            stats_h[:, HEAD_DIM : 2 * HEAD_DIM], queries_h,
            precision=lax.Precision.HIGHEST, preferred_element_type=jnp.float32,
        )
        contexts.append(numerator / denominator)
    context = jnp.concatenate(contexts, axis=0).astype(jnp.bfloat16)
    mix_t = transposed(mix_ref[...]).astype(jnp.bfloat16)
    mixed = jnp.dot(mix_t, context, preferred_element_type=jnp.float32)
    tokens_per_row = width // 4
    expand = jnp.where(
        lax.broadcasted_iota(jnp.int32, (tokens_per_row, width), 0)
        == lax.broadcasted_iota(jnp.int32, (tokens_per_row, width), 1) // 4,
        1.0,
        0.0,
    ).astype(jnp.bfloat16)
    out_w = out_w_ref[...]
    for a in range(band_rows // 4):
        incoming[a].wait()
        spread_mixed = exact_weight_dot(mixed[:, a * tokens_per_row : (a + 1) * tokens_per_row], expand)
        for u in range(4):
            r = 4 * a + u
            start = r * width
            combined = hidden_local[:, start : start + width] + spread_mixed
            act = silu(normalize_features(combined)).astype(jnp.bfloat16)
            field = jnp.dot(out_w, act, preferred_element_type=jnp.float32)
            state = jnp.where(first_step, start_ref[:, r, :], previous_ref[0, :, r, :])
            denoised = scale_skip * state + scale_out * field
            denoised_ref[:, r, :] = denoised
            drift = sigma_gap * (state - denoised) / sigma_low
            seed_ref[:, r, :] = drift + jnp.where(first_step, state, 0.0)


def vmem():
    return pl.BlockSpec(memory_space=pltpu.VMEM)


def smem():
    return pl.BlockSpec(memory_space=pltpu.SMEM)


def edge_rows(x, axis, dim, width):
    length = x.shape[dim]
    last = lax.slice_in_dim(x, length - width, length, axis=dim)
    leading = lax.slice_in_dim(x, 0, width, axis=dim)
    return jnp.where(lax.axis_index(axis) == 0, last, leading)


def local(
    iterates,
    window_start,
    coarse,
    step_levels,
    level_embed,
    lift_weight,
    conv_first,
    conv_second,
    project_weight,
    mix_weight,
    output_weight,
):
    level_count = 2 * lax.axis_size("step") + 1
    bands = lax.axis_size("rows")
    steps = lax.axis_size("step")
    assert bands == 2
    swap = [(0, 1), (1, 0)]
    previous = from_behind(iterates, "step", 1)
    previous_other = lax.ppermute(previous, "rows", swap)
    start_other = lax.ppermute(window_start, "rows", swap)
    coarse_other = lax.ppermute(coarse, "rows", swap)

    channels, band_rows, width = window_start.shape
    feat = lift_weight.shape[1]
    pixels = band_rows * width
    tokens = (band_rows // 4) * (width // 4)
    trunk = pl.pallas_call(
        lambda *refs: trunk_kernel(
            *refs, width=width, band_rows=band_rows, bands=bands, level_count=level_count
        ),
        out_shape=(
            jax.ShapeDtypeStruct((feat, pixels), jnp.float32),
            jax.ShapeDtypeStruct((feat, tokens), jnp.float32),
            jax.ShapeDtypeStruct((feat, 2 * HEAD_DIM), jnp.float32),
        ),
        in_specs=[smem()] + [vmem()] * 11,
        out_specs=(pl.BlockSpec(memory_space=pl.ANY), vmem(), vmem()),
        scratch_shapes=[
            pltpu.VMEM((channels + coarse.shape[0], (band_rows + 2 * HALO) * width), jnp.float32),
            pltpu.VMEM((feat, (band_rows + 2 * HALO) * width), jnp.bfloat16),
            pltpu.VMEM((feat, pixels), jnp.bfloat16),
            pltpu.VMEM((feat, (band_rows + 2) * width), jnp.bfloat16),
            pltpu.VMEM((feat, pixels), jnp.float32),
            pltpu.SemaphoreType.DMA((len(row_chunks(band_rows)),)),
        ],
    )
    hidden, queries, stats_own = trunk(
        step_levels,
        previous,
        window_start,
        start_other,
        previous_other,
        coarse,
        coarse_other,
        lift_weight,
        level_embed,
        conv_first,
        conv_second,
        project_weight,
    )
    stats_other = lax.ppermute(stats_own, "rows", swap)

    head = pl.pallas_call(
        lambda *refs: head_kernel(*refs, width=width, band_rows=band_rows, level_count=level_count),
        out_shape=(
            jax.ShapeDtypeStruct(window_start.shape, jnp.float32),
            jax.ShapeDtypeStruct(window_start.shape, jnp.float32),
        ),
        in_specs=[smem(), pl.BlockSpec(memory_space=pl.ANY), vmem(), vmem(),
                  pl.BlockSpec(memory_space=pl.ANY)] + [vmem()] * 4,
        out_specs=(vmem(), vmem()),
        scratch_shapes=[
            pltpu.VMEM((feat, pixels), jnp.float32),
            pltpu.SemaphoreType.DMA((band_rows // 4,)),
            pltpu.VMEM((feat, 2 * HEAD_DIM), jnp.float32),
            pltpu.SemaphoreType.DMA((1,)),
        ],
    )
    denoised, seed = head(
        step_levels, hidden, queries, stats_own, stats_other, mix_weight, output_weight.T,
        previous, window_start,
    )
    trajectory = prefix_sum(seed, "step")
    return (trajectory[None], denoised[None])


def solution(mesh):
    return jax.shard_map(
        local,
        mesh=mesh,
        in_specs=(
            P("step", "ens", "rows", None),
            P("ens", "rows", None),
            P("ens", "rows", None),
            P("step", None),
            P(),
            P(),
            P(),
            P(),
            P(),
            P(),
            P(),
        ),
        out_specs=(P("step", "ens", "rows", None), P("step", "ens", "rows", None)),
        check_vma=False,
    )
```

```python
import jax
import numpy as np
import jax.numpy as jnp
from jax import lax
from jax.experimental import pallas as pl
from jax.experimental.pallas import tpu as pltpu
from jax.sharding import PartitionSpec as P

HEAD_DIM = 64
HALO = 2
CHUNK_ROWS = 2
CONV_ROWS = 4

SIGMA_TOP = 8.0
SIGMA_END = 0.002
LOG_RATIO = float(np.log(np.float32(SIGMA_END / SIGMA_TOP)))


def from_behind(x, axis, by):
    devices = lax.axis_size(axis)
    pairs = [(i, i + by) for i in range(devices) if 0 <= i + by < devices]
    return lax.ppermute(x, axis, pairs)


def with_halo(x, axis, dim, width):
    devices, length = (lax.axis_size(axis), x.shape[dim])
    last = lax.slice_in_dim(x, length - width, length, axis=dim)
    leading = lax.slice_in_dim(x, 0, width, axis=dim)
    if devices == 2:
        me = lax.axis_index(axis)
        outgoing = jnp.where(me == 0, last, leading)
        incoming = lax.ppermute(outgoing, axis, [(0, 1), (1, 0)])
        zero = jnp.zeros_like(incoming)
        before = jnp.where(me == 0, zero, incoming)
        after = jnp.where(me == 0, incoming, zero)
    else:
        up = [(i, i + 1) for i in range(devices - 1)]
        down = [(j, i) for i, j in up]
        before = lax.ppermute(last, axis, up)
        after = lax.ppermute(leading, axis, down)
    return jnp.concatenate([before, x, after], axis=dim)


def band_sum(x, axis):
    devices = lax.axis_size(axis)
    if devices == 2:
        return x + lax.ppermute(x, axis, [(0, 1), (1, 0)])
    return lax.psum(x, axis)


def prefix_sum(x, axis):
    devices = lax.axis_size(axis)
    shift = 1
    while shift < devices:
        pairs = [(i, i + shift) for i in range(devices - shift)]
        x = x + lax.ppermute(x, axis, pairs)
        shift *= 2
    return x


def noise_level(levels, level_count):
    fraction = levels.astype(jnp.float32) / jnp.float32(level_count - 1)
    return SIGMA_TOP * jnp.exp(fraction * jnp.log(jnp.float32(SIGMA_END / SIGMA_TOP)))


def normalize_features(values):
    mean_square = jnp.sum(values * values, axis=0, keepdims=True) * (1.0 / values.shape[0])
    return values * lax.rsqrt(mean_square + 1e-06)


def silu(values):
    return values / (1.0 + jnp.exp(-values))


def feature_map(values):
    return jnp.where(values > 0, values + 1.0, jnp.exp(jnp.minimum(values, 0.0)))


def conv_chunk(source, weight, first_row, rows, width, column):
    span = rows * width
    stacked = jnp.concatenate(
        [source[:, (first_row + i) * width : (first_row + i) * width + span] for i in range(3)],
        axis=0,
    )
    taps = jnp.dot(weight, stacked, preferred_element_type=jnp.float32)
    feat = taps.shape[0] // 3
    left = pltpu.roll(taps[0:feat], 1, 1)
    right = pltpu.roll(taps[2 * feat : 3 * feat], span - 1, 1)
    result = taps[feat : 2 * feat]
    result = result + jnp.where(column != 0, left, 0.0)
    result = result + jnp.where(column != width - 1, right, 0.0)
    return result


def row_chunks(rows):
    chunks, first = [], 0
    while first < rows:
        size = min(CONV_ROWS, rows - first)
        chunks.append((first, size))
        first += size
    return chunks


def transposed(block):
    return block.astype(jnp.float32).T


def stack_taps(weight_ref):
    return jnp.concatenate(
        [
            jnp.concatenate([transposed(weight_ref[i, j]) for i in range(3)], axis=1)
            for j in range(3)
        ],
        axis=0,
    ).astype(jnp.bfloat16)


def level_sigma(level, level_count, shape):
    fraction = jnp.full(shape, level.astype(jnp.float32)) / jnp.float32(level_count - 1)
    return SIGMA_TOP * jnp.exp(fraction * LOG_RATIO)


def start_level(levels_ref, first_step):
    return jnp.where(first_step, 0, levels_ref[0, 1])


def trunk_kernel(
    levels_ref, previous_ref, start_ref, start_other_ref, previous_other_ref, coarse_ref,
    coarse_other_ref, lift_ref, embed_ref, first_ref, second_ref, project_ref,
    hidden_ref, query_ref, stats_ref, inputs, act_first, lifted_keep, act_next, hidden_local,
    hidden_sems, *, width, band_rows, bands, level_count,
):
    band = lax.axis_index("rows")
    first_step = lax.axis_index("step") == lax.axis_size("step") - 1
    top_outside = band == 0
    bottom_outside = band == bands - 1
    channels = start_ref.shape[0]
    level = start_level(levels_ref, first_step)
    sigma_low = level_sigma(level, level_count, (1, width))
    spread = sigma_low * sigma_low + 0.25
    scale_in = lax.rsqrt(spread)
    for u in range(band_rows + 2 * HALO):
        v = u - HALO
        if 0 <= v < band_rows:
            state = jnp.where(first_step, start_ref[:, v, :], previous_ref[0, :, v, :])
            cond = coarse_ref[:, v, :]
        elif v < 0:
            state = jnp.where(first_step, start_other_ref[:, band_rows + v, :], previous_other_ref[0, :, band_rows + v, :])
            cond = coarse_other_ref[:, band_rows + v, :]
        else:
            state = jnp.where(first_step, start_other_ref[:, v - band_rows, :], previous_other_ref[0, :, v - band_rows, :])
            cond = coarse_other_ref[:, v - band_rows, :]
        scaled = (scale_in * state).astype(jnp.bfloat16).astype(jnp.float32)
        inputs[0:channels, u * width : (u + 1) * width] = scaled
        inputs[channels:, u * width : (u + 1) * width] = cond.astype(jnp.float32)
    table = embed_ref[...].astype(jnp.float32)
    picked = jnp.where(lax.broadcasted_iota(jnp.int32, table.shape, 0) == level, table, 0.0)
    embed_row = jnp.sum(picked, axis=0, keepdims=True)
    feat = table.shape[1]
    embed = jnp.broadcast_to(embed_row, (feat, feat)).T[:, 0:1]
    lift_w = transposed(lift_ref[...]).astype(jnp.bfloat16)

    span = CHUNK_ROWS * width
    in_rows = band_rows + 2 * HALO
    for q in range(in_rows // CHUNK_ROWS):
        start = q * span
        chunk = inputs[:, start : start + span].astype(jnp.bfloat16)
        lifted = jnp.dot(lift_w, chunk, preferred_element_type=jnp.float32)
        lifted = (lifted + embed).astype(jnp.bfloat16)
        row0 = q * CHUNK_ROWS
        if HALO <= row0 < HALO + band_rows:
            keep = (row0 - HALO) * width
            lifted_keep[:, keep : keep + span] = lifted
        act = silu(normalize_features(lifted.astype(jnp.float32)))
        if row0 < HALO:
            act = jnp.where(top_outside, 0.0, act)
        if row0 >= HALO + band_rows:
            act = jnp.where(bottom_outside, 0.0, act)
        act_first[:, start : start + span] = act.astype(jnp.bfloat16)
    first_w = stack_taps(first_ref)
    mid_rows = band_rows + 2
    chunks = row_chunks(mid_rows)
    for q, (first, rows) in enumerate(chunks):
        span = rows * width
        lanes = lax.broadcasted_iota(jnp.int32, (1, span), 1)
        middle = conv_chunk(act_first, first_w, first, rows, width, lanes % width)
        act = silu(normalize_features(middle))
        if q == 0:
            act = jnp.where(jnp.logical_and(top_outside, lanes < width), 0.0, act)
        if q == len(chunks) - 1:
            act = jnp.where(jnp.logical_and(bottom_outside, lanes >= span - width), 0.0, act)
        act_next[:, first * width : first * width + span] = act.astype(jnp.bfloat16)
    second_w = stack_taps(second_ref)
    outgoing = []
    for q, (first, rows) in enumerate(row_chunks(band_rows)):
        span = rows * width
        lanes = lax.broadcasted_iota(jnp.int32, (1, span), 1)
        conv = conv_chunk(act_next, second_w, first, rows, width, lanes % width)
        start = first * width
        hidden_local[:, start : start + span] = lifted_keep[:, start : start + span].astype(jnp.float32) + conv
        copy = pltpu.make_async_copy(
            hidden_local.at[:, pl.ds(start, span)], hidden_ref.at[:, pl.ds(start, span)], hidden_sems.at[q]
        )
        copy.start()
        outgoing.append(copy)
    tokens_per_row = width // 4
    pool_w = jnp.where(
        lax.broadcasted_iota(jnp.int32, (width, tokens_per_row), 0) // 4
        == lax.broadcasted_iota(jnp.int32, (width, tokens_per_row), 1),
        1.0 / 16.0,
        0.0,
    ).astype(jnp.float32)
    pooled = []
    for a in range(band_rows // 4):
        row_sum = hidden_local[:, (4 * a) * width : (4 * a + 1) * width]
        for u in range(1, 4):
            row_sum = row_sum + hidden_local[:, (4 * a + u) * width : (4 * a + u + 1) * width]
        pooled.append(
            jnp.dot(row_sum, pool_w, precision=lax.Precision.HIGHEST, preferred_element_type=jnp.float32)
        )
    pooled = jnp.concatenate(pooled, axis=1)
    tokens = normalize_features(pooled).astype(jnp.bfloat16)
    project_t = jnp.concatenate(
        [transposed(project_ref[:, g * feat : (g + 1) * feat]) for g in range(3)], axis=0
    ).astype(jnp.bfloat16)
    projected = jnp.dot(project_t, tokens, preferred_element_type=jnp.float32)
    query_ref[...] = feature_map(projected[:feat])
    key_feats = feature_map(projected[feat : 2 * feat]).astype(jnp.bfloat16)
    value_rows = projected[2 * feat :].astype(jnp.bfloat16)
    ones = jnp.ones((HEAD_DIM, key_feats.shape[1]), jnp.bfloat16)
    contract_tokens = (((1,), (1,)), ((), ()))
    for h in range(feat // HEAD_DIM):
        keys_h = key_feats[h * HEAD_DIM : (h + 1) * HEAD_DIM]
        values_h = value_rows[h * HEAD_DIM : (h + 1) * HEAD_DIM]
        summary_t = lax.dot_general(values_h, keys_h, contract_tokens, preferred_element_type=jnp.float32)
        totals = lax.dot_general(ones, keys_h, contract_tokens, preferred_element_type=jnp.float32)
        stats_ref[h * HEAD_DIM : (h + 1) * HEAD_DIM, :] = jnp.concatenate([summary_t, totals], axis=1)
    for copy in outgoing:
        copy.wait()


def head_kernel(
    levels_ref, next_levels_ref, hidden_ref, query_ref, stats_own_ref, stats_other_ref, mix_ref, out_w_ref,
    previous_ref, start_ref, denoised_ref, seed_ref, hidden_local, hidden_sems,
    *, width, band_rows, level_count,
):
    group = 4 * width
    incoming = []
    for a in range(band_rows // 4):
        copy = pltpu.make_async_copy(
            hidden_ref.at[:, pl.ds(a * group, group)], hidden_local.at[:, pl.ds(a * group, group)], hidden_sems.at[a]
        )
        copy.start()
        incoming.append(copy)
    first_step = lax.axis_index("step") == lax.axis_size("step") - 1
    sigma_low = level_sigma(start_level(levels_ref, first_step), level_count, (1, width))
    sigma_high = level_sigma(next_levels_ref[0, 1], level_count, (1, width))
    spread = sigma_low * sigma_low + 0.25
    scale_skip = 0.25 / spread
    scale_out = 0.5 * sigma_low * lax.rsqrt(spread)
    sigma_gap = sigma_high - sigma_low
    feat = query_ref.shape[0]
    contexts = []
    for h in range(feat // HEAD_DIM):
        rows = slice(h * HEAD_DIM, (h + 1) * HEAD_DIM)
        queries_h = query_ref[rows, :]
        stats_h = stats_own_ref[rows, :] + stats_other_ref[rows, :]
        numerator = jnp.dot(
            stats_h[:, 0:HEAD_DIM], queries_h,
            precision=lax.Precision.HIGHEST, preferred_element_type=jnp.float32,
        )
        denominator = jnp.dot(
            stats_h[:, HEAD_DIM : 2 * HEAD_DIM], queries_h,
            precision=lax.Precision.HIGHEST, preferred_element_type=jnp.float32,
        )
        contexts.append(numerator / denominator)
    context = jnp.concatenate(contexts, axis=0).astype(jnp.bfloat16)
    mix_t = transposed(mix_ref[...]).astype(jnp.bfloat16)
    mixed = jnp.dot(mix_t, context, preferred_element_type=jnp.float32)
    tokens_per_row = width // 4
    expand = jnp.where(
        lax.broadcasted_iota(jnp.int32, (tokens_per_row, width), 0)
        == lax.broadcasted_iota(jnp.int32, (tokens_per_row, width), 1) // 4,
        1.0,
        0.0,
    ).astype(jnp.float32)
    out_w = out_w_ref[...]
    for a in range(band_rows // 4):
        incoming[a].wait()
        spread_mixed = jnp.dot(
            mixed[:, a * tokens_per_row : (a + 1) * tokens_per_row],
            expand,
            precision=lax.Precision.HIGHEST,
            preferred_element_type=jnp.float32,
        )
        for u in range(4):
            r = 4 * a + u
            start = r * width
            combined = hidden_local[:, start : start + width] + spread_mixed
            act = silu(normalize_features(combined)).astype(jnp.bfloat16)
            field = jnp.dot(out_w, act, preferred_element_type=jnp.float32)
            state = jnp.where(first_step, start_ref[:, r, :], previous_ref[0, :, r, :])
            denoised = scale_skip * state + scale_out * field
            denoised_ref[:, r, :] = denoised
            drift = sigma_gap * (state - denoised) / sigma_low
            seed_ref[:, r, :] = drift + jnp.where(first_step, state, 0.0)


def vmem():
    return pl.BlockSpec(memory_space=pltpu.VMEM)


def smem():
    return pl.BlockSpec(memory_space=pltpu.SMEM)


def edge_rows(x, axis, dim, width):
    length = x.shape[dim]
    last = lax.slice_in_dim(x, length - width, length, axis=dim)
    leading = lax.slice_in_dim(x, 0, width, axis=dim)
    return jnp.where(lax.axis_index(axis) == 0, last, leading)


def local(
    iterates,
    window_start,
    coarse,
    step_levels,
    level_embed,
    lift_weight,
    conv_first,
    conv_second,
    project_weight,
    mix_weight,
    output_weight,
):
    level_count = 2 * lax.axis_size("step") + 1
    bands = lax.axis_size("rows")
    steps = lax.axis_size("step")
    assert bands == 2
    swap = [(0, 1), (1, 0)]
    next_levels = lax.ppermute(step_levels, "step", [((h + 1) % steps, h) for h in range(steps)])
    previous = iterates
    previous_other = lax.ppermute(previous, "rows", swap)
    start_other = lax.ppermute(window_start, "rows", swap)
    coarse_other = lax.ppermute(coarse, "rows", swap)

    channels, band_rows, width = window_start.shape
    feat = lift_weight.shape[1]
    pixels = band_rows * width
    tokens = (band_rows // 4) * (width // 4)
    trunk = pl.pallas_call(
        lambda *refs: trunk_kernel(
            *refs, width=width, band_rows=band_rows, bands=bands, level_count=level_count
        ),
        out_shape=(
            jax.ShapeDtypeStruct((feat, pixels), jnp.float32),
            jax.ShapeDtypeStruct((feat, tokens), jnp.float32),
            jax.ShapeDtypeStruct((feat, 2 * HEAD_DIM), jnp.float32),
        ),
        in_specs=[smem()] + [vmem()] * 11,
        out_specs=(pl.BlockSpec(memory_space=pl.ANY), vmem(), vmem()),
        scratch_shapes=[
            pltpu.VMEM((channels + coarse.shape[0], (band_rows + 2 * HALO) * width), jnp.float32),
            pltpu.VMEM((feat, (band_rows + 2 * HALO) * width), jnp.bfloat16),
            pltpu.VMEM((feat, pixels), jnp.bfloat16),
            pltpu.VMEM((feat, (band_rows + 2) * width), jnp.bfloat16),
            pltpu.VMEM((feat, pixels), jnp.float32),
            pltpu.SemaphoreType.DMA((len(row_chunks(band_rows)),)),
        ],
    )
    hidden, queries, stats_own = trunk(
        step_levels,
        previous,
        window_start,
        start_other,
        previous_other,
        coarse,
        coarse_other,
        lift_weight,
        level_embed,
        conv_first,
        conv_second,
        project_weight,
    )
    stats_other = lax.ppermute(stats_own, "rows", swap)

    head = pl.pallas_call(
        lambda *refs: head_kernel(*refs, width=width, band_rows=band_rows, level_count=level_count),
        out_shape=(
            jax.ShapeDtypeStruct(window_start.shape, jnp.float32),
            jax.ShapeDtypeStruct(window_start.shape, jnp.float32),
        ),
        in_specs=[smem(), smem(), pl.BlockSpec(memory_space=pl.ANY)] + [vmem()] * 7,
        out_specs=(vmem(), vmem()),
        scratch_shapes=[
            pltpu.VMEM((feat, pixels), jnp.float32),
            pltpu.SemaphoreType.DMA((band_rows // 4,)),
        ],
    )
    denoised, seed = head(
        step_levels, next_levels, hidden, queries, stats_own, stats_other, mix_weight, output_weight.T,
        previous, window_start,
    )
    trajectory, denoised = rotated_prefix(seed, denoised, "step")
    return (trajectory[None], denoised[None])


def rotated_prefix(seed, denoised, axis):
    steps = lax.axis_size(axis)
    holder = lambda position: (position - 1) % steps
    shift = 1
    while 2 * shift < steps:
        pairs = [(holder(p), holder(p + shift)) for p in range(steps - shift)]
        seed = seed + lax.ppermute(seed, axis, pairs)
        shift *= 2
    moved = lax.ppermute(
        jnp.concatenate([seed, denoised], axis=0), axis, [(h, (h + 1) % steps) for h in range(steps)]
    )
    channels = seed.shape[0]
    if steps == 1:
        return moved[:channels], moved[channels:]
    far = lax.ppermute(seed, axis, [(holder(q), q + shift) for q in range(steps - shift)])
    return moved[:channels] + far, moved[channels:]


def solution(mesh):
    return jax.shard_map(
        local,
        mesh=mesh,
        in_specs=(
            P("step", "ens", "rows", None),
            P("ens", "rows", None),
            P("ens", "rows", None),
            P("step", None),
            P(),
            P(),
            P(),
            P(),
            P(),
            P(),
            P(),
        ),
        out_specs=(P("step", "ens", "rows", None), P("step", "ens", "rows", None)),
        check_vma=False,
    )
```

```python
import jax
import numpy as np
import jax.numpy as jnp
from jax import lax
from jax.experimental import pallas as pl
from jax.experimental.pallas import tpu as pltpu
from jax.sharding import PartitionSpec as P

HEAD_DIM = 64
HALO = 2
CHUNK_ROWS = 2
CONV_ROWS = 4

SIGMA_TOP = 8.0
SIGMA_END = 0.002
LOG_RATIO = float(np.log(np.float32(SIGMA_END / SIGMA_TOP)))


def from_behind(x, axis, by):
    devices = lax.axis_size(axis)
    pairs = [(i, i + by) for i in range(devices) if 0 <= i + by < devices]
    return lax.ppermute(x, axis, pairs)


def with_halo(x, axis, dim, width):
    devices, length = (lax.axis_size(axis), x.shape[dim])
    last = lax.slice_in_dim(x, length - width, length, axis=dim)
    leading = lax.slice_in_dim(x, 0, width, axis=dim)
    if devices == 2:
        me = lax.axis_index(axis)
        outgoing = jnp.where(me == 0, last, leading)
        incoming = lax.ppermute(outgoing, axis, [(0, 1), (1, 0)])
        zero = jnp.zeros_like(incoming)
        before = jnp.where(me == 0, zero, incoming)
        after = jnp.where(me == 0, incoming, zero)
    else:
        up = [(i, i + 1) for i in range(devices - 1)]
        down = [(j, i) for i, j in up]
        before = lax.ppermute(last, axis, up)
        after = lax.ppermute(leading, axis, down)
    return jnp.concatenate([before, x, after], axis=dim)


def band_sum(x, axis):
    devices = lax.axis_size(axis)
    if devices == 2:
        return x + lax.ppermute(x, axis, [(0, 1), (1, 0)])
    return lax.psum(x, axis)


def prefix_sum(x, axis):
    devices = lax.axis_size(axis)
    shift = 1
    while shift < devices:
        pairs = [(i, i + shift) for i in range(devices - shift)]
        x = x + lax.ppermute(x, axis, pairs)
        shift *= 2
    return x


def noise_level(levels, level_count):
    fraction = levels.astype(jnp.float32) / jnp.float32(level_count - 1)
    return SIGMA_TOP * jnp.exp(fraction * jnp.log(jnp.float32(SIGMA_END / SIGMA_TOP)))


def normalize_features(values):
    mean_square = jnp.sum(values * values, axis=0, keepdims=True) * (1.0 / values.shape[0])
    return values * lax.rsqrt(mean_square + 1e-06)


def silu(values):
    return values / (1.0 + jnp.exp(-values))


def feature_map(values):
    return jnp.where(values > 0, values + 1.0, jnp.exp(jnp.minimum(values, 0.0)))


def conv_chunk(source, weight, first_row, rows, width, column):
    span = rows * width
    stacked = jnp.concatenate(
        [source[:, (first_row + i) * width : (first_row + i) * width + span] for i in range(3)],
        axis=0,
    )
    taps = jnp.dot(weight, stacked, preferred_element_type=jnp.float32)
    feat = taps.shape[0] // 3
    left = pltpu.roll(taps[0:feat], 1, 1)
    right = pltpu.roll(taps[2 * feat : 3 * feat], span - 1, 1)
    result = taps[feat : 2 * feat]
    result = result + jnp.where(column != 0, left, 0.0)
    result = result + jnp.where(column != width - 1, right, 0.0)
    return result


def row_chunks(rows):
    chunks, first = [], 0
    while first < rows:
        size = min(CONV_ROWS, rows - first)
        chunks.append((first, size))
        first += size
    return chunks


def transposed(block):
    return block.astype(jnp.float32).T


def stack_taps(weight_ref):
    return jnp.concatenate(
        [
            jnp.concatenate([transposed(weight_ref[i, j]) for i in range(3)], axis=1)
            for j in range(3)
        ],
        axis=0,
    ).astype(jnp.bfloat16)


def level_sigma(level, level_count, shape):
    fraction = jnp.full(shape, level.astype(jnp.float32)) / jnp.float32(level_count - 1)
    return SIGMA_TOP * jnp.exp(fraction * LOG_RATIO)


def start_level(levels_ref, first_step):
    return jnp.where(first_step, 0, levels_ref[0, 1])


def trunk_kernel(
    levels_ref, next_levels_ref, previous_ref, start_ref, start_other_ref, previous_other_ref, coarse_ref,
    coarse_other_ref, lift_ref, embed_ref, first_ref, second_ref, project_ref,
    hidden_ref, query_ref, stats_ref, inputs, act_first, lifted_keep, act_next, hidden_local,
    hidden_sems, *, width, band_rows, bands, level_count,
):
    band = lax.axis_index("rows")
    first_step = lax.axis_index("step") == lax.axis_size("step") - 1
    top_outside = band == 0
    bottom_outside = band == bands - 1
    channels = start_ref.shape[0]
    level = start_level(levels_ref, first_step)
    sigma_low = level_sigma(level, level_count, (1, width))
    spread = sigma_low * sigma_low + 0.25
    scale_in = lax.rsqrt(spread)
    for u in range(band_rows + 2 * HALO):
        v = u - HALO
        if 0 <= v < band_rows:
            state = jnp.where(first_step, start_ref[:, v, :], previous_ref[0, :, v, :])
            cond = coarse_ref[:, v, :]
        elif v < 0:
            state = jnp.where(first_step, start_other_ref[:, band_rows + v, :], previous_other_ref[0, :, band_rows + v, :])
            cond = coarse_other_ref[:, band_rows + v, :]
        else:
            state = jnp.where(first_step, start_other_ref[:, v - band_rows, :], previous_other_ref[0, :, v - band_rows, :])
            cond = coarse_other_ref[:, v - band_rows, :]
        scaled = (scale_in * state).astype(jnp.bfloat16).astype(jnp.float32)
        inputs[0:channels, u * width : (u + 1) * width] = scaled
        inputs[channels:, u * width : (u + 1) * width] = cond.astype(jnp.float32)
    table = embed_ref[...].astype(jnp.float32)
    picked = jnp.where(lax.broadcasted_iota(jnp.int32, table.shape, 0) == level, table, 0.0)
    embed_row = jnp.sum(picked, axis=0, keepdims=True)
    feat = table.shape[1]
    embed = jnp.broadcast_to(embed_row, (feat, feat)).T[:, 0:1]
    lift_w = transposed(lift_ref[...]).astype(jnp.bfloat16)

    span = CHUNK_ROWS * width
    in_rows = band_rows + 2 * HALO
    for q in range(in_rows // CHUNK_ROWS):
        start = q * span
        chunk = inputs[:, start : start + span].astype(jnp.bfloat16)
        lifted = jnp.dot(lift_w, chunk, preferred_element_type=jnp.float32)
        lifted = (lifted + embed).astype(jnp.bfloat16)
        row0 = q * CHUNK_ROWS
        if HALO <= row0 < HALO + band_rows:
            keep = (row0 - HALO) * width
            lifted_keep[:, keep : keep + span] = lifted
        act = silu(normalize_features(lifted.astype(jnp.float32)))
        if row0 < HALO:
            act = jnp.where(top_outside, 0.0, act)
        if row0 >= HALO + band_rows:
            act = jnp.where(bottom_outside, 0.0, act)
        act_first[:, start : start + span] = act.astype(jnp.bfloat16)
    first_w = stack_taps(first_ref)
    mid_rows = band_rows + 2
    chunks = row_chunks(mid_rows)
    for q, (first, rows) in enumerate(chunks):
        span = rows * width
        lanes = lax.broadcasted_iota(jnp.int32, (1, span), 1)
        middle = conv_chunk(act_first, first_w, first, rows, width, lanes % width)
        act = silu(normalize_features(middle))
        if q == 0:
            act = jnp.where(jnp.logical_and(top_outside, lanes < width), 0.0, act)
        if q == len(chunks) - 1:
            act = jnp.where(jnp.logical_and(bottom_outside, lanes >= span - width), 0.0, act)
        act_next[:, first * width : first * width + span] = act.astype(jnp.bfloat16)
    second_w = stack_taps(second_ref)
    outgoing = []
    for q, (first, rows) in enumerate(row_chunks(band_rows)):
        span = rows * width
        lanes = lax.broadcasted_iota(jnp.int32, (1, span), 1)
        conv = conv_chunk(act_next, second_w, first, rows, width, lanes % width)
        start = first * width
        hidden_local[:, start : start + span] = lifted_keep[:, start : start + span].astype(jnp.float32) + conv
        copy = pltpu.make_async_copy(
            hidden_local.at[:, pl.ds(start, span)], hidden_ref.at[:, pl.ds(start, span)], hidden_sems.at[q]
        )
        copy.start()
        outgoing.append(copy)
    tokens_per_row = width // 4
    pool_w = jnp.where(
        lax.broadcasted_iota(jnp.int32, (width, tokens_per_row), 0) // 4
        == lax.broadcasted_iota(jnp.int32, (width, tokens_per_row), 1),
        1.0 / 16.0,
        0.0,
    ).astype(jnp.float32)
    pooled = []
    for a in range(band_rows // 4):
        row_sum = hidden_local[:, (4 * a) * width : (4 * a + 1) * width]
        for u in range(1, 4):
            row_sum = row_sum + hidden_local[:, (4 * a + u) * width : (4 * a + u + 1) * width]
        pooled.append(
            jnp.dot(row_sum, pool_w, precision=lax.Precision.HIGHEST, preferred_element_type=jnp.float32)
        )
    pooled = jnp.concatenate(pooled, axis=1)
    tokens = normalize_features(pooled).astype(jnp.bfloat16)
    project_t = jnp.concatenate(
        [transposed(project_ref[:, g * feat : (g + 1) * feat]) for g in range(3)], axis=0
    ).astype(jnp.bfloat16)
    projected = jnp.dot(project_t, tokens, preferred_element_type=jnp.float32)
    query_ref[...] = feature_map(projected[:feat])
    key_feats = feature_map(projected[feat : 2 * feat]).astype(jnp.bfloat16)
    value_rows = projected[2 * feat :].astype(jnp.bfloat16)
    ones = jnp.ones((HEAD_DIM, key_feats.shape[1]), jnp.bfloat16)
    contract_tokens = (((1,), (1,)), ((), ()))
    for h in range(feat // HEAD_DIM):
        keys_h = key_feats[h * HEAD_DIM : (h + 1) * HEAD_DIM]
        values_h = value_rows[h * HEAD_DIM : (h + 1) * HEAD_DIM]
        summary_t = lax.dot_general(values_h, keys_h, contract_tokens, preferred_element_type=jnp.float32)
        totals = lax.dot_general(ones, keys_h, contract_tokens, preferred_element_type=jnp.float32)
        stats_ref[h * HEAD_DIM : (h + 1) * HEAD_DIM, :] = jnp.concatenate([summary_t, totals], axis=1)
    for copy in outgoing:
        copy.wait()


def head_kernel(
    levels_ref, next_levels_ref, hidden_ref, query_ref, stats_own_ref, stats_other_ref, mix_ref, out_w_ref,
    previous_ref, start_ref, denoised_ref, seed_ref, hidden_local, hidden_sems,
    *, width, band_rows, level_count,
):
    group = 4 * width
    incoming = []
    for a in range(band_rows // 4):
        copy = pltpu.make_async_copy(
            hidden_ref.at[:, pl.ds(a * group, group)], hidden_local.at[:, pl.ds(a * group, group)], hidden_sems.at[a]
        )
        copy.start()
        incoming.append(copy)
    first_step = lax.axis_index("step") == lax.axis_size("step") - 1
    sigma_low = level_sigma(start_level(levels_ref, first_step), level_count, (1, width))
    sigma_high = level_sigma(next_levels_ref[0, 1], level_count, (1, width))
    spread = sigma_low * sigma_low + 0.25
    scale_skip = 0.25 / spread
    scale_out = 0.5 * sigma_low * lax.rsqrt(spread)
    sigma_gap = sigma_high - sigma_low
    feat = query_ref.shape[0]
    contexts = []
    for h in range(feat // HEAD_DIM):
        rows = slice(h * HEAD_DIM, (h + 1) * HEAD_DIM)
        queries_h = query_ref[rows, :]
        stats_h = stats_own_ref[rows, :] + stats_other_ref[rows, :]
        numerator = jnp.dot(
            stats_h[:, 0:HEAD_DIM], queries_h,
            precision=lax.Precision.HIGHEST, preferred_element_type=jnp.float32,
        )
        denominator = jnp.dot(
            stats_h[:, HEAD_DIM : 2 * HEAD_DIM], queries_h,
            precision=lax.Precision.HIGHEST, preferred_element_type=jnp.float32,
        )
        contexts.append(numerator / denominator)
    context = jnp.concatenate(contexts, axis=0).astype(jnp.bfloat16)
    mix_t = transposed(mix_ref[...]).astype(jnp.bfloat16)
    mixed = jnp.dot(mix_t, context, preferred_element_type=jnp.float32)
    tokens_per_row = width // 4
    expand = jnp.where(
        lax.broadcasted_iota(jnp.int32, (tokens_per_row, width), 0)
        == lax.broadcasted_iota(jnp.int32, (tokens_per_row, width), 1) // 4,
        1.0,
        0.0,
    ).astype(jnp.float32)
    out_w = out_w_ref[...]
    for a in range(band_rows // 4):
        incoming[a].wait()
        spread_mixed = jnp.dot(
            mixed[:, a * tokens_per_row : (a + 1) * tokens_per_row],
            expand,
            precision=lax.Precision.HIGHEST,
            preferred_element_type=jnp.float32,
        )
        for u in range(4):
            r = 4 * a + u
            start = r * width
            combined = hidden_local[:, start : start + width] + spread_mixed
            act = silu(normalize_features(combined)).astype(jnp.bfloat16)
            field = jnp.dot(out_w, act, preferred_element_type=jnp.float32)
            state = jnp.where(first_step, start_ref[:, r, :], previous_ref[0, :, r, :])
            denoised = scale_skip * state + scale_out * field
            denoised_ref[:, r, :] = denoised
            drift = sigma_gap * (state - denoised) / sigma_low
            seed_ref[:, r, :] = drift + jnp.where(first_step, state, 0.0)


def vmem():
    return pl.BlockSpec(memory_space=pltpu.VMEM)


def smem():
    return pl.BlockSpec(memory_space=pltpu.SMEM)


def edge_rows(x, axis, dim, width):
    length = x.shape[dim]
    last = lax.slice_in_dim(x, length - width, length, axis=dim)
    leading = lax.slice_in_dim(x, 0, width, axis=dim)
    return jnp.where(lax.axis_index(axis) == 0, last, leading)


def local(
    iterates,
    window_start,
    coarse,
    step_levels,
    level_embed,
    lift_weight,
    conv_first,
    conv_second,
    project_weight,
    mix_weight,
    output_weight,
):
    level_count = 2 * lax.axis_size("step") + 1
    bands = lax.axis_size("rows")
    steps = lax.axis_size("step")
    assert bands == 2
    swap = [(0, 1), (1, 0)]
    next_levels = lax.ppermute(step_levels, "step", [((h + 1) % steps, h) for h in range(steps)])
    previous = iterates
    previous_other = lax.ppermute(previous, "rows", swap)
    start_other = lax.ppermute(window_start, "rows", swap)
    coarse_other = lax.ppermute(coarse, "rows", swap)

    channels, band_rows, width = window_start.shape
    feat = lift_weight.shape[1]
    pixels = band_rows * width
    tokens = (band_rows // 4) * (width // 4)
    trunk = pl.pallas_call(
        lambda *refs: trunk_kernel(
            *refs, width=width, band_rows=band_rows, bands=bands, level_count=level_count
        ),
        out_shape=(
            jax.ShapeDtypeStruct((feat, pixels), jnp.float32),
            jax.ShapeDtypeStruct((feat, tokens), jnp.float32),
            jax.ShapeDtypeStruct((feat, 2 * HEAD_DIM), jnp.float32),
        ),
        in_specs=[smem(), smem()] + [vmem()] * 11,
        out_specs=(pl.BlockSpec(memory_space=pl.ANY), vmem(), vmem()),
        cost_estimate=pl.CostEstimate(
            flops=2 * (3 * feat) ** 2 * (2 * band_rows + 2) * width,
            transcendentals=3 * feat * (band_rows + 2 * HALO) * width,
            bytes_accessed=6 * feat * pixels,
        ),
        scratch_shapes=[
            pltpu.VMEM((channels + coarse.shape[0], (band_rows + 2 * HALO) * width), jnp.float32),
            pltpu.VMEM((feat, (band_rows + 2 * HALO) * width), jnp.bfloat16),
            pltpu.VMEM((feat, pixels), jnp.bfloat16),
            pltpu.VMEM((feat, (band_rows + 2) * width), jnp.bfloat16),
            pltpu.VMEM((feat, pixels), jnp.float32),
            pltpu.SemaphoreType.DMA((len(row_chunks(band_rows)),)),
        ],
    )
    hidden, queries, stats_own = trunk(
        step_levels,
        next_levels,
        previous,
        window_start,
        start_other,
        previous_other,
        coarse,
        coarse_other,
        lift_weight,
        level_embed,
        conv_first,
        conv_second,
        project_weight,
    )
    stats_other = lax.ppermute(stats_own, "rows", swap)

    head = pl.pallas_call(
        lambda *refs: head_kernel(*refs, width=width, band_rows=band_rows, level_count=level_count),
        out_shape=(
            jax.ShapeDtypeStruct(window_start.shape, jnp.float32),
            jax.ShapeDtypeStruct(window_start.shape, jnp.float32),
        ),
        in_specs=[smem(), smem(), pl.BlockSpec(memory_space=pl.ANY)] + [vmem()] * 7,
        out_specs=(vmem(), vmem()),
        cost_estimate=pl.CostEstimate(
            flops=8 * feat * feat * pixels,
            transcendentals=2 * feat * pixels,
            bytes_accessed=5 * feat * pixels,
        ),
        scratch_shapes=[
            pltpu.VMEM((feat, pixels), jnp.float32),
            pltpu.SemaphoreType.DMA((band_rows // 4,)),
        ],
    )
    denoised, seed = head(
        step_levels, next_levels, hidden, queries, stats_own, stats_other, mix_weight, output_weight.T,
        previous, window_start,
    )
    trajectory, denoised = rotated_prefix(seed, denoised, "step")
    return (trajectory[None], denoised[None])


def rotated_prefix(seed, denoised, axis):
    steps = lax.axis_size(axis)
    holder = lambda position: (position - 1) % steps
    shift = 1
    while 2 * shift < steps:
        pairs = [(holder(p), holder(p + shift)) for p in range(steps - shift)]
        seed = seed + lax.ppermute(seed, axis, pairs)
        shift *= 2
    moved = lax.ppermute(
        jnp.concatenate([seed, denoised], axis=0), axis, [(h, (h + 1) % steps) for h in range(steps)]
    )
    channels = seed.shape[0]
    if steps == 1:
        return moved[:channels], moved[channels:]
    far = lax.ppermute(seed, axis, [(holder(q), q + shift) for q in range(steps - shift)])
    return moved[:channels] + far, moved[channels:]


def solution(mesh):
    return jax.shard_map(
        local,
        mesh=mesh,
        in_specs=(
            P("step", "ens", "rows", None),
            P("ens", "rows", None),
            P("ens", "rows", None),
            P("step", None),
            P(),
            P(),
            P(),
            P(),
            P(),
            P(),
            P(),
        ),
        out_specs=(P("step", "ens", "rows", None), P("step", "ens", "rows", None)),
        check_vma=False,
    )
```

```python
import jax
import numpy as np
import jax.numpy as jnp
from jax import lax
from jax.experimental import pallas as pl
from jax.experimental.pallas import tpu as pltpu
from jax.sharding import PartitionSpec as P

HEAD_DIM = 64
HALO = 2
CHUNK_ROWS = 2
CONV_ROWS = 4

SIGMA_TOP = 8.0
SIGMA_END = 0.002
LOG_RATIO = float(np.log(np.float32(SIGMA_END / SIGMA_TOP)))


def from_behind(x, axis, by):
    devices = lax.axis_size(axis)
    pairs = [(i, i + by) for i in range(devices) if 0 <= i + by < devices]
    return lax.ppermute(x, axis, pairs)


def with_halo(x, axis, dim, width):
    devices, length = (lax.axis_size(axis), x.shape[dim])
    last = lax.slice_in_dim(x, length - width, length, axis=dim)
    leading = lax.slice_in_dim(x, 0, width, axis=dim)
    if devices == 2:
        me = lax.axis_index(axis)
        outgoing = jnp.where(me == 0, last, leading)
        incoming = lax.ppermute(outgoing, axis, [(0, 1), (1, 0)])
        zero = jnp.zeros_like(incoming)
        before = jnp.where(me == 0, zero, incoming)
        after = jnp.where(me == 0, incoming, zero)
    else:
        up = [(i, i + 1) for i in range(devices - 1)]
        down = [(j, i) for i, j in up]
        before = lax.ppermute(last, axis, up)
        after = lax.ppermute(leading, axis, down)
    return jnp.concatenate([before, x, after], axis=dim)


def band_sum(x, axis):
    devices = lax.axis_size(axis)
    if devices == 2:
        return x + lax.ppermute(x, axis, [(0, 1), (1, 0)])
    return lax.psum(x, axis)


def prefix_sum(x, axis):
    devices = lax.axis_size(axis)
    shift = 1
    while shift < devices:
        pairs = [(i, i + shift) for i in range(devices - shift)]
        x = x + lax.ppermute(x, axis, pairs)
        shift *= 2
    return x


def noise_level(levels, level_count):
    fraction = levels.astype(jnp.float32) / jnp.float32(level_count - 1)
    return SIGMA_TOP * jnp.exp(fraction * jnp.log(jnp.float32(SIGMA_END / SIGMA_TOP)))


def normalize_features(values):
    mean_square = jnp.sum(values * values, axis=0, keepdims=True) * (1.0 / values.shape[0])
    return values * lax.rsqrt(mean_square + 1e-06)


def silu(values):
    return values / (1.0 + jnp.exp(-values))


def feature_map(values):
    return jnp.where(values > 0, values + 1.0, jnp.exp(jnp.minimum(values, 0.0)))


def conv_chunk(source, weight, first_row, rows, width, column):
    span = rows * width
    stacked = jnp.concatenate(
        [source[:, (first_row + i) * width : (first_row + i) * width + span] for i in range(3)],
        axis=0,
    )
    taps = jnp.dot(weight, stacked, preferred_element_type=jnp.float32)
    feat = taps.shape[0] // 3
    left = pltpu.roll(taps[0:feat], 1, 1)
    right = pltpu.roll(taps[2 * feat : 3 * feat], span - 1, 1)
    result = taps[feat : 2 * feat]
    result = result + jnp.where(column != 0, left, 0.0)
    result = result + jnp.where(column != width - 1, right, 0.0)
    return result


def row_chunks(rows):
    chunks, first = [], 0
    while first < rows:
        size = min(CONV_ROWS, rows - first)
        chunks.append((first, size))
        first += size
    return chunks


def transposed(block):
    return block.astype(jnp.float32).T


def stack_taps(weight_ref):
    return jnp.concatenate(
        [
            jnp.concatenate([transposed(weight_ref[i, j]) for i in range(3)], axis=1)
            for j in range(3)
        ],
        axis=0,
    ).astype(jnp.bfloat16)


def level_sigma(level, level_count, shape):
    fraction = jnp.full(shape, level.astype(jnp.float32)) / jnp.float32(level_count - 1)
    return SIGMA_TOP * jnp.exp(fraction * LOG_RATIO)


def start_level(levels_ref, first_step):
    return jnp.where(first_step, 0, levels_ref[0, 1])


def trunk_kernel(
    levels_ref, previous_ref, start_ref, start_other_ref, previous_other_ref, coarse_ref,
    coarse_other_ref, lift_ref, embed_ref, first_ref, second_ref, project_ref,
    hidden_ref, query_ref, stats_ref, inputs, act_first, lifted_keep, act_next, hidden_local,
    hidden_staged, hidden_sems, *, width, band_rows, bands, level_count,
):
    band = lax.axis_index("rows")
    first_step = lax.axis_index("step") == lax.axis_size("step") - 1
    top_outside = band == 0
    bottom_outside = band == bands - 1
    channels = start_ref.shape[0]
    level = start_level(levels_ref, first_step)
    sigma_low = level_sigma(level, level_count, (1, width))
    spread = sigma_low * sigma_low + 0.25
    scale_in = lax.rsqrt(spread)
    for u in range(band_rows + 2 * HALO):
        v = u - HALO
        if 0 <= v < band_rows:
            state = jnp.where(first_step, start_ref[:, v, :], previous_ref[0, :, v, :])
            cond = coarse_ref[:, v, :]
        elif v < 0:
            state = jnp.where(first_step, start_other_ref[:, band_rows + v, :], previous_other_ref[0, :, band_rows + v, :])
            cond = coarse_other_ref[:, band_rows + v, :]
        else:
            state = jnp.where(first_step, start_other_ref[:, v - band_rows, :], previous_other_ref[0, :, v - band_rows, :])
            cond = coarse_other_ref[:, v - band_rows, :]
        scaled = (scale_in * state).astype(jnp.bfloat16).astype(jnp.float32)
        inputs[0:channels, u * width : (u + 1) * width] = scaled
        inputs[channels:, u * width : (u + 1) * width] = cond.astype(jnp.float32)
    table = embed_ref[...].astype(jnp.float32)
    picked = jnp.where(lax.broadcasted_iota(jnp.int32, table.shape, 0) == level, table, 0.0)
    embed_row = jnp.sum(picked, axis=0, keepdims=True)
    feat = table.shape[1]
    embed = jnp.broadcast_to(embed_row, (feat, feat)).T[:, 0:1]
    lift_w = transposed(lift_ref[...]).astype(jnp.bfloat16)

    span = CHUNK_ROWS * width
    in_rows = band_rows + 2 * HALO
    for q in range(in_rows // CHUNK_ROWS):
        start = q * span
        chunk = inputs[:, start : start + span].astype(jnp.bfloat16)
        lifted = jnp.dot(lift_w, chunk, preferred_element_type=jnp.float32)
        lifted = (lifted + embed).astype(jnp.bfloat16)
        row0 = q * CHUNK_ROWS
        if HALO <= row0 < HALO + band_rows:
            keep = (row0 - HALO) * width
            lifted_keep[:, keep : keep + span] = lifted
        act = silu(normalize_features(lifted.astype(jnp.float32)))
        if row0 < HALO:
            act = jnp.where(top_outside, 0.0, act)
        if row0 >= HALO + band_rows:
            act = jnp.where(bottom_outside, 0.0, act)
        act_first[:, start : start + span] = act.astype(jnp.bfloat16)
    first_w = stack_taps(first_ref)
    mid_rows = band_rows + 2
    chunks = row_chunks(mid_rows)
    for q, (first, rows) in enumerate(chunks):
        span = rows * width
        lanes = lax.broadcasted_iota(jnp.int32, (1, span), 1)
        middle = conv_chunk(act_first, first_w, first, rows, width, lanes % width)
        act = silu(normalize_features(middle))
        if q == 0:
            act = jnp.where(jnp.logical_and(top_outside, lanes < width), 0.0, act)
        if q == len(chunks) - 1:
            act = jnp.where(jnp.logical_and(bottom_outside, lanes >= span - width), 0.0, act)
        act_next[:, first * width : first * width + span] = act.astype(jnp.bfloat16)
    second_w = stack_taps(second_ref)
    outgoing = []
    for q, (first, rows) in enumerate(row_chunks(band_rows)):
        span = rows * width
        lanes = lax.broadcasted_iota(jnp.int32, (1, span), 1)
        conv = conv_chunk(act_next, second_w, first, rows, width, lanes % width)
        start = first * width
        hidden = lifted_keep[:, start : start + span].astype(jnp.float32) + conv
        hidden_local[:, start : start + span] = hidden
        hidden_staged[:, start : start + span] = hidden.astype(jnp.bfloat16)
        copy = pltpu.make_async_copy(
            hidden_staged.at[:, pl.ds(start, span)], hidden_ref.at[:, pl.ds(start, span)], hidden_sems.at[q]
        )
        copy.start()
        outgoing.append(copy)
    tokens_per_row = width // 4
    pool_w = jnp.where(
        lax.broadcasted_iota(jnp.int32, (width, tokens_per_row), 0) // 4
        == lax.broadcasted_iota(jnp.int32, (width, tokens_per_row), 1),
        1.0 / 16.0,
        0.0,
    ).astype(jnp.float32)
    pooled = []
    for a in range(band_rows // 4):
        row_sum = hidden_local[:, (4 * a) * width : (4 * a + 1) * width]
        for u in range(1, 4):
            row_sum = row_sum + hidden_local[:, (4 * a + u) * width : (4 * a + u + 1) * width]
        pooled.append(
            jnp.dot(row_sum, pool_w, precision=lax.Precision.HIGHEST, preferred_element_type=jnp.float32)
        )
    pooled = jnp.concatenate(pooled, axis=1)
    tokens = normalize_features(pooled).astype(jnp.bfloat16)
    project_t = jnp.concatenate(
        [transposed(project_ref[:, g * feat : (g + 1) * feat]) for g in range(3)], axis=0
    ).astype(jnp.bfloat16)
    projected = jnp.dot(project_t, tokens, preferred_element_type=jnp.float32)
    query_ref[...] = feature_map(projected[:feat])
    key_feats = feature_map(projected[feat : 2 * feat]).astype(jnp.bfloat16)
    value_rows = projected[2 * feat :].astype(jnp.bfloat16)
    ones = jnp.ones((HEAD_DIM, key_feats.shape[1]), jnp.bfloat16)
    contract_tokens = (((1,), (1,)), ((), ()))
    for h in range(feat // HEAD_DIM):
        keys_h = key_feats[h * HEAD_DIM : (h + 1) * HEAD_DIM]
        values_h = value_rows[h * HEAD_DIM : (h + 1) * HEAD_DIM]
        summary_t = lax.dot_general(values_h, keys_h, contract_tokens, preferred_element_type=jnp.float32)
        totals = lax.dot_general(ones, keys_h, contract_tokens, preferred_element_type=jnp.float32)
        stats_ref[h * HEAD_DIM : (h + 1) * HEAD_DIM, :] = jnp.concatenate([summary_t, totals], axis=1)
    for copy in outgoing:
        copy.wait()


def head_kernel(
    levels_ref, next_levels_ref, hidden_ref, query_ref, stats_own_ref, stats_other_ref, mix_ref, out_w_ref,
    previous_ref, start_ref, denoised_ref, seed_ref, hidden_local, hidden_sems,
    *, width, band_rows, level_count,
):
    group = 4 * width
    incoming = []
    for a in range(band_rows // 4):
        copy = pltpu.make_async_copy(
            hidden_ref.at[:, pl.ds(a * group, group)], hidden_local.at[:, pl.ds(a * group, group)], hidden_sems.at[a]
        )
        copy.start()
        incoming.append(copy)
    first_step = lax.axis_index("step") == lax.axis_size("step") - 1
    sigma_low = level_sigma(start_level(levels_ref, first_step), level_count, (1, width))
    sigma_high = level_sigma(next_levels_ref[0, 1], level_count, (1, width))
    spread = sigma_low * sigma_low + 0.25
    scale_skip = 0.25 / spread
    scale_out = 0.5 * sigma_low * lax.rsqrt(spread)
    sigma_gap = sigma_high - sigma_low
    feat = query_ref.shape[0]
    contexts = []
    for h in range(feat // HEAD_DIM):
        rows = slice(h * HEAD_DIM, (h + 1) * HEAD_DIM)
        queries_h = query_ref[rows, :]
        stats_h = stats_own_ref[rows, :] + stats_other_ref[rows, :]
        numerator = jnp.dot(
            stats_h[:, 0:HEAD_DIM], queries_h,
            precision=lax.Precision.HIGHEST, preferred_element_type=jnp.float32,
        )
        denominator = jnp.dot(
            stats_h[:, HEAD_DIM : 2 * HEAD_DIM], queries_h,
            precision=lax.Precision.HIGHEST, preferred_element_type=jnp.float32,
        )
        contexts.append(numerator / denominator)
    context = jnp.concatenate(contexts, axis=0).astype(jnp.bfloat16)
    mix_t = transposed(mix_ref[...]).astype(jnp.bfloat16)
    mixed = jnp.dot(mix_t, context, preferred_element_type=jnp.float32)
    tokens_per_row = width // 4
    expand = jnp.where(
        lax.broadcasted_iota(jnp.int32, (tokens_per_row, width), 0)
        == lax.broadcasted_iota(jnp.int32, (tokens_per_row, width), 1) // 4,
        1.0,
        0.0,
    ).astype(jnp.float32)
    out_w = out_w_ref[...]
    for a in range(band_rows // 4):
        incoming[a].wait()
        spread_mixed = jnp.dot(
            mixed[:, a * tokens_per_row : (a + 1) * tokens_per_row],
            expand,
            precision=lax.Precision.HIGHEST,
            preferred_element_type=jnp.float32,
        )
        for u in range(4):
            r = 4 * a + u
            start = r * width
            combined = hidden_local[:, start : start + width].astype(jnp.float32) + spread_mixed
            act = silu(normalize_features(combined)).astype(jnp.bfloat16)
            field = jnp.dot(out_w, act, preferred_element_type=jnp.float32)
            state = jnp.where(first_step, start_ref[:, r, :], previous_ref[0, :, r, :])
            denoised = scale_skip * state + scale_out * field
            denoised_ref[:, r, :] = denoised
            drift = sigma_gap * (state - denoised) / sigma_low
            seed_ref[:, r, :] = drift + jnp.where(first_step, state, 0.0)


def vmem():
    return pl.BlockSpec(memory_space=pltpu.VMEM)


def smem():
    return pl.BlockSpec(memory_space=pltpu.SMEM)


def edge_rows(x, axis, dim, width):
    length = x.shape[dim]
    last = lax.slice_in_dim(x, length - width, length, axis=dim)
    leading = lax.slice_in_dim(x, 0, width, axis=dim)
    return jnp.where(lax.axis_index(axis) == 0, last, leading)


def local(
    iterates,
    window_start,
    coarse,
    step_levels,
    level_embed,
    lift_weight,
    conv_first,
    conv_second,
    project_weight,
    mix_weight,
    output_weight,
):
    level_count = 2 * lax.axis_size("step") + 1
    bands = lax.axis_size("rows")
    steps = lax.axis_size("step")
    assert bands == 2
    swap = [(0, 1), (1, 0)]
    next_levels = lax.ppermute(step_levels, "step", [((h + 1) % steps, h) for h in range(steps)])
    previous = iterates
    previous_other = lax.ppermute(previous, "rows", swap)
    start_other = lax.ppermute(window_start, "rows", swap)
    coarse_other = lax.ppermute(coarse, "rows", swap)

    channels, band_rows, width = window_start.shape
    feat = lift_weight.shape[1]
    pixels = band_rows * width
    tokens = (band_rows // 4) * (width // 4)
    trunk = pl.pallas_call(
        lambda *refs: trunk_kernel(
            *refs, width=width, band_rows=band_rows, bands=bands, level_count=level_count
        ),
        out_shape=(
            jax.ShapeDtypeStruct((feat, pixels), jnp.bfloat16),
            jax.ShapeDtypeStruct((feat, tokens), jnp.float32),
            jax.ShapeDtypeStruct((feat, 2 * HEAD_DIM), jnp.float32),
        ),
        in_specs=[smem()] + [vmem()] * 11,
        out_specs=(pl.BlockSpec(memory_space=pl.ANY), vmem(), vmem()),
        scratch_shapes=[
            pltpu.VMEM((channels + coarse.shape[0], (band_rows + 2 * HALO) * width), jnp.float32),
            pltpu.VMEM((feat, (band_rows + 2 * HALO) * width), jnp.bfloat16),
            pltpu.VMEM((feat, pixels), jnp.bfloat16),
            pltpu.VMEM((feat, (band_rows + 2) * width), jnp.bfloat16),
            pltpu.VMEM((feat, pixels), jnp.float32),
            pltpu.VMEM((feat, pixels), jnp.bfloat16),
            pltpu.SemaphoreType.DMA((len(row_chunks(band_rows)),)),
        ],
    )
    hidden, queries, stats_own = trunk(
        step_levels,
        previous,
        window_start,
        start_other,
        previous_other,
        coarse,
        coarse_other,
        lift_weight,
        level_embed,
        conv_first,
        conv_second,
        project_weight,
    )
    stats_other = lax.ppermute(stats_own, "rows", swap)

    head = pl.pallas_call(
        lambda *refs: head_kernel(*refs, width=width, band_rows=band_rows, level_count=level_count),
        out_shape=(
            jax.ShapeDtypeStruct(window_start.shape, jnp.float32),
            jax.ShapeDtypeStruct(window_start.shape, jnp.float32),
        ),
        in_specs=[smem(), smem(), pl.BlockSpec(memory_space=pl.ANY)] + [vmem()] * 7,
        out_specs=(vmem(), vmem()),
        scratch_shapes=[
            pltpu.VMEM((feat, pixels), jnp.bfloat16),
            pltpu.SemaphoreType.DMA((band_rows // 4,)),
        ],
    )
    denoised, seed = head(
        step_levels, next_levels, hidden, queries, stats_own, stats_other, mix_weight, output_weight.T,
        previous, window_start,
    )
    trajectory, denoised = rotated_prefix(seed, denoised, "step")
    return (trajectory[None], denoised[None])


def rotated_prefix(seed, denoised, axis):
    steps = lax.axis_size(axis)
    holder = lambda position: (position - 1) % steps
    shift = 1
    while 2 * shift < steps:
        pairs = [(holder(p), holder(p + shift)) for p in range(steps - shift)]
        seed = seed + lax.ppermute(seed, axis, pairs)
        shift *= 2
    moved = lax.ppermute(
        jnp.concatenate([seed, denoised], axis=0), axis, [(h, (h + 1) % steps) for h in range(steps)]
    )
    channels = seed.shape[0]
    if steps == 1:
        return moved[:channels], moved[channels:]
    far = lax.ppermute(seed, axis, [(holder(q), q + shift) for q in range(steps - shift)])
    return moved[:channels] + far, moved[channels:]


def solution(mesh):
    return jax.shard_map(
        local,
        mesh=mesh,
        in_specs=(
            P("step", "ens", "rows", None),
            P("ens", "rows", None),
            P("ens", "rows", None),
            P("step", None),
            P(),
            P(),
            P(),
            P(),
            P(),
            P(),
            P(),
        ),
        out_specs=(P("step", "ens", "rows", None), P("step", "ens", "rows", None)),
        check_vma=False,
    )
```

```python
import jax
import numpy as np
import jax.numpy as jnp
from jax import lax
from jax.experimental import pallas as pl
from jax.experimental.pallas import tpu as pltpu
from jax.sharding import PartitionSpec as P

HEAD_DIM = 64
HALO = 2
CHUNK_ROWS = 2
CONV_ROWS = 8

SIGMA_TOP = 8.0
SIGMA_END = 0.002
LOG_RATIO = float(np.log(np.float32(SIGMA_END / SIGMA_TOP)))


def from_behind(x, axis, by):
    devices = lax.axis_size(axis)
    pairs = [(i, i + by) for i in range(devices) if 0 <= i + by < devices]
    return lax.ppermute(x, axis, pairs)


def with_halo(x, axis, dim, width):
    devices, length = (lax.axis_size(axis), x.shape[dim])
    last = lax.slice_in_dim(x, length - width, length, axis=dim)
    leading = lax.slice_in_dim(x, 0, width, axis=dim)
    if devices == 2:
        me = lax.axis_index(axis)
        outgoing = jnp.where(me == 0, last, leading)
        incoming = lax.ppermute(outgoing, axis, [(0, 1), (1, 0)])
        zero = jnp.zeros_like(incoming)
        before = jnp.where(me == 0, zero, incoming)
        after = jnp.where(me == 0, incoming, zero)
    else:
        up = [(i, i + 1) for i in range(devices - 1)]
        down = [(j, i) for i, j in up]
        before = lax.ppermute(last, axis, up)
        after = lax.ppermute(leading, axis, down)
    return jnp.concatenate([before, x, after], axis=dim)


def band_sum(x, axis):
    devices = lax.axis_size(axis)
    if devices == 2:
        return x + lax.ppermute(x, axis, [(0, 1), (1, 0)])
    return lax.psum(x, axis)


def prefix_sum(x, axis):
    devices = lax.axis_size(axis)
    shift = 1
    while shift < devices:
        pairs = [(i, i + shift) for i in range(devices - shift)]
        x = x + lax.ppermute(x, axis, pairs)
        shift *= 2
    return x


def noise_level(levels, level_count):
    fraction = levels.astype(jnp.float32) / jnp.float32(level_count - 1)
    return SIGMA_TOP * jnp.exp(fraction * jnp.log(jnp.float32(SIGMA_END / SIGMA_TOP)))


def normalize_features(values):
    mean_square = jnp.sum(values * values, axis=0, keepdims=True) * (1.0 / values.shape[0])
    return values * lax.rsqrt(mean_square + 1e-06)


def silu(values):
    return values / (1.0 + jnp.exp(-values))


def feature_map(values):
    return jnp.where(values > 0, values + 1.0, jnp.exp(jnp.minimum(values, 0.0)))


def conv_chunk(source, weight, first_row, rows, width, column):
    span = rows * width
    stacked = jnp.concatenate(
        [source[:, (first_row + i) * width : (first_row + i) * width + span] for i in range(3)],
        axis=0,
    )
    taps = jnp.dot(weight, stacked, preferred_element_type=jnp.float32)
    feat = taps.shape[0] // 3
    left = pltpu.roll(taps[0:feat], 1, 1)
    right = pltpu.roll(taps[2 * feat : 3 * feat], span - 1, 1)
    result = taps[feat : 2 * feat]
    result = result + jnp.where(column != 0, left, 0.0)
    result = result + jnp.where(column != width - 1, right, 0.0)
    return result


def row_chunks(rows):
    chunks, first = [], 0
    while first < rows:
        size = min(CONV_ROWS, rows - first)
        chunks.append((first, size))
        first += size
    return chunks


def transposed(block):
    return block.astype(jnp.float32).T


def stack_taps(weight_ref):
    return jnp.concatenate(
        [
            jnp.concatenate([transposed(weight_ref[i, j]) for i in range(3)], axis=1)
            for j in range(3)
        ],
        axis=0,
    ).astype(jnp.bfloat16)


def level_sigma(level, level_count, shape):
    fraction = jnp.full(shape, level.astype(jnp.float32)) / jnp.float32(level_count - 1)
    return SIGMA_TOP * jnp.exp(fraction * LOG_RATIO)


def start_level(levels_ref, first_step):
    return jnp.where(first_step, 0, levels_ref[0, 1])


def trunk_kernel(
    levels_ref, previous_ref, start_ref, start_other_ref, previous_other_ref, coarse_ref,
    coarse_other_ref, lift_ref, embed_ref, first_ref, second_ref, project_ref,
    hidden_ref, query_ref, stats_ref, inputs, act_first, lifted_keep, act_next, hidden_local,
    hidden_sems, *, width, band_rows, bands, level_count,
):
    band = lax.axis_index("rows")
    first_step = lax.axis_index("step") == lax.axis_size("step") - 1
    top_outside = band == 0
    bottom_outside = band == bands - 1
    channels = start_ref.shape[0]
    level = start_level(levels_ref, first_step)
    sigma_low = level_sigma(level, level_count, (1, width))
    spread = sigma_low * sigma_low + 0.25
    scale_in = lax.rsqrt(spread)
    for u in range(band_rows + 2 * HALO):
        v = u - HALO
        if 0 <= v < band_rows:
            state = jnp.where(first_step, start_ref[:, v, :], previous_ref[0, :, v, :])
            cond = coarse_ref[:, v, :]
        elif v < 0:
            state = jnp.where(first_step, start_other_ref[:, band_rows + v, :], previous_other_ref[0, :, band_rows + v, :])
            cond = coarse_other_ref[:, band_rows + v, :]
        else:
            state = jnp.where(first_step, start_other_ref[:, v - band_rows, :], previous_other_ref[0, :, v - band_rows, :])
            cond = coarse_other_ref[:, v - band_rows, :]
        scaled = (scale_in * state).astype(jnp.bfloat16).astype(jnp.float32)
        inputs[0:channels, u * width : (u + 1) * width] = scaled
        inputs[channels:, u * width : (u + 1) * width] = cond.astype(jnp.float32)
    table = embed_ref[...].astype(jnp.float32)
    picked = jnp.where(lax.broadcasted_iota(jnp.int32, table.shape, 0) == level, table, 0.0)
    embed_row = jnp.sum(picked, axis=0, keepdims=True)
    feat = table.shape[1]
    embed = jnp.broadcast_to(embed_row, (feat, feat)).T[:, 0:1]
    lift_w = transposed(lift_ref[...]).astype(jnp.bfloat16)

    span = CHUNK_ROWS * width
    in_rows = band_rows + 2 * HALO
    for q in range(in_rows // CHUNK_ROWS):
        start = q * span
        chunk = inputs[:, start : start + span].astype(jnp.bfloat16)
        lifted = jnp.dot(lift_w, chunk, preferred_element_type=jnp.float32)
        lifted = (lifted + embed).astype(jnp.bfloat16)
        row0 = q * CHUNK_ROWS
        if HALO <= row0 < HALO + band_rows:
            keep = (row0 - HALO) * width
            lifted_keep[:, keep : keep + span] = lifted
        act = silu(normalize_features(lifted.astype(jnp.float32)))
        if row0 < HALO:
            act = jnp.where(top_outside, 0.0, act)
        if row0 >= HALO + band_rows:
            act = jnp.where(bottom_outside, 0.0, act)
        act_first[:, start : start + span] = act.astype(jnp.bfloat16)
    first_w = stack_taps(first_ref)
    mid_rows = band_rows + 2
    chunks = row_chunks(mid_rows)
    for q, (first, rows) in enumerate(chunks):
        span = rows * width
        lanes = lax.broadcasted_iota(jnp.int32, (1, span), 1)
        middle = conv_chunk(act_first, first_w, first, rows, width, lanes % width)
        act = silu(normalize_features(middle))
        if q == 0:
            act = jnp.where(jnp.logical_and(top_outside, lanes < width), 0.0, act)
        if q == len(chunks) - 1:
            act = jnp.where(jnp.logical_and(bottom_outside, lanes >= span - width), 0.0, act)
        act_next[:, first * width : first * width + span] = act.astype(jnp.bfloat16)
    second_w = stack_taps(second_ref)
    outgoing = []
    for q, (first, rows) in enumerate(row_chunks(band_rows)):
        span = rows * width
        lanes = lax.broadcasted_iota(jnp.int32, (1, span), 1)
        conv = conv_chunk(act_next, second_w, first, rows, width, lanes % width)
        start = first * width
        hidden_local[:, start : start + span] = lifted_keep[:, start : start + span].astype(jnp.float32) + conv
        copy = pltpu.make_async_copy(
            hidden_local.at[:, pl.ds(start, span)], hidden_ref.at[:, pl.ds(start, span)], hidden_sems.at[q]
        )
        copy.start()
        outgoing.append(copy)
    tokens_per_row = width // 4
    pool_w = jnp.where(
        lax.broadcasted_iota(jnp.int32, (width, tokens_per_row), 0) // 4
        == lax.broadcasted_iota(jnp.int32, (width, tokens_per_row), 1),
        1.0 / 16.0,
        0.0,
    ).astype(jnp.float32)
    pooled = []
    for a in range(band_rows // 4):
        row_sum = hidden_local[:, (4 * a) * width : (4 * a + 1) * width]
        for u in range(1, 4):
            row_sum = row_sum + hidden_local[:, (4 * a + u) * width : (4 * a + u + 1) * width]
        pooled.append(
            jnp.dot(row_sum, pool_w, precision=lax.Precision.HIGHEST, preferred_element_type=jnp.float32)
        )
    pooled = jnp.concatenate(pooled, axis=1)
    tokens = normalize_features(pooled).astype(jnp.bfloat16)
    project_t = jnp.concatenate(
        [transposed(project_ref[:, g * feat : (g + 1) * feat]) for g in range(3)], axis=0
    ).astype(jnp.bfloat16)
    projected = jnp.dot(project_t, tokens, preferred_element_type=jnp.float32)
    query_ref[...] = feature_map(projected[:feat])
    key_feats = feature_map(projected[feat : 2 * feat]).astype(jnp.bfloat16)
    value_rows = projected[2 * feat :].astype(jnp.bfloat16)
    ones = jnp.ones((HEAD_DIM, key_feats.shape[1]), jnp.bfloat16)
    contract_tokens = (((1,), (1,)), ((), ()))
    for h in range(feat // HEAD_DIM):
        keys_h = key_feats[h * HEAD_DIM : (h + 1) * HEAD_DIM]
        values_h = value_rows[h * HEAD_DIM : (h + 1) * HEAD_DIM]
        summary_t = lax.dot_general(values_h, keys_h, contract_tokens, preferred_element_type=jnp.float32)
        totals = lax.dot_general(ones, keys_h, contract_tokens, preferred_element_type=jnp.float32)
        stats_ref[h * HEAD_DIM : (h + 1) * HEAD_DIM, :] = jnp.concatenate([summary_t, totals], axis=1)
    for copy in outgoing:
        copy.wait()


def head_kernel(
    levels_ref, next_levels_ref, hidden_ref, query_ref, stats_own_ref, stats_other_ref, mix_ref, out_w_ref,
    previous_ref, start_ref, denoised_ref, seed_ref, hidden_local, hidden_sems,
    *, width, band_rows, level_count,
):
    group = 4 * width
    incoming = []
    for a in range(band_rows // 4):
        copy = pltpu.make_async_copy(
            hidden_ref.at[:, pl.ds(a * group, group)], hidden_local.at[:, pl.ds(a * group, group)], hidden_sems.at[a]
        )
        copy.start()
        incoming.append(copy)
    first_step = lax.axis_index("step") == lax.axis_size("step") - 1
    sigma_low = level_sigma(start_level(levels_ref, first_step), level_count, (1, width))
    sigma_high = level_sigma(next_levels_ref[0, 1], level_count, (1, width))
    spread = sigma_low * sigma_low + 0.25
    scale_skip = 0.25 / spread
    scale_out = 0.5 * sigma_low * lax.rsqrt(spread)
    sigma_gap = sigma_high - sigma_low
    feat = query_ref.shape[0]
    contexts = []
    for h in range(feat // HEAD_DIM):
        rows = slice(h * HEAD_DIM, (h + 1) * HEAD_DIM)
        queries_h = query_ref[rows, :]
        stats_h = stats_own_ref[rows, :] + stats_other_ref[rows, :]
        numerator = jnp.dot(
            stats_h[:, 0:HEAD_DIM], queries_h,
            precision=lax.Precision.HIGHEST, preferred_element_type=jnp.float32,
        )
        denominator = jnp.dot(
            stats_h[:, HEAD_DIM : 2 * HEAD_DIM], queries_h,
            precision=lax.Precision.HIGHEST, preferred_element_type=jnp.float32,
        )
        contexts.append(numerator / denominator)
    context = jnp.concatenate(contexts, axis=0).astype(jnp.bfloat16)
    mix_t = transposed(mix_ref[...]).astype(jnp.bfloat16)
    mixed = jnp.dot(mix_t, context, preferred_element_type=jnp.float32)
    tokens_per_row = width // 4
    expand = jnp.where(
        lax.broadcasted_iota(jnp.int32, (tokens_per_row, width), 0)
        == lax.broadcasted_iota(jnp.int32, (tokens_per_row, width), 1) // 4,
        1.0,
        0.0,
    ).astype(jnp.float32)
    out_w = out_w_ref[...]
    for a in range(band_rows // 4):
        incoming[a].wait()
        spread_mixed = jnp.dot(
            mixed[:, a * tokens_per_row : (a + 1) * tokens_per_row],
            expand,
            precision=lax.Precision.HIGHEST,
            preferred_element_type=jnp.float32,
        )
        for u in range(4):
            r = 4 * a + u
            start = r * width
            combined = hidden_local[:, start : start + width] + spread_mixed
            act = silu(normalize_features(combined)).astype(jnp.bfloat16)
            field = jnp.dot(out_w, act, preferred_element_type=jnp.float32)
            state = jnp.where(first_step, start_ref[:, r, :], previous_ref[0, :, r, :])
            denoised = scale_skip * state + scale_out * field
            denoised_ref[:, r, :] = denoised
            drift = sigma_gap * (state - denoised) / sigma_low
            seed_ref[:, r, :] = drift + jnp.where(first_step, state, 0.0)


def vmem():
    return pl.BlockSpec(memory_space=pltpu.VMEM)


def smem():
    return pl.BlockSpec(memory_space=pltpu.SMEM)


def edge_rows(x, axis, dim, width):
    length = x.shape[dim]
    last = lax.slice_in_dim(x, length - width, length, axis=dim)
    leading = lax.slice_in_dim(x, 0, width, axis=dim)
    return jnp.where(lax.axis_index(axis) == 0, last, leading)


def local(
    iterates,
    window_start,
    coarse,
    step_levels,
    level_embed,
    lift_weight,
    conv_first,
    conv_second,
    project_weight,
    mix_weight,
    output_weight,
):
    level_count = 2 * lax.axis_size("step") + 1
    bands = lax.axis_size("rows")
    steps = lax.axis_size("step")
    assert bands == 2
    swap = [(0, 1), (1, 0)]
    next_levels = lax.ppermute(step_levels, "step", [((h + 1) % steps, h) for h in range(steps)])
    previous = iterates
    previous_other = lax.ppermute(previous, "rows", swap)
    start_other = lax.ppermute(window_start, "rows", swap)
    coarse_other = lax.ppermute(coarse, "rows", swap)

    channels, band_rows, width = window_start.shape
    feat = lift_weight.shape[1]
    pixels = band_rows * width
    tokens = (band_rows // 4) * (width // 4)
    trunk = pl.pallas_call(
        lambda *refs: trunk_kernel(
            *refs, width=width, band_rows=band_rows, bands=bands, level_count=level_count
        ),
        out_shape=(
            jax.ShapeDtypeStruct((feat, pixels), jnp.float32),
            jax.ShapeDtypeStruct((feat, tokens), jnp.float32),
            jax.ShapeDtypeStruct((feat, 2 * HEAD_DIM), jnp.float32),
        ),
        in_specs=[smem()] + [vmem()] * 11,
        out_specs=(pl.BlockSpec(memory_space=pl.ANY), vmem(), vmem()),
        scratch_shapes=[
            pltpu.VMEM((channels + coarse.shape[0], (band_rows + 2 * HALO) * width), jnp.float32),
            pltpu.VMEM((feat, (band_rows + 2 * HALO) * width), jnp.bfloat16),
            pltpu.VMEM((feat, pixels), jnp.bfloat16),
            pltpu.VMEM((feat, (band_rows + 2) * width), jnp.bfloat16),
            pltpu.VMEM((feat, pixels), jnp.float32),
            pltpu.SemaphoreType.DMA((len(row_chunks(band_rows)),)),
        ],
    )
    hidden, queries, stats_own = trunk(
        step_levels,
        previous,
        window_start,
        start_other,
        previous_other,
        coarse,
        coarse_other,
        lift_weight,
        level_embed,
        conv_first,
        conv_second,
        project_weight,
    )
    stats_other = lax.ppermute(stats_own, "rows", swap)

    head = pl.pallas_call(
        lambda *refs: head_kernel(*refs, width=width, band_rows=band_rows, level_count=level_count),
        out_shape=(
            jax.ShapeDtypeStruct(window_start.shape, jnp.float32),
            jax.ShapeDtypeStruct(window_start.shape, jnp.float32),
        ),
        in_specs=[smem(), smem(), pl.BlockSpec(memory_space=pl.ANY)] + [vmem()] * 7,
        out_specs=(vmem(), vmem()),
        scratch_shapes=[
            pltpu.VMEM((feat, pixels), jnp.float32),
            pltpu.SemaphoreType.DMA((band_rows // 4,)),
        ],
    )
    denoised, seed = head(
        step_levels, next_levels, hidden, queries, stats_own, stats_other, mix_weight, output_weight.T,
        previous, window_start,
    )
    trajectory, denoised = rotated_prefix(seed, denoised, "step")
    return (trajectory[None], denoised[None])


def rotated_prefix(seed, denoised, axis):
    steps = lax.axis_size(axis)
    holder = lambda position: (position - 1) % steps
    shift = 1
    while 2 * shift < steps:
        pairs = [(holder(p), holder(p + shift)) for p in range(steps - shift)]
        seed = seed + lax.ppermute(seed, axis, pairs)
        shift *= 2
    moved = lax.ppermute(
        jnp.concatenate([seed, denoised], axis=0), axis, [(h, (h + 1) % steps) for h in range(steps)]
    )
    channels = seed.shape[0]
    if steps == 1:
        return moved[:channels], moved[channels:]
    far = lax.ppermute(seed, axis, [(holder(q), q + shift) for q in range(steps - shift)])
    return moved[:channels] + far, moved[channels:]


def solution(mesh):
    return jax.shard_map(
        local,
        mesh=mesh,
        in_specs=(
            P("step", "ens", "rows", None),
            P("ens", "rows", None),
            P("ens", "rows", None),
            P("step", None),
            P(),
            P(),
            P(),
            P(),
            P(),
            P(),
            P(),
        ),
        out_specs=(P("step", "ens", "rows", None), P("step", "ens", "rows", None)),
        check_vma=False,
    )
```

```python
import jax
import numpy as np
import jax.numpy as jnp
from jax import lax
from jax.experimental import pallas as pl
from jax.experimental.pallas import tpu as pltpu
from jax.sharding import PartitionSpec as P

HEAD_DIM = 64
HALO = 2
CHUNK_ROWS = 2
CONV_ROWS = 4

SIGMA_TOP = 8.0
SIGMA_END = 0.002
LOG_RATIO = float(np.log(np.float32(SIGMA_END / SIGMA_TOP)))


def from_behind(x, axis, by):
    devices = lax.axis_size(axis)
    pairs = [(i, i + by) for i in range(devices) if 0 <= i + by < devices]
    return lax.ppermute(x, axis, pairs)


def with_halo(x, axis, dim, width):
    devices, length = (lax.axis_size(axis), x.shape[dim])
    last = lax.slice_in_dim(x, length - width, length, axis=dim)
    leading = lax.slice_in_dim(x, 0, width, axis=dim)
    if devices == 2:
        me = lax.axis_index(axis)
        outgoing = jnp.where(me == 0, last, leading)
        incoming = lax.ppermute(outgoing, axis, [(0, 1), (1, 0)])
        zero = jnp.zeros_like(incoming)
        before = jnp.where(me == 0, zero, incoming)
        after = jnp.where(me == 0, incoming, zero)
    else:
        up = [(i, i + 1) for i in range(devices - 1)]
        down = [(j, i) for i, j in up]
        before = lax.ppermute(last, axis, up)
        after = lax.ppermute(leading, axis, down)
    return jnp.concatenate([before, x, after], axis=dim)


def band_sum(x, axis):
    devices = lax.axis_size(axis)
    if devices == 2:
        return x + lax.ppermute(x, axis, [(0, 1), (1, 0)])
    return lax.psum(x, axis)


def prefix_sum(x, axis):
    devices = lax.axis_size(axis)
    shift = 1
    while shift < devices:
        pairs = [(i, i + shift) for i in range(devices - shift)]
        x = x + lax.ppermute(x, axis, pairs)
        shift *= 2
    return x


def noise_level(levels, level_count):
    fraction = levels.astype(jnp.float32) / jnp.float32(level_count - 1)
    return SIGMA_TOP * jnp.exp(fraction * jnp.log(jnp.float32(SIGMA_END / SIGMA_TOP)))


def normalize_features(values):
    mean_square = jnp.sum(values * values, axis=0, keepdims=True) * (1.0 / values.shape[0])
    return values * lax.rsqrt(mean_square + 1e-06)


def silu(values):
    return values / (1.0 + jnp.exp(-values))


def silu_tanh(values):
    half = 0.5 * values
    return half + half * jnp.tanh(half)


def feature_map(values):
    return jnp.where(values > 0, values + 1.0, jnp.exp(jnp.minimum(values, 0.0)))


def conv_chunk(source, weight, first_row, rows, width, column):
    span = rows * width
    stacked = jnp.concatenate(
        [source[:, (first_row + i) * width : (first_row + i) * width + span] for i in range(3)],
        axis=0,
    )
    taps = jnp.dot(weight, stacked, preferred_element_type=jnp.float32)
    feat = taps.shape[0] // 3
    left = pltpu.roll(taps[0:feat], 1, 1)
    right = pltpu.roll(taps[2 * feat : 3 * feat], span - 1, 1)
    result = taps[feat : 2 * feat]
    result = result + jnp.where(column != 0, left, 0.0)
    result = result + jnp.where(column != width - 1, right, 0.0)
    return result


def row_chunks(rows):
    chunks, first = [], 0
    while first < rows:
        size = min(CONV_ROWS, rows - first)
        chunks.append((first, size))
        first += size
    return chunks


def transposed(block):
    return block.astype(jnp.float32).T


def stack_taps(weight_ref):
    return jnp.concatenate(
        [
            jnp.concatenate([transposed(weight_ref[i, j]) for i in range(3)], axis=1)
            for j in range(3)
        ],
        axis=0,
    ).astype(jnp.bfloat16)


def level_sigma(level, level_count, shape):
    fraction = jnp.full(shape, level.astype(jnp.float32)) / jnp.float32(level_count - 1)
    return SIGMA_TOP * jnp.exp(fraction * LOG_RATIO)


def start_level(levels_ref, first_step):
    return jnp.where(first_step, 0, levels_ref[0, 1])


def trunk_kernel(
    levels_ref, previous_ref, start_ref, start_other_ref, previous_other_ref, coarse_ref,
    coarse_other_ref, lift_ref, embed_ref, first_ref, second_ref, project_ref,
    hidden_ref, query_ref, stats_ref, inputs, act_first, lifted_keep, act_next, hidden_local,
    hidden_staged, hidden_sems, *, width, band_rows, bands, level_count,
):
    band = lax.axis_index("rows")
    first_step = lax.axis_index("step") == lax.axis_size("step") - 1
    top_outside = band == 0
    bottom_outside = band == bands - 1
    channels = start_ref.shape[0]
    level = start_level(levels_ref, first_step)
    sigma_low = level_sigma(level, level_count, (1, width))
    spread = sigma_low * sigma_low + 0.25
    scale_in = lax.rsqrt(spread)
    for u in range(band_rows + 2 * HALO):
        v = u - HALO
        if 0 <= v < band_rows:
            state = jnp.where(first_step, start_ref[:, v, :], previous_ref[0, :, v, :])
            cond = coarse_ref[:, v, :]
        elif v < 0:
            state = jnp.where(first_step, start_other_ref[:, band_rows + v, :], previous_other_ref[0, :, band_rows + v, :])
            cond = coarse_other_ref[:, band_rows + v, :]
        else:
            state = jnp.where(first_step, start_other_ref[:, v - band_rows, :], previous_other_ref[0, :, v - band_rows, :])
            cond = coarse_other_ref[:, v - band_rows, :]
        scaled = (scale_in * state).astype(jnp.bfloat16).astype(jnp.float32)
        inputs[0:channels, u * width : (u + 1) * width] = scaled
        inputs[channels:, u * width : (u + 1) * width] = cond.astype(jnp.float32)
    table = embed_ref[...].astype(jnp.float32)
    picked = jnp.where(lax.broadcasted_iota(jnp.int32, table.shape, 0) == level, table, 0.0)
    embed_row = jnp.sum(picked, axis=0, keepdims=True)
    feat = table.shape[1]
    embed = jnp.broadcast_to(embed_row, (feat, feat)).T[:, 0:1]
    lift_w = transposed(lift_ref[...]).astype(jnp.bfloat16)

    span = CHUNK_ROWS * width
    in_rows = band_rows + 2 * HALO
    for q in range(in_rows // CHUNK_ROWS):
        start = q * span
        chunk = inputs[:, start : start + span].astype(jnp.bfloat16)
        lifted = jnp.dot(lift_w, chunk, preferred_element_type=jnp.float32)
        lifted = (lifted + embed).astype(jnp.bfloat16)
        row0 = q * CHUNK_ROWS
        if HALO <= row0 < HALO + band_rows:
            keep = (row0 - HALO) * width
            lifted_keep[:, keep : keep + span] = lifted
        act = silu(normalize_features(lifted.astype(jnp.float32)))
        if row0 < HALO:
            act = jnp.where(top_outside, 0.0, act)
        if row0 >= HALO + band_rows:
            act = jnp.where(bottom_outside, 0.0, act)
        act_first[:, start : start + span] = act.astype(jnp.bfloat16)
    first_w = stack_taps(first_ref)
    mid_rows = band_rows + 2
    chunks = row_chunks(mid_rows)
    for q, (first, rows) in enumerate(chunks):
        span = rows * width
        lanes = lax.broadcasted_iota(jnp.int32, (1, span), 1)
        middle = conv_chunk(act_first, first_w, first, rows, width, lanes % width)
        act = silu(normalize_features(middle))
        if q == 0:
            act = jnp.where(jnp.logical_and(top_outside, lanes < width), 0.0, act)
        if q == len(chunks) - 1:
            act = jnp.where(jnp.logical_and(bottom_outside, lanes >= span - width), 0.0, act)
        act_next[:, first * width : first * width + span] = act.astype(jnp.bfloat16)
    second_w = stack_taps(second_ref)
    outgoing = []
    for q, (first, rows) in enumerate(row_chunks(band_rows)):
        span = rows * width
        lanes = lax.broadcasted_iota(jnp.int32, (1, span), 1)
        conv = conv_chunk(act_next, second_w, first, rows, width, lanes % width)
        start = first * width
        hidden = lifted_keep[:, start : start + span].astype(jnp.float32) + conv
        hidden_local[:, start : start + span] = hidden
        hidden_staged[:, start : start + span] = hidden.astype(jnp.bfloat16)
        copy = pltpu.make_async_copy(
            hidden_staged.at[:, pl.ds(start, span)], hidden_ref.at[:, pl.ds(start, span)], hidden_sems.at[q]
        )
        copy.start()
        outgoing.append(copy)
    tokens_per_row = width // 4
    pool_w = jnp.where(
        lax.broadcasted_iota(jnp.int32, (width, tokens_per_row), 0) // 4
        == lax.broadcasted_iota(jnp.int32, (width, tokens_per_row), 1),
        1.0 / 16.0,
        0.0,
    ).astype(jnp.float32)
    pooled = []
    for a in range(band_rows // 4):
        row_sum = hidden_local[:, (4 * a) * width : (4 * a + 1) * width]
        for u in range(1, 4):
            row_sum = row_sum + hidden_local[:, (4 * a + u) * width : (4 * a + u + 1) * width]
        pooled.append(
            jnp.dot(row_sum, pool_w, precision=lax.Precision.HIGHEST, preferred_element_type=jnp.float32)
        )
    pooled = jnp.concatenate(pooled, axis=1)
    tokens = normalize_features(pooled).astype(jnp.bfloat16)
    project_t = jnp.concatenate(
        [transposed(project_ref[:, g * feat : (g + 1) * feat]) for g in range(3)], axis=0
    ).astype(jnp.bfloat16)
    projected = jnp.dot(project_t, tokens, preferred_element_type=jnp.float32)
    query_ref[...] = feature_map(projected[:feat])
    key_feats = feature_map(projected[feat : 2 * feat]).astype(jnp.bfloat16)
    value_rows = projected[2 * feat :].astype(jnp.bfloat16)
    ones = jnp.ones((HEAD_DIM, key_feats.shape[1]), jnp.bfloat16)
    contract_tokens = (((1,), (1,)), ((), ()))
    for h in range(feat // HEAD_DIM):
        keys_h = key_feats[h * HEAD_DIM : (h + 1) * HEAD_DIM]
        values_h = value_rows[h * HEAD_DIM : (h + 1) * HEAD_DIM]
        summary_t = lax.dot_general(values_h, keys_h, contract_tokens, preferred_element_type=jnp.float32)
        totals = lax.dot_general(ones, keys_h, contract_tokens, preferred_element_type=jnp.float32)
        stats_ref[h * HEAD_DIM : (h + 1) * HEAD_DIM, :] = jnp.concatenate([summary_t, totals], axis=1)
    for copy in outgoing:
        copy.wait()


def head_kernel(
    levels_ref, next_levels_ref, hidden_ref, query_ref, stats_own_ref, stats_other_ref, mix_ref, out_w_ref,
    previous_ref, start_ref, denoised_ref, seed_ref, hidden_local, hidden_sems,
    *, width, band_rows, level_count,
):
    group = 4 * width
    incoming = []
    for a in range(band_rows // 4):
        copy = pltpu.make_async_copy(
            hidden_ref.at[:, pl.ds(a * group, group)], hidden_local.at[:, pl.ds(a * group, group)], hidden_sems.at[a]
        )
        copy.start()
        incoming.append(copy)
    first_step = lax.axis_index("step") == lax.axis_size("step") - 1
    sigma_low = level_sigma(start_level(levels_ref, first_step), level_count, (1, width))
    sigma_high = level_sigma(next_levels_ref[0, 1], level_count, (1, width))
    spread = sigma_low * sigma_low + 0.25
    scale_skip = 0.25 / spread
    scale_out = 0.5 * sigma_low * lax.rsqrt(spread)
    sigma_gap = sigma_high - sigma_low
    feat = query_ref.shape[0]
    contexts = []
    for h in range(feat // HEAD_DIM):
        rows = slice(h * HEAD_DIM, (h + 1) * HEAD_DIM)
        queries_h = query_ref[rows, :]
        stats_h = stats_own_ref[rows, :] + stats_other_ref[rows, :]
        numerator = jnp.dot(
            stats_h[:, 0:HEAD_DIM], queries_h,
            precision=lax.Precision.HIGHEST, preferred_element_type=jnp.float32,
        )
        denominator = jnp.dot(
            stats_h[:, HEAD_DIM : 2 * HEAD_DIM], queries_h,
            precision=lax.Precision.HIGHEST, preferred_element_type=jnp.float32,
        )
        contexts.append(numerator / denominator)
    context = jnp.concatenate(contexts, axis=0).astype(jnp.bfloat16)
    mix_t = transposed(mix_ref[...]).astype(jnp.bfloat16)
    mixed = jnp.dot(mix_t, context, preferred_element_type=jnp.float32)
    tokens_per_row = width // 4
    expand = jnp.where(
        lax.broadcasted_iota(jnp.int32, (tokens_per_row, width), 0)
        == lax.broadcasted_iota(jnp.int32, (tokens_per_row, width), 1) // 4,
        1.0,
        0.0,
    ).astype(jnp.float32)
    out_w = out_w_ref[...]
    for a in range(band_rows // 4):
        incoming[a].wait()
        spread_mixed = jnp.dot(
            mixed[:, a * tokens_per_row : (a + 1) * tokens_per_row],
            expand,
            precision=lax.Precision.HIGHEST,
            preferred_element_type=jnp.float32,
        )
        for u in range(4):
            r = 4 * a + u
            start = r * width
            combined = hidden_local[:, start : start + width].astype(jnp.float32) + spread_mixed
            act = silu_tanh(normalize_features(combined)).astype(jnp.bfloat16)
            field = jnp.dot(out_w, act, preferred_element_type=jnp.float32)
            state = jnp.where(first_step, start_ref[:, r, :], previous_ref[0, :, r, :])
            denoised = scale_skip * state + scale_out * field
            denoised_ref[:, r, :] = denoised
            drift = sigma_gap * (state - denoised) / sigma_low
            seed_ref[:, r, :] = drift + jnp.where(first_step, state, 0.0)


def vmem():
    return pl.BlockSpec(memory_space=pltpu.VMEM)


def smem():
    return pl.BlockSpec(memory_space=pltpu.SMEM)


def edge_rows(x, axis, dim, width):
    length = x.shape[dim]
    last = lax.slice_in_dim(x, length - width, length, axis=dim)
    leading = lax.slice_in_dim(x, 0, width, axis=dim)
    return jnp.where(lax.axis_index(axis) == 0, last, leading)


def local(
    iterates,
    window_start,
    coarse,
    step_levels,
    level_embed,
    lift_weight,
    conv_first,
    conv_second,
    project_weight,
    mix_weight,
    output_weight,
):
    level_count = 2 * lax.axis_size("step") + 1
    bands = lax.axis_size("rows")
    steps = lax.axis_size("step")
    assert bands == 2
    swap = [(0, 1), (1, 0)]
    next_levels = lax.ppermute(step_levels, "step", [((h + 1) % steps, h) for h in range(steps)])
    previous = iterates
    previous_other = lax.ppermute(previous, "rows", swap)
    start_other = lax.ppermute(window_start, "rows", swap)
    coarse_other = lax.ppermute(coarse, "rows", swap)

    channels, band_rows, width = window_start.shape
    feat = lift_weight.shape[1]
    pixels = band_rows * width
    tokens = (band_rows // 4) * (width // 4)
    trunk = pl.pallas_call(
        lambda *refs: trunk_kernel(
            *refs, width=width, band_rows=band_rows, bands=bands, level_count=level_count
        ),
        out_shape=(
            jax.ShapeDtypeStruct((feat, pixels), jnp.bfloat16),
            jax.ShapeDtypeStruct((feat, tokens), jnp.float32),
            jax.ShapeDtypeStruct((feat, 2 * HEAD_DIM), jnp.float32),
        ),
        in_specs=[smem()] + [vmem()] * 11,
        out_specs=(pl.BlockSpec(memory_space=pl.ANY), vmem(), vmem()),
        scratch_shapes=[
            pltpu.VMEM((channels + coarse.shape[0], (band_rows + 2 * HALO) * width), jnp.float32),
            pltpu.VMEM((feat, (band_rows + 2 * HALO) * width), jnp.bfloat16),
            pltpu.VMEM((feat, pixels), jnp.bfloat16),
            pltpu.VMEM((feat, (band_rows + 2) * width), jnp.bfloat16),
            pltpu.VMEM((feat, pixels), jnp.float32),
            pltpu.VMEM((feat, pixels), jnp.bfloat16),
            pltpu.SemaphoreType.DMA((len(row_chunks(band_rows)),)),
        ],
    )
    hidden, queries, stats_own = trunk(
        step_levels,
        previous,
        window_start,
        start_other,
        previous_other,
        coarse,
        coarse_other,
        lift_weight,
        level_embed,
        conv_first,
        conv_second,
        project_weight,
    )
    stats_other = lax.ppermute(stats_own, "rows", swap)

    head = pl.pallas_call(
        lambda *refs: head_kernel(*refs, width=width, band_rows=band_rows, level_count=level_count),
        out_shape=(
            jax.ShapeDtypeStruct(window_start.shape, jnp.float32),
            jax.ShapeDtypeStruct(window_start.shape, jnp.float32),
        ),
        in_specs=[smem(), smem(), pl.BlockSpec(memory_space=pl.ANY)] + [vmem()] * 7,
        out_specs=(vmem(), vmem()),
        scratch_shapes=[
            pltpu.VMEM((feat, pixels), jnp.bfloat16),
            pltpu.SemaphoreType.DMA((band_rows // 4,)),
        ],
    )
    denoised, seed = head(
        step_levels, next_levels, hidden, queries, stats_own, stats_other, mix_weight, output_weight.T,
        previous, window_start,
    )
    trajectory, denoised = rotated_prefix(seed, denoised, "step")
    return (trajectory[None], denoised[None])


def rotated_prefix(seed, denoised, axis):
    steps = lax.axis_size(axis)
    holder = lambda position: (position - 1) % steps
    shift = 1
    while 2 * shift < steps:
        pairs = [(holder(p), holder(p + shift)) for p in range(steps - shift)]
        seed = seed + lax.ppermute(seed, axis, pairs)
        shift *= 2
    moved = lax.ppermute(
        jnp.concatenate([seed, denoised], axis=0), axis, [(h, (h + 1) % steps) for h in range(steps)]
    )
    channels = seed.shape[0]
    if steps == 1:
        return moved[:channels], moved[channels:]
    far = lax.ppermute(seed, axis, [(holder(q), q + shift) for q in range(steps - shift)])
    return moved[:channels] + far, moved[channels:]


def solution(mesh):
    return jax.shard_map(
        local,
        mesh=mesh,
        in_specs=(
            P("step", "ens", "rows", None),
            P("ens", "rows", None),
            P("ens", "rows", None),
            P("step", None),
            P(),
            P(),
            P(),
            P(),
            P(),
            P(),
            P(),
        ),
        out_specs=(P("step", "ens", "rows", None), P("step", "ens", "rows", None)),
        check_vma=False,
    )
```

```python
import jax
import numpy as np
import jax.numpy as jnp
from jax import lax
from jax.experimental import pallas as pl
from jax.experimental.pallas import tpu as pltpu
from jax.sharding import PartitionSpec as P

HEAD_DIM = 64
HALO = 2
CHUNK_ROWS = 2
CONV_ROWS = 4

SIGMA_TOP = 8.0
SIGMA_END = 0.002
LOG_RATIO = float(np.log(np.float32(SIGMA_END / SIGMA_TOP)))


def from_behind(x, axis, by):
    devices = lax.axis_size(axis)
    pairs = [(i, i + by) for i in range(devices) if 0 <= i + by < devices]
    return lax.ppermute(x, axis, pairs)


def with_halo(x, axis, dim, width):
    devices, length = (lax.axis_size(axis), x.shape[dim])
    last = lax.slice_in_dim(x, length - width, length, axis=dim)
    leading = lax.slice_in_dim(x, 0, width, axis=dim)
    if devices == 2:
        me = lax.axis_index(axis)
        outgoing = jnp.where(me == 0, last, leading)
        incoming = lax.ppermute(outgoing, axis, [(0, 1), (1, 0)])
        zero = jnp.zeros_like(incoming)
        before = jnp.where(me == 0, zero, incoming)
        after = jnp.where(me == 0, incoming, zero)
    else:
        up = [(i, i + 1) for i in range(devices - 1)]
        down = [(j, i) for i, j in up]
        before = lax.ppermute(last, axis, up)
        after = lax.ppermute(leading, axis, down)
    return jnp.concatenate([before, x, after], axis=dim)


def band_sum(x, axis):
    devices = lax.axis_size(axis)
    if devices == 2:
        return x + lax.ppermute(x, axis, [(0, 1), (1, 0)])
    return lax.psum(x, axis)


def prefix_sum(x, axis):
    devices = lax.axis_size(axis)
    shift = 1
    while shift < devices:
        pairs = [(i, i + shift) for i in range(devices - shift)]
        x = x + lax.ppermute(x, axis, pairs)
        shift *= 2
    return x


def noise_level(levels, level_count):
    fraction = levels.astype(jnp.float32) / jnp.float32(level_count - 1)
    return SIGMA_TOP * jnp.exp(fraction * jnp.log(jnp.float32(SIGMA_END / SIGMA_TOP)))


def normalize_features(values):
    mean_square = jnp.sum(values * values, axis=0, keepdims=True) * (1.0 / values.shape[0])
    return values * lax.rsqrt(mean_square + 1e-06)


def silu(values):
    return values / (1.0 + jnp.exp(-values))


def silu_tanh(values):
    half = 0.5 * values
    return half + half * jnp.tanh(half)


def feature_map(values):
    return jnp.where(values > 0, values + 1.0, jnp.exp(jnp.minimum(values, 0.0)))


def conv_chunk(source, weight, first_row, rows, width, column):
    span = rows * width
    stacked = jnp.concatenate(
        [source[:, (first_row + i) * width : (first_row + i) * width + span] for i in range(3)],
        axis=0,
    )
    taps = jnp.dot(weight, stacked, preferred_element_type=jnp.float32)
    feat = taps.shape[0] // 3
    left = pltpu.roll(taps[0:feat], 1, 1)
    right = pltpu.roll(taps[2 * feat : 3 * feat], span - 1, 1)
    result = taps[feat : 2 * feat]
    result = result + jnp.where(column != 0, left, 0.0)
    result = result + jnp.where(column != width - 1, right, 0.0)
    return result


def row_chunks(rows):
    chunks, first = [], 0
    while first < rows:
        size = min(CONV_ROWS, rows - first)
        chunks.append((first, size))
        first += size
    return chunks


def transposed(block):
    return block.astype(jnp.float32).T


def stack_taps(weight_ref):
    return jnp.concatenate(
        [
            jnp.concatenate([transposed(weight_ref[i, j]) for i in range(3)], axis=1)
            for j in range(3)
        ],
        axis=0,
    ).astype(jnp.bfloat16)


def level_sigma(level, level_count, shape):
    fraction = jnp.full(shape, level.astype(jnp.float32)) / jnp.float32(level_count - 1)
    return SIGMA_TOP * jnp.exp(fraction * LOG_RATIO)


def start_level(levels_ref, first_step):
    return jnp.where(first_step, 0, levels_ref[0, 1])


def trunk_kernel(
    levels_ref, previous_ref, start_ref, start_other_ref, previous_other_ref, coarse_ref,
    coarse_other_ref, lift_ref, embed_ref, first_ref, second_ref, project_ref,
    hidden_ref, query_ref, stats_ref, inputs, act_first, lifted_keep, act_next, hidden_local,
    hidden_staged, hidden_sems, *, width, band_rows, bands, level_count,
):
    band = lax.axis_index("rows")
    first_step = lax.axis_index("step") == lax.axis_size("step") - 1
    top_outside = band == 0
    bottom_outside = band == bands - 1
    channels = start_ref.shape[0]
    level = start_level(levels_ref, first_step)
    sigma_low = level_sigma(level, level_count, (1, width))
    spread = sigma_low * sigma_low + 0.25
    scale_in = lax.rsqrt(spread)
    for u in range(band_rows + 2 * HALO):
        v = u - HALO
        if 0 <= v < band_rows:
            state = jnp.where(first_step, start_ref[:, v, :], previous_ref[0, :, v, :])
            cond = coarse_ref[:, v, :]
        elif v < 0:
            state = jnp.where(first_step, start_other_ref[:, band_rows + v, :], previous_other_ref[0, :, band_rows + v, :])
            cond = coarse_other_ref[:, band_rows + v, :]
        else:
            state = jnp.where(first_step, start_other_ref[:, v - band_rows, :], previous_other_ref[0, :, v - band_rows, :])
            cond = coarse_other_ref[:, v - band_rows, :]
        scaled = (scale_in * state).astype(jnp.bfloat16).astype(jnp.float32)
        inputs[0:channels, u * width : (u + 1) * width] = scaled
        inputs[channels:, u * width : (u + 1) * width] = cond.astype(jnp.float32)
    table = embed_ref[...].astype(jnp.float32)
    picked = jnp.where(lax.broadcasted_iota(jnp.int32, table.shape, 0) == level, table, 0.0)
    embed_row = jnp.sum(picked, axis=0, keepdims=True)
    feat = table.shape[1]
    embed = jnp.broadcast_to(embed_row, (feat, feat)).T[:, 0:1]
    lift_w = transposed(lift_ref[...]).astype(jnp.bfloat16)

    span = CHUNK_ROWS * width
    in_rows = band_rows + 2 * HALO
    def lift_chunk(start, keep):
        chunk = inputs[:, start : start + span].astype(jnp.bfloat16)
        lifted = jnp.dot(lift_w, chunk, preferred_element_type=jnp.float32)
        lifted = (lifted + embed).astype(jnp.bfloat16)
        if keep is not None:
            lifted_keep[:, keep : keep + span] = lifted
        act = silu(normalize_features(lifted.astype(jnp.float32)))
        act_first[:, start : start + span] = act.astype(jnp.bfloat16)

    for q in range(in_rows // CHUNK_ROWS):
        start = q * span
        row0 = q * CHUNK_ROWS
        if HALO <= row0 < HALO + band_rows:
            lift_chunk(start, (row0 - HALO) * width)
            continue
        outside = top_outside if row0 < HALO else bottom_outside

        @pl.when(outside)
        def _():
            act_first[:, start : start + span] = jnp.zeros((act_first.shape[0], span), jnp.bfloat16)

        @pl.when(jnp.logical_not(outside))
        def _():
            lift_chunk(start, None)
    first_w = stack_taps(first_ref)
    mid_rows = band_rows + 2
    chunks = row_chunks(mid_rows)
    for q, (first, rows) in enumerate(chunks):
        span = rows * width
        lanes = lax.broadcasted_iota(jnp.int32, (1, span), 1)
        middle = conv_chunk(act_first, first_w, first, rows, width, lanes % width)
        act = silu(normalize_features(middle))
        if q == 0:
            act = jnp.where(jnp.logical_and(top_outside, lanes < width), 0.0, act)
        if q == len(chunks) - 1:
            act = jnp.where(jnp.logical_and(bottom_outside, lanes >= span - width), 0.0, act)
        act_next[:, first * width : first * width + span] = act.astype(jnp.bfloat16)
    second_w = stack_taps(second_ref)
    outgoing = []
    for q, (first, rows) in enumerate(row_chunks(band_rows)):
        span = rows * width
        lanes = lax.broadcasted_iota(jnp.int32, (1, span), 1)
        conv = conv_chunk(act_next, second_w, first, rows, width, lanes % width)
        start = first * width
        hidden = lifted_keep[:, start : start + span].astype(jnp.float32) + conv
        hidden_local[:, start : start + span] = hidden
        hidden_staged[:, start : start + span] = hidden.astype(jnp.bfloat16)
        copy = pltpu.make_async_copy(
            hidden_staged.at[:, pl.ds(start, span)], hidden_ref.at[:, pl.ds(start, span)], hidden_sems.at[q]
        )
        copy.start()
        outgoing.append(copy)
    tokens_per_row = width // 4
    pool_w = jnp.where(
        lax.broadcasted_iota(jnp.int32, (width, tokens_per_row), 0) // 4
        == lax.broadcasted_iota(jnp.int32, (width, tokens_per_row), 1),
        1.0 / 16.0,
        0.0,
    ).astype(jnp.float32)
    pooled = []
    for a in range(band_rows // 4):
        row_sum = hidden_local[:, (4 * a) * width : (4 * a + 1) * width]
        for u in range(1, 4):
            row_sum = row_sum + hidden_local[:, (4 * a + u) * width : (4 * a + u + 1) * width]
        pooled.append(
            jnp.dot(row_sum, pool_w, precision=lax.Precision.HIGHEST, preferred_element_type=jnp.float32)
        )
    pooled = jnp.concatenate(pooled, axis=1)
    tokens = normalize_features(pooled).astype(jnp.bfloat16)
    project_t = jnp.concatenate(
        [transposed(project_ref[:, g * feat : (g + 1) * feat]) for g in range(3)], axis=0
    ).astype(jnp.bfloat16)
    projected = jnp.dot(project_t, tokens, preferred_element_type=jnp.float32)
    query_ref[...] = feature_map(projected[:feat])
    key_feats = feature_map(projected[feat : 2 * feat]).astype(jnp.bfloat16)
    value_rows = projected[2 * feat :].astype(jnp.bfloat16)
    ones = jnp.ones((HEAD_DIM, key_feats.shape[1]), jnp.bfloat16)
    contract_tokens = (((1,), (1,)), ((), ()))
    for h in range(feat // HEAD_DIM):
        keys_h = key_feats[h * HEAD_DIM : (h + 1) * HEAD_DIM]
        values_h = value_rows[h * HEAD_DIM : (h + 1) * HEAD_DIM]
        summary_t = lax.dot_general(values_h, keys_h, contract_tokens, preferred_element_type=jnp.float32)
        totals = lax.dot_general(ones, keys_h, contract_tokens, preferred_element_type=jnp.float32)
        stats_ref[h * HEAD_DIM : (h + 1) * HEAD_DIM, :] = jnp.concatenate([summary_t, totals], axis=1)
    for copy in outgoing:
        copy.wait()


def head_kernel(
    levels_ref, next_levels_ref, hidden_ref, query_ref, stats_own_ref, stats_other_ref, mix_ref, out_w_ref,
    previous_ref, start_ref, denoised_ref, seed_ref, hidden_local, hidden_sems,
    *, width, band_rows, level_count,
):
    group = 4 * width
    incoming = []
    for a in range(band_rows // 4):
        copy = pltpu.make_async_copy(
            hidden_ref.at[:, pl.ds(a * group, group)], hidden_local.at[:, pl.ds(a * group, group)], hidden_sems.at[a]
        )
        copy.start()
        incoming.append(copy)
    first_step = lax.axis_index("step") == lax.axis_size("step") - 1
    sigma_low = level_sigma(start_level(levels_ref, first_step), level_count, (1, width))
    sigma_high = level_sigma(next_levels_ref[0, 1], level_count, (1, width))
    spread = sigma_low * sigma_low + 0.25
    scale_skip = 0.25 / spread
    scale_out = 0.5 * sigma_low * lax.rsqrt(spread)
    sigma_gap = sigma_high - sigma_low
    feat = query_ref.shape[0]
    contexts = []
    for h in range(feat // HEAD_DIM):
        rows = slice(h * HEAD_DIM, (h + 1) * HEAD_DIM)
        queries_h = query_ref[rows, :]
        stats_h = stats_own_ref[rows, :] + stats_other_ref[rows, :]
        numerator = jnp.dot(
            stats_h[:, 0:HEAD_DIM], queries_h,
            precision=lax.Precision.HIGHEST, preferred_element_type=jnp.float32,
        )
        denominator = jnp.dot(
            stats_h[:, HEAD_DIM : 2 * HEAD_DIM], queries_h,
            precision=lax.Precision.HIGHEST, preferred_element_type=jnp.float32,
        )
        contexts.append(numerator / denominator)
    context = jnp.concatenate(contexts, axis=0).astype(jnp.bfloat16)
    mix_t = transposed(mix_ref[...]).astype(jnp.bfloat16)
    mixed = jnp.dot(mix_t, context, preferred_element_type=jnp.float32)
    tokens_per_row = width // 4
    expand = jnp.where(
        lax.broadcasted_iota(jnp.int32, (tokens_per_row, width), 0)
        == lax.broadcasted_iota(jnp.int32, (tokens_per_row, width), 1) // 4,
        1.0,
        0.0,
    ).astype(jnp.float32)
    out_w = out_w_ref[...]
    for a in range(band_rows // 4):
        incoming[a].wait()
        spread_mixed = jnp.dot(
            mixed[:, a * tokens_per_row : (a + 1) * tokens_per_row],
            expand,
            precision=lax.Precision.HIGHEST,
            preferred_element_type=jnp.float32,
        )
        for u in range(4):
            r = 4 * a + u
            start = r * width
            combined = hidden_local[:, start : start + width].astype(jnp.float32) + spread_mixed
            act = silu_tanh(normalize_features(combined)).astype(jnp.bfloat16)
            field = jnp.dot(out_w, act, preferred_element_type=jnp.float32)
            state = jnp.where(first_step, start_ref[:, r, :], previous_ref[0, :, r, :])
            denoised = scale_skip * state + scale_out * field
            denoised_ref[:, r, :] = denoised
            drift = sigma_gap * (state - denoised) / sigma_low
            seed_ref[:, r, :] = drift + jnp.where(first_step, state, 0.0)


def vmem():
    return pl.BlockSpec(memory_space=pltpu.VMEM)


def smem():
    return pl.BlockSpec(memory_space=pltpu.SMEM)


def edge_rows(x, axis, dim, width):
    length = x.shape[dim]
    last = lax.slice_in_dim(x, length - width, length, axis=dim)
    leading = lax.slice_in_dim(x, 0, width, axis=dim)
    return jnp.where(lax.axis_index(axis) == 0, last, leading)


def local(
    iterates,
    window_start,
    coarse,
    step_levels,
    level_embed,
    lift_weight,
    conv_first,
    conv_second,
    project_weight,
    mix_weight,
    output_weight,
):
    level_count = 2 * lax.axis_size("step") + 1
    bands = lax.axis_size("rows")
    steps = lax.axis_size("step")
    assert bands == 2
    swap = [(0, 1), (1, 0)]
    next_levels = lax.ppermute(step_levels, "step", [((h + 1) % steps, h) for h in range(steps)])
    previous = iterates
    previous_other = lax.ppermute(previous, "rows", swap)
    start_other = lax.ppermute(window_start, "rows", swap)
    coarse_other = lax.ppermute(coarse, "rows", swap)

    channels, band_rows, width = window_start.shape
    feat = lift_weight.shape[1]
    pixels = band_rows * width
    tokens = (band_rows // 4) * (width // 4)
    trunk = pl.pallas_call(
        lambda *refs: trunk_kernel(
            *refs, width=width, band_rows=band_rows, bands=bands, level_count=level_count
        ),
        out_shape=(
            jax.ShapeDtypeStruct((feat, pixels), jnp.bfloat16),
            jax.ShapeDtypeStruct((feat, tokens), jnp.float32),
            jax.ShapeDtypeStruct((feat, 2 * HEAD_DIM), jnp.float32),
        ),
        in_specs=[smem()] + [vmem()] * 11,
        out_specs=(pl.BlockSpec(memory_space=pl.ANY), vmem(), vmem()),
        scratch_shapes=[
            pltpu.VMEM((channels + coarse.shape[0], (band_rows + 2 * HALO) * width), jnp.float32),
            pltpu.VMEM((feat, (band_rows + 2 * HALO) * width), jnp.bfloat16),
            pltpu.VMEM((feat, pixels), jnp.bfloat16),
            pltpu.VMEM((feat, (band_rows + 2) * width), jnp.bfloat16),
            pltpu.VMEM((feat, pixels), jnp.float32),
            pltpu.VMEM((feat, pixels), jnp.bfloat16),
            pltpu.SemaphoreType.DMA((len(row_chunks(band_rows)),)),
        ],
    )
    hidden, queries, stats_own = trunk(
        step_levels,
        previous,
        window_start,
        start_other,
        previous_other,
        coarse,
        coarse_other,
        lift_weight,
        level_embed,
        conv_first,
        conv_second,
        project_weight,
    )
    stats_other = lax.ppermute(stats_own, "rows", swap)

    head = pl.pallas_call(
        lambda *refs: head_kernel(*refs, width=width, band_rows=band_rows, level_count=level_count),
        out_shape=(
            jax.ShapeDtypeStruct(window_start.shape, jnp.float32),
            jax.ShapeDtypeStruct(window_start.shape, jnp.float32),
        ),
        in_specs=[smem(), smem(), pl.BlockSpec(memory_space=pl.ANY)] + [vmem()] * 7,
        out_specs=(vmem(), vmem()),
        scratch_shapes=[
            pltpu.VMEM((feat, pixels), jnp.bfloat16),
            pltpu.SemaphoreType.DMA((band_rows // 4,)),
        ],
    )
    denoised, seed = head(
        step_levels, next_levels, hidden, queries, stats_own, stats_other, mix_weight, output_weight.T,
        previous, window_start,
    )
    trajectory, denoised = rotated_prefix(seed, denoised, "step")
    return (trajectory[None], denoised[None])


def rotated_prefix(seed, denoised, axis):
    steps = lax.axis_size(axis)
    holder = lambda position: (position - 1) % steps
    shift = 1
    while 2 * shift < steps:
        pairs = [(holder(p), holder(p + shift)) for p in range(steps - shift)]
        seed = seed + lax.ppermute(seed, axis, pairs)
        shift *= 2
    moved = lax.ppermute(
        jnp.concatenate([seed, denoised], axis=0), axis, [(h, (h + 1) % steps) for h in range(steps)]
    )
    channels = seed.shape[0]
    if steps == 1:
        return moved[:channels], moved[channels:]
    far = lax.ppermute(seed, axis, [(holder(q), q + shift) for q in range(steps - shift)])
    return moved[:channels] + far, moved[channels:]


def solution(mesh):
    return jax.shard_map(
        local,
        mesh=mesh,
        in_specs=(
            P("step", "ens", "rows", None),
            P("ens", "rows", None),
            P("ens", "rows", None),
            P("step", None),
            P(),
            P(),
            P(),
            P(),
            P(),
            P(),
            P(),
        ),
        out_specs=(P("step", "ens", "rows", None), P("step", "ens", "rows", None)),
        check_vma=False,
    )
```

```python
import jax
import numpy as np
import jax.numpy as jnp
from jax import lax
from jax.experimental import pallas as pl
from jax.experimental.pallas import tpu as pltpu
from jax.sharding import PartitionSpec as P

HEAD_DIM = 64
HALO = 2
CHUNK_ROWS = 2
CONV_ROWS = 4

SIGMA_TOP = 8.0
SIGMA_END = 0.002
LOG_RATIO = float(np.log(np.float32(SIGMA_END / SIGMA_TOP)))


def from_behind(x, axis, by):
    devices = lax.axis_size(axis)
    pairs = [(i, i + by) for i in range(devices) if 0 <= i + by < devices]
    return lax.ppermute(x, axis, pairs)


def with_halo(x, axis, dim, width):
    devices, length = (lax.axis_size(axis), x.shape[dim])
    last = lax.slice_in_dim(x, length - width, length, axis=dim)
    leading = lax.slice_in_dim(x, 0, width, axis=dim)
    if devices == 2:
        me = lax.axis_index(axis)
        outgoing = jnp.where(me == 0, last, leading)
        incoming = lax.ppermute(outgoing, axis, [(0, 1), (1, 0)])
        zero = jnp.zeros_like(incoming)
        before = jnp.where(me == 0, zero, incoming)
        after = jnp.where(me == 0, incoming, zero)
    else:
        up = [(i, i + 1) for i in range(devices - 1)]
        down = [(j, i) for i, j in up]
        before = lax.ppermute(last, axis, up)
        after = lax.ppermute(leading, axis, down)
    return jnp.concatenate([before, x, after], axis=dim)


def band_sum(x, axis):
    devices = lax.axis_size(axis)
    if devices == 2:
        return x + lax.ppermute(x, axis, [(0, 1), (1, 0)])
    return lax.psum(x, axis)


def prefix_sum(x, axis):
    devices = lax.axis_size(axis)
    shift = 1
    while shift < devices:
        pairs = [(i, i + shift) for i in range(devices - shift)]
        x = x + lax.ppermute(x, axis, pairs)
        shift *= 2
    return x


def noise_level(levels, level_count):
    fraction = levels.astype(jnp.float32) / jnp.float32(level_count - 1)
    return SIGMA_TOP * jnp.exp(fraction * jnp.log(jnp.float32(SIGMA_END / SIGMA_TOP)))


def normalize_features(values):
    mean_square = jnp.sum(values * values, axis=0, keepdims=True) * (1.0 / values.shape[0])
    return values * lax.rsqrt(mean_square + 1e-06)


def silu(values):
    return values / (1.0 + jnp.exp(-values))


def silu_tanh(values):
    half = 0.5 * values
    return half + half * jnp.tanh(half)


def feature_map(values):
    return jnp.where(values > 0, values + 1.0, jnp.exp(jnp.minimum(values, 0.0)))


def conv_chunk(source, weight, first_row, rows, width, column):
    span = rows * width
    stacked = jnp.concatenate(
        [source[:, (first_row + i) * width : (first_row + i) * width + span] for i in range(3)],
        axis=0,
    )
    taps = jnp.dot(weight, stacked, preferred_element_type=jnp.float32)
    feat = taps.shape[0] // 3
    left = pltpu.roll(taps[0:feat], 1, 1)
    right = pltpu.roll(taps[2 * feat : 3 * feat], span - 1, 1)
    result = taps[feat : 2 * feat]
    result = result + jnp.where(column != 0, left, 0.0)
    result = result + jnp.where(column != width - 1, right, 0.0)
    return result


def row_chunks(rows):
    chunks, first = [], 0
    while first < rows:
        size = min(CONV_ROWS, rows - first)
        chunks.append((first, size))
        first += size
    return chunks


def transposed(block):
    return block.astype(jnp.float32).T


def stack_taps(weight_ref):
    return jnp.concatenate(
        [
            jnp.concatenate([transposed(weight_ref[i, j]) for i in range(3)], axis=1)
            for j in range(3)
        ],
        axis=0,
    ).astype(jnp.bfloat16)


def level_sigma(level, level_count, shape):
    fraction = jnp.full(shape, level.astype(jnp.float32)) / jnp.float32(level_count - 1)
    return SIGMA_TOP * jnp.exp(fraction * LOG_RATIO)


def start_level(levels_ref, first_step):
    return jnp.where(first_step, 0, levels_ref[0, 1])


def trunk_kernel(
    levels_ref, previous_ref, start_ref, start_other_ref, previous_other_ref, coarse_ref,
    coarse_other_ref, lift_ref, embed_ref, first_ref, second_ref, project_ref,
    hidden_ref, query_ref, stats_ref, inputs, act_first, lifted_keep, act_next, hidden_local,
    hidden_staged, hidden_sems, *, width, band_rows, bands, level_count,
):
    band = lax.axis_index("rows")
    first_step = lax.axis_index("step") == lax.axis_size("step") - 1
    top_outside = band == 0
    bottom_outside = band == bands - 1
    channels = start_ref.shape[0]
    level = start_level(levels_ref, first_step)
    sigma_low = level_sigma(level, level_count, (1, width))
    spread = sigma_low * sigma_low + 0.25
    scale_in = lax.rsqrt(spread)
    for u in range(band_rows + 2 * HALO):
        v = u - HALO
        if 0 <= v < band_rows:
            state = jnp.where(first_step, start_ref[:, v, :], previous_ref[0, :, v, :])
            cond = coarse_ref[:, v, :]
        elif v < 0:
            state = jnp.where(first_step, start_other_ref[:, band_rows + v, :], previous_other_ref[0, :, band_rows + v, :])
            cond = coarse_other_ref[:, band_rows + v, :]
        else:
            state = jnp.where(first_step, start_other_ref[:, v - band_rows, :], previous_other_ref[0, :, v - band_rows, :])
            cond = coarse_other_ref[:, v - band_rows, :]
        scaled = (scale_in * state).astype(jnp.bfloat16).astype(jnp.float32)
        inputs[0:channels, u * width : (u + 1) * width] = scaled
        inputs[channels:, u * width : (u + 1) * width] = cond.astype(jnp.float32)
    table = embed_ref[...].astype(jnp.float32)
    picked = jnp.where(lax.broadcasted_iota(jnp.int32, table.shape, 0) == level, table, 0.0)
    embed_row = jnp.sum(picked, axis=0, keepdims=True)
    feat = table.shape[1]
    embed = jnp.broadcast_to(embed_row, (feat, feat)).T[:, 0:1]
    lift_w = transposed(lift_ref[...]).astype(jnp.bfloat16)

    span = CHUNK_ROWS * width
    in_rows = band_rows + 2 * HALO
    for q in range(in_rows // CHUNK_ROWS):
        start = q * span
        chunk = inputs[:, start : start + span].astype(jnp.bfloat16)
        lifted = jnp.dot(lift_w, chunk, preferred_element_type=jnp.float32)
        lifted = (lifted + embed).astype(jnp.bfloat16)
        row0 = q * CHUNK_ROWS
        if HALO <= row0 < HALO + band_rows:
            keep = (row0 - HALO) * width
            lifted_keep[:, keep : keep + span] = lifted
        act = silu(normalize_features(lifted.astype(jnp.float32)))
        if row0 < HALO:
            act = jnp.where(top_outside, 0.0, act)
        if row0 >= HALO + band_rows:
            act = jnp.where(bottom_outside, 0.0, act)
        act_first[:, start : start + span] = act.astype(jnp.bfloat16)
    first_w = stack_taps(first_ref)
    mid_rows = band_rows + 2
    chunks = row_chunks(mid_rows)
    for q, (first, rows) in enumerate(chunks):
        span = rows * width
        lanes = lax.broadcasted_iota(jnp.int32, (1, span), 1)
        middle = conv_chunk(act_first, first_w, first, rows, width, lanes % width)
        act = silu_tanh(normalize_features(middle))
        if q == 0:
            act = jnp.where(jnp.logical_and(top_outside, lanes < width), 0.0, act)
        if q == len(chunks) - 1:
            act = jnp.where(jnp.logical_and(bottom_outside, lanes >= span - width), 0.0, act)
        act_next[:, first * width : first * width + span] = act.astype(jnp.bfloat16)
    second_w = stack_taps(second_ref)
    outgoing = []
    for q, (first, rows) in enumerate(row_chunks(band_rows)):
        span = rows * width
        lanes = lax.broadcasted_iota(jnp.int32, (1, span), 1)
        conv = conv_chunk(act_next, second_w, first, rows, width, lanes % width)
        start = first * width
        hidden = lifted_keep[:, start : start + span].astype(jnp.float32) + conv
        hidden_local[:, start : start + span] = hidden
        hidden_staged[:, start : start + span] = hidden.astype(jnp.bfloat16)
        copy = pltpu.make_async_copy(
            hidden_staged.at[:, pl.ds(start, span)], hidden_ref.at[:, pl.ds(start, span)], hidden_sems.at[q]
        )
        copy.start()
        outgoing.append(copy)
    tokens_per_row = width // 4
    pool_w = jnp.where(
        lax.broadcasted_iota(jnp.int32, (width, tokens_per_row), 0) // 4
        == lax.broadcasted_iota(jnp.int32, (width, tokens_per_row), 1),
        1.0 / 16.0,
        0.0,
    ).astype(jnp.float32)
    pooled = []
    for a in range(band_rows // 4):
        row_sum = hidden_local[:, (4 * a) * width : (4 * a + 1) * width]
        for u in range(1, 4):
            row_sum = row_sum + hidden_local[:, (4 * a + u) * width : (4 * a + u + 1) * width]
        pooled.append(
            jnp.dot(row_sum, pool_w, precision=lax.Precision.HIGHEST, preferred_element_type=jnp.float32)
        )
    pooled = jnp.concatenate(pooled, axis=1)
    tokens = normalize_features(pooled).astype(jnp.bfloat16)
    project_t = jnp.concatenate(
        [transposed(project_ref[:, g * feat : (g + 1) * feat]) for g in range(3)], axis=0
    ).astype(jnp.bfloat16)
    projected = jnp.dot(project_t, tokens, preferred_element_type=jnp.float32)
    query_ref[...] = feature_map(projected[:feat])
    key_feats = feature_map(projected[feat : 2 * feat]).astype(jnp.bfloat16)
    value_rows = projected[2 * feat :].astype(jnp.bfloat16)
    ones = jnp.ones((HEAD_DIM, key_feats.shape[1]), jnp.bfloat16)
    contract_tokens = (((1,), (1,)), ((), ()))
    for h in range(feat // HEAD_DIM):
        keys_h = key_feats[h * HEAD_DIM : (h + 1) * HEAD_DIM]
        values_h = value_rows[h * HEAD_DIM : (h + 1) * HEAD_DIM]
        summary_t = lax.dot_general(values_h, keys_h, contract_tokens, preferred_element_type=jnp.float32)
        totals = lax.dot_general(ones, keys_h, contract_tokens, preferred_element_type=jnp.float32)
        stats_ref[h * HEAD_DIM : (h + 1) * HEAD_DIM, :] = jnp.concatenate([summary_t, totals], axis=1)
    for copy in outgoing:
        copy.wait()


def head_kernel(
    levels_ref, next_levels_ref, hidden_ref, query_ref, stats_own_ref, stats_other_ref, mix_ref, out_w_ref,
    previous_ref, start_ref, denoised_ref, seed_ref, hidden_local, hidden_sems,
    *, width, band_rows, level_count,
):
    group = 4 * width
    incoming = []
    for a in range(band_rows // 4):
        copy = pltpu.make_async_copy(
            hidden_ref.at[:, pl.ds(a * group, group)], hidden_local.at[:, pl.ds(a * group, group)], hidden_sems.at[a]
        )
        copy.start()
        incoming.append(copy)
    first_step = lax.axis_index("step") == lax.axis_size("step") - 1
    sigma_low = level_sigma(start_level(levels_ref, first_step), level_count, (1, width))
    sigma_high = level_sigma(next_levels_ref[0, 1], level_count, (1, width))
    spread = sigma_low * sigma_low + 0.25
    scale_skip = 0.25 / spread
    scale_out = 0.5 * sigma_low * lax.rsqrt(spread)
    sigma_gap = sigma_high - sigma_low
    feat = query_ref.shape[0]
    contexts = []
    for h in range(feat // HEAD_DIM):
        rows = slice(h * HEAD_DIM, (h + 1) * HEAD_DIM)
        queries_h = query_ref[rows, :]
        stats_h = stats_own_ref[rows, :] + stats_other_ref[rows, :]
        numerator = jnp.dot(
            stats_h[:, 0:HEAD_DIM], queries_h,
            precision=lax.Precision.HIGHEST, preferred_element_type=jnp.float32,
        )
        denominator = jnp.dot(
            stats_h[:, HEAD_DIM : 2 * HEAD_DIM], queries_h,
            precision=lax.Precision.HIGHEST, preferred_element_type=jnp.float32,
        )
        contexts.append(numerator / denominator)
    context = jnp.concatenate(contexts, axis=0).astype(jnp.bfloat16)
    mix_t = transposed(mix_ref[...]).astype(jnp.bfloat16)
    mixed = jnp.dot(mix_t, context, preferred_element_type=jnp.float32)
    tokens_per_row = width // 4
    expand = jnp.where(
        lax.broadcasted_iota(jnp.int32, (tokens_per_row, width), 0)
        == lax.broadcasted_iota(jnp.int32, (tokens_per_row, width), 1) // 4,
        1.0,
        0.0,
    ).astype(jnp.float32)
    out_w = out_w_ref[...]
    for a in range(band_rows // 4):
        incoming[a].wait()
        spread_mixed = jnp.dot(
            mixed[:, a * tokens_per_row : (a + 1) * tokens_per_row],
            expand,
            precision=lax.Precision.HIGHEST,
            preferred_element_type=jnp.float32,
        )
        for u in range(4):
            r = 4 * a + u
            start = r * width
            combined = hidden_local[:, start : start + width].astype(jnp.float32) + spread_mixed
            act = silu_tanh(normalize_features(combined)).astype(jnp.bfloat16)
            field = jnp.dot(out_w, act, preferred_element_type=jnp.float32)
            state = jnp.where(first_step, start_ref[:, r, :], previous_ref[0, :, r, :])
            denoised = scale_skip * state + scale_out * field
            denoised_ref[:, r, :] = denoised
            drift = sigma_gap * (state - denoised) / sigma_low
            seed_ref[:, r, :] = drift + jnp.where(first_step, state, 0.0)


def vmem():
    return pl.BlockSpec(memory_space=pltpu.VMEM)


def smem():
    return pl.BlockSpec(memory_space=pltpu.SMEM)


def edge_rows(x, axis, dim, width):
    length = x.shape[dim]
    last = lax.slice_in_dim(x, length - width, length, axis=dim)
    leading = lax.slice_in_dim(x, 0, width, axis=dim)
    return jnp.where(lax.axis_index(axis) == 0, last, leading)


def local(
    iterates,
    window_start,
    coarse,
    step_levels,
    level_embed,
    lift_weight,
    conv_first,
    conv_second,
    project_weight,
    mix_weight,
    output_weight,
):
    level_count = 2 * lax.axis_size("step") + 1
    bands = lax.axis_size("rows")
    steps = lax.axis_size("step")
    assert bands == 2
    swap = [(0, 1), (1, 0)]
    next_levels = lax.ppermute(step_levels, "step", [((h + 1) % steps, h) for h in range(steps)])
    previous = iterates
    previous_other = lax.ppermute(previous, "rows", swap)
    start_other = lax.ppermute(window_start, "rows", swap)
    coarse_other = lax.ppermute(coarse, "rows", swap)

    channels, band_rows, width = window_start.shape
    feat = lift_weight.shape[1]
    pixels = band_rows * width
    tokens = (band_rows // 4) * (width // 4)
    trunk = pl.pallas_call(
        lambda *refs: trunk_kernel(
            *refs, width=width, band_rows=band_rows, bands=bands, level_count=level_count
        ),
        out_shape=(
            jax.ShapeDtypeStruct((feat, pixels), jnp.bfloat16),
            jax.ShapeDtypeStruct((feat, tokens), jnp.float32),
            jax.ShapeDtypeStruct((feat, 2 * HEAD_DIM), jnp.float32),
        ),
        in_specs=[smem()] + [vmem()] * 11,
        out_specs=(pl.BlockSpec(memory_space=pl.ANY), vmem(), vmem()),
        scratch_shapes=[
            pltpu.VMEM((channels + coarse.shape[0], (band_rows + 2 * HALO) * width), jnp.float32),
            pltpu.VMEM((feat, (band_rows + 2 * HALO) * width), jnp.bfloat16),
            pltpu.VMEM((feat, pixels), jnp.bfloat16),
            pltpu.VMEM((feat, (band_rows + 2) * width), jnp.bfloat16),
            pltpu.VMEM((feat, pixels), jnp.float32),
            pltpu.VMEM((feat, pixels), jnp.bfloat16),
            pltpu.SemaphoreType.DMA((len(row_chunks(band_rows)),)),
        ],
    )
    hidden, queries, stats_own = trunk(
        step_levels,
        previous,
        window_start,
        start_other,
        previous_other,
        coarse,
        coarse_other,
        lift_weight,
        level_embed,
        conv_first,
        conv_second,
        project_weight,
    )
    stats_other = lax.ppermute(stats_own, "rows", swap)

    head = pl.pallas_call(
        lambda *refs: head_kernel(*refs, width=width, band_rows=band_rows, level_count=level_count),
        out_shape=(
            jax.ShapeDtypeStruct(window_start.shape, jnp.float32),
            jax.ShapeDtypeStruct(window_start.shape, jnp.float32),
        ),
        in_specs=[smem(), smem(), pl.BlockSpec(memory_space=pl.ANY)] + [vmem()] * 7,
        out_specs=(vmem(), vmem()),
        scratch_shapes=[
            pltpu.VMEM((feat, pixels), jnp.bfloat16),
            pltpu.SemaphoreType.DMA((band_rows // 4,)),
        ],
    )
    denoised, seed = head(
        step_levels, next_levels, hidden, queries, stats_own, stats_other, mix_weight, output_weight.T,
        previous, window_start,
    )
    trajectory, denoised = rotated_prefix(seed, denoised, "step")
    return (trajectory[None], denoised[None])


def rotated_prefix(seed, denoised, axis):
    steps = lax.axis_size(axis)
    holder = lambda position: (position - 1) % steps
    shift = 1
    while 2 * shift < steps:
        pairs = [(holder(p), holder(p + shift)) for p in range(steps - shift)]
        seed = seed + lax.ppermute(seed, axis, pairs)
        shift *= 2
    moved = lax.ppermute(
        jnp.concatenate([seed, denoised], axis=0), axis, [(h, (h + 1) % steps) for h in range(steps)]
    )
    channels = seed.shape[0]
    if steps == 1:
        return moved[:channels], moved[channels:]
    far = lax.ppermute(seed, axis, [(holder(q), q + shift) for q in range(steps - shift)])
    return moved[:channels] + far, moved[channels:]


def solution(mesh):
    return jax.shard_map(
        local,
        mesh=mesh,
        in_specs=(
            P("step", "ens", "rows", None),
            P("ens", "rows", None),
            P("ens", "rows", None),
            P("step", None),
            P(),
            P(),
            P(),
            P(),
            P(),
            P(),
            P(),
        ),
        out_specs=(P("step", "ens", "rows", None), P("step", "ens", "rows", None)),
        check_vma=False,
    )
```
